32 devices in a mesh: grp: 2 (over x), lat: 16 (over z, y, core).
Axes of the slice: x: 2, y: 2, z: 4, core: 2. Of those that a mesh axis runs over, the one named last changes fastest.
Arguments:
- activations: bfloat16 [64, 1440, 384], P(('grp', 'lat')), parts along dimension 0, may hold values from -6 to 6
- upstream: bfloat16 [64, 1440, 384], P(('grp', 'lat')), parts along dimension 0, may hold values from -6 to 6
- skip_weight: bfloat16 [384, 384], replicated, may hold values from -0.3125 to 0.3125
- spectral_weight: bfloat16 [32, 2, 384, 384], P('lat'), may hold values from -2.5 to 2.5
- slot_degree: int32 [32], replicated, may hold values from 0 to 31, each once
Outputs:
- grad_activations: bfloat16 [64, 1440, 384], P(('grp', 'lat')), parts along dimension 0
- grad_spectral: bfloat16 [64, 2, 384, 384], P(('grp', 'lat')), parts along dimension 0
- grad_skip: float32 [768, 384], P(('grp', 'lat')), parts along dimension 0
The draws below stay inside these ranges and needn't reach their ends.
There are 2 independent parts, one for each index of `grp`. The reference program is written for one: setup_inputs(seed, part) draws one part's arguments, and reference() takes and returns one part's arrays. A program takes and returns all parts, laid end to end along the dimension named above; an argument that names none is the same for every part. Nothing has to cross between parts.
Inputs may be any that keep to these rules, and one draw needn't show every extreme that they name: `slot_degree`: device d holds slots d * 2 to (d + 1) * 2 - 1 of spectral_weight and grad_spectral; every degree appears in exactly one slot.
All inputs are finite; a program needn't handle non-finite values.
Results may differ from the reference program's by a relative error of at most 0.013.
Values may be sent and summed in bfloat16 or wider, within the bound.
No kernel may reach another device: no remote copies, remote signals or barrier semaphores. Data moves between devices by JAX's collectives and lax.ppermute only.
A program may use at most 64 MiB of HBM per device.

```python
import math
import jax
import jax.numpy as jnp
from jax import lax

C = 384
NLON = 1440
LAT_DEV = 2
ORDERS = 4
NLAT = 32
DEGREES = 32


def spiked(values, stream_key, source, target, blocks, factor):
    def block_of(axis_at):
        return (jnp.arange(values.shape[axis_at]) // (values.shape[axis_at] // blocks)).reshape((-1,) + (1,) * (values.ndim - 1 - axis_at))

    near = jax.random.permutation(stream_key, blocks)[block_of(target)]
    far = (block_of(target) + blocks // 2) % blocks
    return jnp.where((block_of(source) == near) | (block_of(source) == far), factor * values, values)


def shard_levels(rng, shape, shards, least, largest):
    factor_of, own = 1.0, jax.random.fold_in(rng, 6)
    for axis_at, parts in shards:
        heights = jnp.exp(jax.random.uniform(jax.random.fold_in(own, axis_at), (parts,), jnp.float32, least / len(shards), largest / len(shards)))
        factor_of = factor_of * jnp.repeat(heights, shape[axis_at] // parts).reshape([-1 if axis == axis_at else 1 for axis in range(len(shape))])
    return factor_of


def normal_values(rng, dims, scale, limit, cuts=(), kind=jnp.bfloat16):
    entries = jax.random.normal(rng, dims, jnp.float32) * scale
    if len(cuts) > 0:
        entries = shard_levels(rng, dims, cuts, -0.22, 0.18) * entries
    return jnp.clip(entries, min=-limit, max=limit).astype(kind)


def gaussian_with(stream_key, extent, spread, most, cuts, heavy, kind=jnp.bfloat16):
    values = spread * jax.random.normal(stream_key, extent, jnp.float32)
    if cuts:
        values = values * shard_levels(stream_key, extent, cuts, -0.22, 0.18)
    return jnp.clip(spiked(values, jax.random.fold_in(stream_key, 3), *heavy), -most, most).astype(kind)


def setup_inputs(seed: int = 0, part: int = 0) -> dict:
    keys = jax.random.split(jax.random.key(seed), 6)
    own_keys = jax.random.split(jax.random.fold_in(keys[5], part), 6)
    return {
        "activations": gaussian_with(own_keys[0], (NLAT, NLON, C), 1.0, 6.0, ((0, 16),), (0, 2, 16, 2.0)),
        "upstream": normal_values(own_keys[1], (NLAT, NLON, C), 1.0, 6.0, ((0, 16),)),
        "skip_weight": normal_values(keys[2], (C, C), C ** -0.5, 0.3125),
        "spectral_weight": normal_values(keys[3], (DEGREES, 2, C, C), (C // 64) ** -0.5, 2.5, ((0, 16),)),
        "slot_degree": jax.random.permutation(keys[4], DEGREES).astype(jnp.int32),
    }


highest = lax.Precision.HIGHEST

def fourier_table(lon_total, orders):
    lon_ids = jnp.arange(lon_total, dtype=jnp.int32)[:, None]
    order_ids = jnp.arange(orders, dtype=jnp.int32)[None, :]
    angles = (lon_ids * order_ids % lon_total).astype(jnp.float32) * (2.0 * math.pi / lon_total)
    amplitude = math.sqrt(2.0 / lon_total)
    return jnp.concatenate([amplitude * jnp.cos(angles), -amplitude * jnp.sin(angles)], axis=1).astype(jnp.bfloat16)

def colatitudes(row_ids, lat_total):
    mirror = jnp.minimum(row_ids, lat_total - 1 - row_ids)
    colatitude = (mirror.astype(jnp.float32) + 0.5) * (math.pi / lat_total)
    cosines = jnp.where(row_ids < lat_total // 2, jnp.cos(colatitude), -jnp.cos(colatitude))
    return (cosines, jnp.sin(colatitude))

def legendre_table(cosines, sines, degrees, orders):
    order_col = jnp.arange(orders, dtype=jnp.float32)[:, None]
    factors = [math.sqrt(0.5)]
    for order_num in range(1, orders):
        factors.append(factors[-1] * math.sqrt((2.0 * order_num + 1.0) / (2.0 * order_num)))
    diagonal_start = jnp.array(factors, dtype=jnp.float32)[:, None] * jnp.power(sines[None, :], order_col)
    next_start = jnp.sqrt(2.0 * order_col + 3.0) * cosines[None, :] * diagonal_start

    def advance(state_pair, degree):
        previous, earlier = state_pair
        deg_value = degree.astype(jnp.float32)
        deg_below = deg_value - 1.0
        ratio_up = jnp.sqrt(jnp.maximum(4.0 * deg_value * deg_value - 1.0, 1.0) / jnp.maximum(deg_value * deg_value - order_col * order_col, 1.0))
        ratio_down = jnp.sqrt(jnp.maximum(deg_below * deg_below - order_col * order_col, 0.0) / jnp.maximum(4.0 * deg_below * deg_below - 1.0, 1.0))
        recurred = ratio_up * (cosines[None, :] * previous - ratio_down * earlier)
        current = jnp.where(deg_value == order_col, diagonal_start, jnp.where(deg_value == order_col + 1.0, next_start, jnp.where(deg_value > order_col + 1.0, recurred, 0.0)))
        return ((current, previous), current)
    zeroed = jnp.zeros((orders, cosines.shape[0]), jnp.float32)
    _, stacked = lax.scan(advance, (zeroed, zeroed), jnp.arange(degrees, dtype=jnp.int32))
    return jnp.concatenate([stacked, stacked], axis=1)

def gelu_tanh(values):
    return jax.nn.gelu(values, approximate=True)

def rounded(values):
    return lax.optimization_barrier(values.astype(jnp.bfloat16))

def complex_apply(coeffs, weights, orders):
    coeff_f = coeffs.astype(jnp.float32)
    weight_f = weights.astype(jnp.float32)
    real_in, imag_in = (coeff_f[:, :orders], coeff_f[:, orders:])
    real_w, imag_w = (weight_f[:, 0], weight_f[:, 1])

    def complex_term(operand_a, operand_b):
        return jnp.einsum('smc,scd->smd', operand_a, operand_b, precision=highest)
    real_out = complex_term(real_in, real_w) - complex_term(imag_in, imag_w)
    imag_out = complex_term(real_in, imag_w) + complex_term(imag_in, real_w)
    return jnp.concatenate([real_out, imag_out], axis=1)

def complex_adjoint(coeffs, cotangents, weights, orders):
    coeff_f = coeffs.astype(jnp.float32)
    cot_f = cotangents.astype(jnp.float32)
    weight_f = weights.astype(jnp.float32)
    real_in, imag_in = (coeff_f[:, :orders], coeff_f[:, orders:])
    real_g, imag_g = (cot_f[:, :orders], cot_f[:, orders:])
    real_w, imag_w = (weight_f[:, 0], weight_f[:, 1])

    def outer_sum(operand_a, operand_b):
        return jnp.einsum('smc,smd->scd', operand_a, operand_b, precision=highest)

    def back_term(operand_a, operand_b):
        return jnp.einsum('smd,scd->smc', operand_a, operand_b, precision=highest)
    grad_real = outer_sum(real_in, real_g) + outer_sum(imag_in, imag_g)
    grad_imag = outer_sum(real_in, imag_g) - outer_sum(imag_in, real_g)
    back_real = back_term(real_g, real_w) + back_term(imag_g, imag_w)
    back_imag = back_term(imag_g, real_w) - back_term(real_g, imag_w)
    return (jnp.stack([grad_real, grad_imag], axis=1), jnp.concatenate([back_real, back_imag], axis=1))

def reference(activations, upstream, skip_weight, spectral_weight, slot_degree):
    fourier = fourier_table(NLON, ORDERS)
    fourier_f = fourier.astype(jnp.float32)
    cosines, sines = colatitudes(jnp.arange(NLAT, dtype=jnp.int32), NLAT)
    plm = legendre_table(cosines, sines, DEGREES, ORDERS)
    quad = plm * (math.pi / NLAT * sines)[None, None, :]
    nblocks = NLAT // LAT_DEV
    act_blocks = activations.reshape(nblocks, LAT_DEV, NLON, C)
    up_blocks = upstream.reshape(nblocks, LAT_DEV, NLON, C)

    def to_modes(act_block):
        return jnp.einsum('jkc,kf->jfc', act_block.astype(jnp.float32), fourier_f, precision=highest)
    spectrum = lax.map(to_modes, act_blocks).reshape(NLAT, 2 * ORDERS, C)
    coeffs = rounded(jnp.einsum('lfj,jfc->lfc', quad, spectrum, precision=highest))
    degree_weight = jnp.zeros(spectral_weight.shape, spectral_weight.dtype).at[slot_degree].set(spectral_weight)
    filtered = rounded(complex_apply(coeffs, degree_weight, ORDERS))
    grid_modes = rounded(jnp.einsum('lfj,lfc->jfc', plm, filtered.astype(jnp.float32), precision=highest))
    mode_blocks = grid_modes.reshape(nblocks, LAT_DEV, 2 * ORDERS, C)
    skip_f = skip_weight.astype(jnp.float32)

    def forward_block(running, inputs):
        act_block, up_block, modes = inputs
        act_f = act_block.astype(jnp.float32)
        spatial = jnp.einsum('jfc,kf->jkc', modes.astype(jnp.float32), fourier_f, precision=highest)
        skip_out = jnp.einsum('jkc,cd->jkd', act_f, skip_f, precision=highest)
        _, pullback = jax.vjp(gelu_tanh, spatial + skip_out)
        slope_b = rounded(pullback(up_block.astype(jnp.float32))[0])
        slope_f = slope_b.astype(jnp.float32)
        running = running + jnp.einsum('jkc,jkd->cd', act_f, slope_f, precision=highest)
        mode_part = jnp.einsum('jkc,kf->jfc', slope_f, fourier_f, precision=highest)
        return (running, (slope_b, mode_part))
    skip_sum, (slopes, mode_parts) = lax.scan(forward_block, jnp.zeros((C, C), jnp.float32), (act_blocks, up_blocks, mode_blocks))
    grad_skip = skip_sum * (1.0 / math.sqrt(NLAT * NLON))
    mode_grads = mode_parts.reshape(NLAT, 2 * ORDERS, C)
    coeff_grads = rounded(jnp.einsum('lfj,jfc->lfc', plm, mode_grads, precision=highest))
    weight_grads, back_coeffs = complex_adjoint(coeffs, coeff_grads, degree_weight, ORDERS)
    back_b = rounded(back_coeffs)
    row_grads = rounded(jnp.einsum('lfj,lfc->jfc', quad, back_b.astype(jnp.float32), precision=highest))
    row_blocks = row_grads.reshape(nblocks, LAT_DEV, 2 * ORDERS, C)

    def backward_block(inputs):
        up_block, slope_b, row_part = inputs
        skip_part = jnp.einsum('jkd,cd->jkc', slope_b.astype(jnp.float32), skip_f, precision=highest)
        mode_part = jnp.einsum('jfc,kf->jkc', row_part.astype(jnp.float32), fourier_f, precision=highest)
        return (up_block.astype(jnp.float32) + skip_part + mode_part).astype(jnp.bfloat16)
    grad_activations = lax.map(backward_block, (up_blocks, slopes, row_blocks)).reshape(NLAT, NLON, C)
    grad_spectral = jnp.take(weight_grads.astype(jnp.bfloat16), slot_degree, axis=0)
    return (grad_activations, grad_spectral, grad_skip)
```

```python
import math

import jax
import jax.numpy as jnp
import ml_dtypes
import numpy as np
from jax import lax
from jax.sharding import PartitionSpec as P

ORDERS = 4


def fourier_table(lon_total, orders):
    lon_ids = np.arange(lon_total, dtype=np.int64)[:, None]
    order_ids = np.arange(orders, dtype=np.int64)[None, :]
    angles = (lon_ids * order_ids % lon_total).astype(np.float64) * (2.0 * math.pi / lon_total)
    amplitude = math.sqrt(2.0 / lon_total)
    table = np.concatenate([amplitude * np.cos(angles), -amplitude * np.sin(angles)], axis=1)
    return table.astype(ml_dtypes.bfloat16)


def colatitudes(lat_total):
    row_ids = np.arange(lat_total)
    mirror = np.minimum(row_ids, lat_total - 1 - row_ids)
    colatitude = (mirror.astype(np.float64) + 0.5) * (math.pi / lat_total)
    cosines = np.where(row_ids < lat_total // 2, np.cos(colatitude), -np.cos(colatitude))
    return cosines, np.sin(colatitude)


def legendre_table(cosines, sines, degrees, orders):
    rows = cosines.shape[0]
    table = np.zeros((degrees, orders, rows), np.float64)
    factor = math.sqrt(0.5)
    for m in range(orders):
        if m > 0:
            factor *= math.sqrt((2.0 * m + 1.0) / (2.0 * m))
        diagonal = factor * sines**m
        if m < degrees:
            table[m, m] = diagonal
        if m + 1 < degrees:
            table[m + 1, m] = math.sqrt(2.0 * m + 3.0) * cosines * diagonal
        for l in range(m + 2, degrees):
            a = math.sqrt((4.0 * l * l - 1.0) / (l * l - m * m))
            b = math.sqrt(((l - 1.0) ** 2 - m * m) / (4.0 * (l - 1.0) ** 2 - 1.0))
            table[l, m] = a * (cosines * table[l - 1, m] - b * table[l - 2, m])
    return np.concatenate([table, table], axis=1)


def legendre_scan(cosines_np, sines_np, degrees, orders):
    cosines = jnp.asarray(cosines_np.astype(np.float32))
    sines = jnp.asarray(sines_np.astype(np.float32))
    order_col = jnp.arange(orders, dtype=jnp.float32)[:, None]
    factors = [math.sqrt(0.5)]
    for order_num in range(1, orders):
        factors.append(factors[-1] * math.sqrt((2.0 * order_num + 1.0) / (2.0 * order_num)))
    diagonal_start = jnp.array(factors, dtype=jnp.float32)[:, None] * jnp.power(sines[None, :], order_col)
    next_start = jnp.sqrt(2.0 * order_col + 3.0) * cosines[None, :] * diagonal_start

    def advance(state_pair, degree):
        previous, earlier = state_pair
        deg_value = degree.astype(jnp.float32)
        deg_below = deg_value - 1.0
        ratio_up = jnp.sqrt(
            jnp.maximum(4.0 * deg_value * deg_value - 1.0, 1.0)
            / jnp.maximum(deg_value * deg_value - order_col * order_col, 1.0)
        )
        ratio_down = jnp.sqrt(
            jnp.maximum(deg_below * deg_below - order_col * order_col, 0.0)
            / jnp.maximum(4.0 * deg_below * deg_below - 1.0, 1.0)
        )
        recurred = ratio_up * (cosines[None, :] * previous - ratio_down * earlier)
        current = jnp.where(
            deg_value == order_col,
            diagonal_start,
            jnp.where(
                deg_value == order_col + 1.0,
                next_start,
                jnp.where(deg_value > order_col + 1.0, recurred, 0.0),
            ),
        )
        return ((current, previous), current)

    zeroed = jnp.zeros((orders, cosines.shape[0]), jnp.float32)
    _, stacked = lax.scan(advance, (zeroed, zeroed), jnp.arange(degrees, dtype=jnp.int32))
    return jnp.concatenate([stacked, stacked], axis=1)


def gelu_tanh(values):
    return jax.nn.gelu(values, approximate=True)


def xor_gather(x, axis_name, groups):
    bits = groups.bit_length() - 1
    cur = x[None]
    low = 0
    while low < bits:
        width = min(2, bits - low)
        parts = [cur]
        for k in range(1, 1 << width):
            mask = k << low
            parts.append(lax.ppermute(cur, axis_name, [(i, i ^ mask) for i in range(groups)]))
        cur = jnp.concatenate(parts, axis=0)
        low += width
    return cur


def xor_reduce_scatter(part, axis_name, groups, me):
    bits = groups.bit_length() - 1
    cur = part.reshape((groups, part.shape[0] // groups) + part.shape[1:])
    for b in range(bits):
        pairs = cur.reshape((cur.shape[0] // 2, 2) + cur.shape[1:])
        bit = (me >> b) & 1
        keep = jnp.where(bit == 0, pairs[:, 0], pairs[:, 1])
        send = jnp.where(bit == 0, pairs[:, 1], pairs[:, 0])
        mask = 1 << b
        cur = keep + lax.ppermute(send, axis_name, [(i, i ^ mask) for i in range(groups)])
    return cur.reshape(cur.shape[1:])


def complex_apply(coeffs, weights, orders):
    real_in, imag_in = (coeffs[:, :orders], coeffs[:, orders:])
    real_w, imag_w = (weights[:, 0], weights[:, 1])

    def complex_term(operand_a, operand_b):
        return jnp.einsum("smc,scd->smd", operand_a, operand_b, preferred_element_type=jnp.float32)

    real_out = complex_term(real_in, real_w) - complex_term(imag_in, imag_w)
    imag_out = complex_term(real_in, imag_w) + complex_term(imag_in, real_w)
    return jnp.concatenate([real_out, imag_out], axis=1)


def complex_adjoint(coeffs, cotangents, weights, orders):
    real_in, imag_in = (coeffs[:, :orders], coeffs[:, orders:])
    real_g, imag_g = (cotangents[:, :orders], cotangents[:, orders:])
    real_w, imag_w = (weights[:, 0], weights[:, 1])

    def outer_sum(operand_a, operand_b):
        return jnp.einsum("smc,smd->scd", operand_a, operand_b, preferred_element_type=jnp.float32)

    def back_term(operand_a, operand_b):
        return jnp.einsum("smd,scd->smc", operand_a, operand_b, preferred_element_type=jnp.float32)

    grad_real = outer_sum(real_in, real_g) + outer_sum(imag_in, imag_g)
    grad_imag = outer_sum(real_in, imag_g) - outer_sum(imag_in, real_g)
    back_real = back_term(real_g, real_w) + back_term(imag_g, imag_w)
    back_imag = back_term(imag_g, real_w) - back_term(real_g, imag_w)
    return (
        jnp.stack([grad_real, grad_imag], axis=1),
        jnp.concatenate([back_real, back_imag], axis=1),
    )


def local(activations, upstream, skip_weight, spectral_weight, slot_degree):
    groups = lax.axis_size("lat")
    me = lax.axis_index("lat")
    lat_rows = activations.shape[0]
    lon_total = activations.shape[1]
    lat_total = lat_rows * groups
    per_owner = spectral_weight.shape[0]
    degrees = per_owner * groups
    orders = ORDERS
    highest = lax.Precision.HIGHEST

    fourier = jnp.asarray(fourier_table(lon_total, orders))
    cosines, sines = colatitudes(lat_total)
    plm_np = legendre_table(cosines, sines, degrees, orders)
    quad_np = plm_np * (math.pi / lat_total * sines)[None, None, :]
    if degrees * lat_total <= 64 * 64:
        plm_all = jnp.asarray(plm_np.astype(np.float32))
        quad_all = jnp.asarray(quad_np.astype(np.float32))
    else:
        plm_all = legendre_scan(cosines, sines, degrees, orders)
        quad_all = plm_all * jnp.asarray((math.pi / lat_total * sines).astype(np.float32))[None, None, :]

    row_ids = jnp.arange(lat_total, dtype=jnp.int32)
    row_cols = jnp.bitwise_xor(me, row_ids // lat_rows) * lat_rows + row_ids % lat_rows
    slot_ids = jnp.arange(degrees, dtype=jnp.int32)
    slot_src = jnp.bitwise_xor(me, slot_ids // per_owner) * per_owner + slot_ids % per_owner
    slot_deg = jnp.take(slot_degree, slot_src, axis=0)
    own_deg = lax.dynamic_slice_in_dim(slot_degree, me * per_owner, per_owner)

    own_quad = jnp.take(jnp.take(quad_all, own_deg, axis=0), row_cols, axis=2)
    own_plm = jnp.take(jnp.take(plm_all, own_deg, axis=0), row_cols, axis=2)
    rows_plm = jnp.take(lax.dynamic_slice_in_dim(plm_all, me * lat_rows, lat_rows, axis=2), slot_deg, axis=0)
    rows_quad = jnp.take(lax.dynamic_slice_in_dim(quad_all, me * lat_rows, lat_rows, axis=2), slot_deg, axis=0)

    def gather(values):
        out = xor_gather(values, "lat", groups)
        return out.reshape((-1,) + out.shape[2:])

    spectrum = jnp.einsum("jkc,kf->jfc", activations, fourier, preferred_element_type=jnp.float32)
    all_spectrum = gather(spectrum)
    coeffs = jnp.einsum("sfj,jfc->sfc", own_quad, all_spectrum, precision=highest).astype(jnp.bfloat16)
    filtered = complex_apply(coeffs, spectral_weight, orders).astype(jnp.bfloat16)
    all_filtered = gather(filtered).astype(jnp.float32)
    grid_modes = jnp.einsum("sfj,sfc->jfc", rows_plm, all_filtered, precision=highest).astype(jnp.bfloat16)

    spatial = jnp.einsum("jfc,kf->jkc", grid_modes, fourier, preferred_element_type=jnp.float32)
    skip_out = jnp.einsum("jkc,cd->jkd", activations, skip_weight, preferred_element_type=jnp.float32)
    _, pullback = jax.vjp(gelu_tanh, spatial + skip_out)
    slope_b = pullback(upstream.astype(jnp.float32))[0].astype(jnp.bfloat16)

    skip_terms = jnp.einsum("jkc,jkd->cd", activations, slope_b, preferred_element_type=jnp.float32)
    grad_skip = xor_reduce_scatter(skip_terms, "lat", groups, me) * (1.0 / math.sqrt(lat_total * lon_total))
    through_skip = jnp.einsum("jkd,cd->jkc", slope_b, skip_weight, preferred_element_type=jnp.float32)

    mode_grads = jnp.einsum("jkc,kf->jfc", slope_b, fourier, preferred_element_type=jnp.float32)
    all_mode_grads = gather(mode_grads)
    coeff_grads = jnp.einsum("sfj,jfc->sfc", own_plm, all_mode_grads, precision=highest).astype(jnp.bfloat16)
    weight_grads, back_coeffs = complex_adjoint(coeffs, coeff_grads, spectral_weight, orders)
    back_b = back_coeffs.astype(jnp.bfloat16)
    all_back = gather(back_b).astype(jnp.float32)
    row_grads = jnp.einsum("sfj,sfc->jfc", rows_quad, all_back, precision=highest).astype(jnp.bfloat16)
    through_modes = jnp.einsum("jfc,kf->jkc", row_grads, fourier, preferred_element_type=jnp.float32)
    grad_activations = (upstream.astype(jnp.float32) + through_skip + through_modes).astype(jnp.bfloat16)
    return (grad_activations, weight_grads.astype(jnp.bfloat16), grad_skip)


def solution(mesh):
    in_specs = (
        P(("grp", "lat"), None, None),
        P(("grp", "lat"), None, None),
        P(),
        P("lat", None, None, None),
        P(),
    )
    out_specs = (
        P(("grp", "lat"), None, None),
        P(("grp", "lat"), None, None, None),
        P(("grp", "lat"), None),
    )
    return jax.shard_map(local, mesh=mesh, in_specs=in_specs, out_specs=out_specs, check_vma=False)
```

```python
import math

import jax
import jax.numpy as jnp
import ml_dtypes
import numpy as np
from jax import lax
from jax.sharding import PartitionSpec as P

ORDERS = 4


def fourier_table(lon_total, orders):
    lon_ids = np.arange(lon_total, dtype=np.int64)[:, None]
    order_ids = np.arange(orders, dtype=np.int64)[None, :]
    angles = (lon_ids * order_ids % lon_total).astype(np.float64) * (2.0 * math.pi / lon_total)
    amplitude = math.sqrt(2.0 / lon_total)
    table = np.concatenate([amplitude * np.cos(angles), -amplitude * np.sin(angles)], axis=1)
    return table.astype(ml_dtypes.bfloat16)


def colatitudes(lat_total):
    row_ids = np.arange(lat_total)
    mirror = np.minimum(row_ids, lat_total - 1 - row_ids)
    colatitude = (mirror.astype(np.float64) + 0.5) * (math.pi / lat_total)
    cosines = np.where(row_ids < lat_total // 2, np.cos(colatitude), -np.cos(colatitude))
    return cosines, np.sin(colatitude)


def legendre_table(cosines, sines, degrees, orders):
    rows = cosines.shape[0]
    table = np.zeros((degrees, orders, rows), np.float64)
    factor = math.sqrt(0.5)
    for m in range(orders):
        if m > 0:
            factor *= math.sqrt((2.0 * m + 1.0) / (2.0 * m))
        diagonal = factor * sines**m
        if m < degrees:
            table[m, m] = diagonal
        if m + 1 < degrees:
            table[m + 1, m] = math.sqrt(2.0 * m + 3.0) * cosines * diagonal
        for l in range(m + 2, degrees):
            a = math.sqrt((4.0 * l * l - 1.0) / (l * l - m * m))
            b = math.sqrt(((l - 1.0) ** 2 - m * m) / (4.0 * (l - 1.0) ** 2 - 1.0))
            table[l, m] = a * (cosines * table[l - 1, m] - b * table[l - 2, m])
    return np.concatenate([table, table], axis=1)


def legendre_scan(cosines_np, sines_np, degrees, orders):
    cosines = jnp.asarray(cosines_np.astype(np.float32))
    sines = jnp.asarray(sines_np.astype(np.float32))
    order_col = jnp.arange(orders, dtype=jnp.float32)[:, None]
    factors = [math.sqrt(0.5)]
    for order_num in range(1, orders):
        factors.append(factors[-1] * math.sqrt((2.0 * order_num + 1.0) / (2.0 * order_num)))
    diagonal_start = jnp.array(factors, dtype=jnp.float32)[:, None] * jnp.power(sines[None, :], order_col)
    next_start = jnp.sqrt(2.0 * order_col + 3.0) * cosines[None, :] * diagonal_start

    def advance(state_pair, degree):
        previous, earlier = state_pair
        deg_value = degree.astype(jnp.float32)
        deg_below = deg_value - 1.0
        ratio_up = jnp.sqrt(
            jnp.maximum(4.0 * deg_value * deg_value - 1.0, 1.0)
            / jnp.maximum(deg_value * deg_value - order_col * order_col, 1.0)
        )
        ratio_down = jnp.sqrt(
            jnp.maximum(deg_below * deg_below - order_col * order_col, 0.0)
            / jnp.maximum(4.0 * deg_below * deg_below - 1.0, 1.0)
        )
        recurred = ratio_up * (cosines[None, :] * previous - ratio_down * earlier)
        current = jnp.where(
            deg_value == order_col,
            diagonal_start,
            jnp.where(
                deg_value == order_col + 1.0,
                next_start,
                jnp.where(deg_value > order_col + 1.0, recurred, 0.0),
            ),
        )
        return ((current, previous), current)

    zeroed = jnp.zeros((orders, cosines.shape[0]), jnp.float32)
    _, stacked = lax.scan(advance, (zeroed, zeroed), jnp.arange(degrees, dtype=jnp.int32))
    return jnp.concatenate([stacked, stacked], axis=1)


def gelu_tanh(values):
    return jax.nn.gelu(values, approximate=True)


def xor_reduce_scatter(part, axis_name, groups, me):
    bits = groups.bit_length() - 1
    cur = part
    low = 0
    while low < bits:
        width = min(2, bits - low)
        fan = 1 << width
        view = cur.reshape((cur.shape[0] // fan, fan) + cur.shape[1:])
        mine = (me >> low) & (fan - 1)
        total = lax.dynamic_index_in_dim(view, mine, axis=1, keepdims=False)
        for k in range(1, fan):
            mask = k << low
            sent = lax.dynamic_index_in_dim(view, jnp.bitwise_xor(mine, k), axis=1, keepdims=False)
            total = total + lax.ppermute(sent, axis_name, [(i, i ^ mask) for i in range(groups)])
        cur = total
        low += width
    return cur[0]


def complex_apply(coeffs, weights, orders):
    real_in, imag_in = (coeffs[:, :orders], coeffs[:, orders:])
    real_w, imag_w = (weights[:, 0], weights[:, 1])

    def complex_term(operand_a, operand_b):
        return jnp.einsum("smc,scd->smd", operand_a, operand_b, preferred_element_type=jnp.float32)

    real_out = complex_term(real_in, real_w) - complex_term(imag_in, imag_w)
    imag_out = complex_term(real_in, imag_w) + complex_term(imag_in, real_w)
    return jnp.concatenate([real_out, imag_out], axis=1)


def complex_adjoint(coeffs, cotangents, weights, orders):
    real_in, imag_in = (coeffs[:, :orders], coeffs[:, orders:])
    real_g, imag_g = (cotangents[:, :orders], cotangents[:, orders:])
    real_w, imag_w = (weights[:, 0], weights[:, 1])

    def outer_sum(operand_a, operand_b):
        return jnp.einsum("smc,smd->scd", operand_a, operand_b, preferred_element_type=jnp.float32)

    def back_term(operand_a, operand_b):
        return jnp.einsum("smd,scd->smc", operand_a, operand_b, preferred_element_type=jnp.float32)

    grad_real = outer_sum(real_in, real_g) + outer_sum(imag_in, imag_g)
    grad_imag = outer_sum(real_in, imag_g) - outer_sum(imag_in, real_g)
    back_real = back_term(real_g, real_w) + back_term(imag_g, imag_w)
    back_imag = back_term(imag_g, real_w) - back_term(real_g, imag_w)
    return (
        jnp.stack([grad_real, grad_imag], axis=1),
        jnp.concatenate([back_real, back_imag], axis=1),
    )


def local(activations, upstream, skip_weight, spectral_weight, slot_degree):
    groups = lax.axis_size("lat")
    me = lax.axis_index("lat")
    lat_rows = activations.shape[0]
    lon_total = activations.shape[1]
    lat_total = lat_rows * groups
    per_owner = spectral_weight.shape[0]
    degrees = per_owner * groups
    orders = ORDERS
    highest = lax.Precision.HIGHEST

    fourier = jnp.asarray(fourier_table(lon_total, orders))
    cosines, sines = colatitudes(lat_total)
    plm_np = legendre_table(cosines, sines, degrees, orders)
    quad_np = plm_np * (math.pi / lat_total * sines)[None, None, :]
    if degrees * lat_total <= 64 * 64:
        plm_all = jnp.asarray(plm_np.astype(np.float32))
        quad_all = jnp.asarray(quad_np.astype(np.float32))
    else:
        plm_all = legendre_scan(cosines, sines, degrees, orders)
        quad_all = plm_all * jnp.asarray((math.pi / lat_total * sines).astype(np.float32))[None, None, :]

    own_deg = lax.dynamic_slice_in_dim(slot_degree, me * per_owner, per_owner)
    own_quad = jnp.take(quad_all, own_deg, axis=0)
    own_plm = jnp.take(plm_all, own_deg, axis=0)
    rows_plm = jnp.take(lax.dynamic_slice_in_dim(plm_all, me * lat_rows, lat_rows, axis=2), slot_degree, axis=0)
    rows_quad = jnp.take(lax.dynamic_slice_in_dim(quad_all, me * lat_rows, lat_rows, axis=2), slot_degree, axis=0)

    def to_owners(table, values):
        part = jnp.einsum("sfj,jfc->sfc", table, values, precision=highest)
        part = part.reshape((groups, per_owner) + part.shape[1:])
        return xor_reduce_scatter(part, "lat", groups, me)

    def to_rows(table, values, extra=None):
        part = jnp.einsum("sfj,sfc->jfc", table, values, precision=highest)
        part = part.reshape((groups, -1))
        if extra is not None:
            part = jnp.concatenate([part, extra.reshape((groups, -1))], axis=1)
        out = xor_reduce_scatter(part, "lat", groups, me)
        size = lat_rows * 2 * orders * activations.shape[2]
        return out[:size].reshape((lat_rows, 2 * orders, activations.shape[2])), out[size:]

    spectrum = jnp.einsum("jkc,kf->jfc", activations, fourier, preferred_element_type=jnp.float32)
    coeffs = to_owners(rows_quad, spectrum).astype(jnp.bfloat16)
    filtered = complex_apply(coeffs, spectral_weight, orders).astype(jnp.bfloat16)
    grid_modes = to_rows(own_plm, filtered.astype(jnp.float32))[0].astype(jnp.bfloat16)

    spatial = jnp.einsum("jfc,kf->jkc", grid_modes, fourier, preferred_element_type=jnp.float32)
    skip_out = jnp.einsum("jkc,cd->jkd", activations, skip_weight, preferred_element_type=jnp.float32)
    _, pullback = jax.vjp(gelu_tanh, spatial + skip_out)
    slope_b = pullback(upstream.astype(jnp.float32))[0].astype(jnp.bfloat16)

    skip_terms = jnp.einsum("jkc,jkd->cd", activations, slope_b, preferred_element_type=jnp.float32)
    through_skip = jnp.einsum("jkd,cd->jkc", slope_b, skip_weight, preferred_element_type=jnp.float32)

    mode_grads = jnp.einsum("jkc,kf->jfc", slope_b, fourier, preferred_element_type=jnp.float32)
    coeff_grads = to_owners(rows_plm, mode_grads).astype(jnp.bfloat16)
    weight_grads, back_coeffs = complex_adjoint(coeffs, coeff_grads, spectral_weight, orders)
    back_b = back_coeffs.astype(jnp.bfloat16)
    row_sums, skip_sums = to_rows(own_quad, back_b.astype(jnp.float32), skip_terms)
    row_grads = row_sums.astype(jnp.bfloat16)
    grad_skip = skip_sums.reshape((-1, skip_terms.shape[1])) * (1.0 / math.sqrt(lat_total * lon_total))
    through_modes = jnp.einsum("jfc,kf->jkc", row_grads, fourier, preferred_element_type=jnp.float32)
    grad_activations = (upstream.astype(jnp.float32) + through_skip + through_modes).astype(jnp.bfloat16)
    return (grad_activations, weight_grads.astype(jnp.bfloat16), grad_skip)


def solution(mesh):
    in_specs = (
        P(("grp", "lat"), None, None),
        P(("grp", "lat"), None, None),
        P(),
        P("lat", None, None, None),
        P(),
    )
    out_specs = (
        P(("grp", "lat"), None, None),
        P(("grp", "lat"), None, None, None),
        P(("grp", "lat"), None),
    )
    return jax.shard_map(local, mesh=mesh, in_specs=in_specs, out_specs=out_specs, check_vma=False)
```

```python
import math

import jax
import jax.numpy as jnp
import ml_dtypes
import numpy as np
from jax import lax
from jax.sharding import PartitionSpec as P

ORDERS = 4


def fourier_table(lon_total, orders):
    lon_ids = np.arange(lon_total, dtype=np.int64)[:, None]
    order_ids = np.arange(orders, dtype=np.int64)[None, :]
    angles = (lon_ids * order_ids % lon_total).astype(np.float64) * (2.0 * math.pi / lon_total)
    amplitude = math.sqrt(2.0 / lon_total)
    table = np.concatenate([amplitude * np.cos(angles), -amplitude * np.sin(angles)], axis=1)
    return table.astype(ml_dtypes.bfloat16)


def colatitudes(lat_total):
    row_ids = np.arange(lat_total)
    mirror = np.minimum(row_ids, lat_total - 1 - row_ids)
    colatitude = (mirror.astype(np.float64) + 0.5) * (math.pi / lat_total)
    cosines = np.where(row_ids < lat_total // 2, np.cos(colatitude), -np.cos(colatitude))
    return cosines, np.sin(colatitude)


def legendre_table(cosines, sines, degrees, orders):
    rows = cosines.shape[0]
    table = np.zeros((degrees, orders, rows), np.float64)
    factor = math.sqrt(0.5)
    for m in range(orders):
        if m > 0:
            factor *= math.sqrt((2.0 * m + 1.0) / (2.0 * m))
        diagonal = factor * sines**m
        if m < degrees:
            table[m, m] = diagonal
        if m + 1 < degrees:
            table[m + 1, m] = math.sqrt(2.0 * m + 3.0) * cosines * diagonal
        for l in range(m + 2, degrees):
            a = math.sqrt((4.0 * l * l - 1.0) / (l * l - m * m))
            b = math.sqrt(((l - 1.0) ** 2 - m * m) / (4.0 * (l - 1.0) ** 2 - 1.0))
            table[l, m] = a * (cosines * table[l - 1, m] - b * table[l - 2, m])
    return np.concatenate([table, table], axis=1)


def legendre_scan(cosines_np, sines_np, degrees, orders):
    cosines = jnp.asarray(cosines_np.astype(np.float32))
    sines = jnp.asarray(sines_np.astype(np.float32))
    order_col = jnp.arange(orders, dtype=jnp.float32)[:, None]
    factors = [math.sqrt(0.5)]
    for order_num in range(1, orders):
        factors.append(factors[-1] * math.sqrt((2.0 * order_num + 1.0) / (2.0 * order_num)))
    diagonal_start = jnp.array(factors, dtype=jnp.float32)[:, None] * jnp.power(sines[None, :], order_col)
    next_start = jnp.sqrt(2.0 * order_col + 3.0) * cosines[None, :] * diagonal_start

    def advance(state_pair, degree):
        previous, earlier = state_pair
        deg_value = degree.astype(jnp.float32)
        deg_below = deg_value - 1.0
        ratio_up = jnp.sqrt(
            jnp.maximum(4.0 * deg_value * deg_value - 1.0, 1.0)
            / jnp.maximum(deg_value * deg_value - order_col * order_col, 1.0)
        )
        ratio_down = jnp.sqrt(
            jnp.maximum(deg_below * deg_below - order_col * order_col, 0.0)
            / jnp.maximum(4.0 * deg_below * deg_below - 1.0, 1.0)
        )
        recurred = ratio_up * (cosines[None, :] * previous - ratio_down * earlier)
        current = jnp.where(
            deg_value == order_col,
            diagonal_start,
            jnp.where(
                deg_value == order_col + 1.0,
                next_start,
                jnp.where(deg_value > order_col + 1.0, recurred, 0.0),
            ),
        )
        return ((current, previous), current)

    zeroed = jnp.zeros((orders, cosines.shape[0]), jnp.float32)
    _, stacked = lax.scan(advance, (zeroed, zeroed), jnp.arange(degrees, dtype=jnp.int32))
    return jnp.concatenate([stacked, stacked], axis=1)


def gelu_tanh(values):
    return jax.nn.gelu(values, approximate=True)


def xor_gather_parts(x, axis_name, groups):
    bits = groups.bit_length() - 1
    parts = [x[None]]
    low = 0
    while low < bits:
        width = min(2, bits - low)
        cur = parts[0] if len(parts) == 1 else jnp.concatenate(parts, axis=0)
        parts = [cur]
        for k in range(1, 1 << width):
            mask = k << low
            parts.append(lax.ppermute(cur, axis_name, [(i, i ^ mask) for i in range(groups)]))
        low += width
    return parts


def xor_blocks(table, me, groups, axis):
    bits = groups.bit_length() - 1
    shape = table.shape
    size = shape[axis] // groups
    for b in range(bits):
        view = table.reshape(shape[:axis] + (groups >> (b + 1), 2, size << b) + shape[axis + 1:])
        swapped = jnp.flip(view, axis=axis + 1).reshape(shape)
        table = jnp.where(((me >> b) & 1) == 1, swapped, table)
    return table


def xor_reduce_scatter(part, axis_name, groups, me, high_first):
    bits = groups.bit_length() - 1
    rounds = []
    low = 0
    while low < bits:
        rounds.append((low, min(2, bits - low)))
        low += 2
    if high_first:
        rounds = [(bits - low - width, width) for low, width in rounds]
    cur = part
    for low, width in rounds:
        fan = 1 << width
        rest = cur.shape[1:]
        axis = 0 if high_first else 1
        view = cur.reshape(((fan, cur.shape[0] // fan) if high_first else (cur.shape[0] // fan, fan)) + rest)
        mine = (me >> low) & (fan - 1)
        total = lax.dynamic_index_in_dim(view, mine, axis=axis, keepdims=False)
        for k in range(1, fan):
            mask = k << low
            sent = lax.dynamic_index_in_dim(view, jnp.bitwise_xor(mine, k), axis=axis, keepdims=False)
            total = total + lax.ppermute(sent, axis_name, [(i, i ^ mask) for i in range(groups)])
        cur = total
    return cur[0]


def complex_apply(coeffs, weights, orders):
    real_in, imag_in = (coeffs[:, :orders], coeffs[:, orders:])
    real_w, imag_w = (weights[:, 0], weights[:, 1])

    def complex_term(operand_a, operand_b):
        return jnp.einsum("smc,scd->smd", operand_a, operand_b, preferred_element_type=jnp.float32)

    real_out = complex_term(real_in, real_w) - complex_term(imag_in, imag_w)
    imag_out = complex_term(real_in, imag_w) + complex_term(imag_in, real_w)
    return jnp.concatenate([real_out, imag_out], axis=1)


def complex_adjoint(coeffs, cotangents, weights, orders):
    real_in, imag_in = (coeffs[:, :orders], coeffs[:, orders:])
    real_g, imag_g = (cotangents[:, :orders], cotangents[:, orders:])
    real_w, imag_w = (weights[:, 0], weights[:, 1])

    def outer_sum(operand_a, operand_b):
        return jnp.einsum("smc,smd->scd", operand_a, operand_b, preferred_element_type=jnp.float32)

    def back_term(operand_a, operand_b):
        return jnp.einsum("smd,scd->smc", operand_a, operand_b, preferred_element_type=jnp.float32)

    grad_real = outer_sum(real_in, real_g) + outer_sum(imag_in, imag_g)
    grad_imag = outer_sum(real_in, imag_g) - outer_sum(imag_in, real_g)
    back_real = back_term(real_g, real_w) + back_term(imag_g, imag_w)
    back_imag = back_term(imag_g, real_w) - back_term(real_g, imag_w)
    return (
        jnp.stack([grad_real, grad_imag], axis=1),
        jnp.concatenate([back_real, back_imag], axis=1),
    )


def local(activations, upstream, skip_weight, spectral_weight, slot_degree):
    groups = lax.axis_size("lat")
    me = lax.axis_index("lat")
    lat_rows = activations.shape[0]
    lon_total = activations.shape[1]
    lat_total = lat_rows * groups
    per_owner = spectral_weight.shape[0]
    degrees = per_owner * groups
    orders = ORDERS
    highest = lax.Precision.HIGHEST

    fourier = jnp.asarray(fourier_table(lon_total, orders))
    cosines, sines = colatitudes(lat_total)
    plm_np = legendre_table(cosines, sines, degrees, orders)
    quad_np = plm_np * (math.pi / lat_total * sines)[None, None, :]
    if degrees * lat_total <= 64 * 64:
        plm_all = jnp.asarray(plm_np.astype(np.float32))
        quad_all = jnp.asarray(quad_np.astype(np.float32))
    else:
        plm_all = legendre_scan(cosines, sines, degrees, orders)
        quad_all = plm_all * jnp.asarray((math.pi / lat_total * sines).astype(np.float32))[None, None, :]

    own_deg = lax.dynamic_slice_in_dim(slot_degree, me * per_owner, per_owner)
    own_pick = own_deg[:, None] == jnp.arange(degrees, dtype=jnp.int32)[None, :]
    slot_pick = slot_degree[:, None] == jnp.arange(degrees, dtype=jnp.int32)[None, :]

    def pick(choice, table):
        return jnp.sum(jnp.where(choice[:, :, None, None], table[None], 0.0), axis=1)

    own_quad = xor_blocks(pick(own_pick, quad_all), me, groups, axis=2)
    own_plm = xor_blocks(pick(own_pick, plm_all), me, groups, axis=2)
    my_rows_plm = lax.dynamic_slice_in_dim(plm_all, me * lat_rows, lat_rows, axis=2)
    my_rows_quad = lax.dynamic_slice_in_dim(quad_all, me * lat_rows, lat_rows, axis=2)
    rows_plm = xor_blocks(pick(slot_pick, my_rows_plm), me, groups, axis=0)
    rows_quad = xor_blocks(pick(slot_pick, my_rows_quad), me, groups, axis=0)

    def gathered_sum(values, table, to_rows):
        parts = xor_gather_parts(values, "lat", groups)
        total = None
        start = 0
        for part in parts:
            flat = part.reshape((-1,) + part.shape[2:]).astype(jnp.float32)
            n = flat.shape[0]
            if to_rows:
                piece = jnp.einsum("sfj,sfc->jfc", table[start:start + n], flat, precision=highest)
            else:
                piece = jnp.einsum("sfj,jfc->sfc", table[:, :, start:start + n], flat, precision=highest)
            total = piece if total is None else total + piece
            start += n
        return total

    spectrum = jnp.einsum("jkc,kf->jfc", activations, fourier, preferred_element_type=jnp.float32)
    coeffs = gathered_sum(spectrum, own_quad, False).astype(jnp.bfloat16)
    filtered = complex_apply(coeffs, spectral_weight, orders).astype(jnp.bfloat16)
    grid_modes = gathered_sum(filtered, rows_plm, True).astype(jnp.bfloat16)

    spatial = jnp.einsum("jfc,kf->jkc", grid_modes, fourier, preferred_element_type=jnp.float32)
    skip_out = jnp.einsum("jkc,cd->jkd", activations, skip_weight, preferred_element_type=jnp.float32)
    _, pullback = jax.vjp(gelu_tanh, spatial + skip_out)
    slope_b = pullback(upstream.astype(jnp.float32))[0].astype(jnp.bfloat16)

    skip_terms = jnp.einsum("jkc,jkd->cd", activations, slope_b, preferred_element_type=jnp.float32)
    skip_blocks = skip_terms.reshape((groups, -1) + skip_terms.shape[1:])
    grad_skip = xor_reduce_scatter(skip_blocks, "lat", groups, me, True) * (1.0 / math.sqrt(lat_total * lon_total))
    through_skip = jnp.einsum("jkd,cd->jkc", slope_b, skip_weight, preferred_element_type=jnp.float32)

    mode_grads = jnp.einsum("jkc,kf->jfc", slope_b, fourier, preferred_element_type=jnp.float32)
    coeff_grads = gathered_sum(mode_grads, own_plm, False).astype(jnp.bfloat16)
    weight_grads, back_coeffs = complex_adjoint(coeffs, coeff_grads, spectral_weight, orders)
    row_grads = gathered_sum(back_coeffs.astype(jnp.bfloat16), rows_quad, True).astype(jnp.bfloat16)
    through_modes = jnp.einsum("jfc,kf->jkc", row_grads, fourier, preferred_element_type=jnp.float32)
    grad_activations = (upstream.astype(jnp.float32) + through_skip + through_modes).astype(jnp.bfloat16)
    return (grad_activations, weight_grads.astype(jnp.bfloat16), grad_skip)


def solution(mesh):
    in_specs = (
        P(("grp", "lat"), None, None),
        P(("grp", "lat"), None, None),
        P(),
        P("lat", None, None, None),
        P(),
    )
    out_specs = (
        P(("grp", "lat"), None, None),
        P(("grp", "lat"), None, None, None),
        P(("grp", "lat"), None),
    )
    return jax.shard_map(local, mesh=mesh, in_specs=in_specs, out_specs=out_specs, check_vma=False)
```

```python
import math

import jax
import jax.numpy as jnp
import ml_dtypes
import numpy as np
from jax import lax
from jax.sharding import PartitionSpec as P

ORDERS = 4


def fourier_table(lon_total, orders):
    lon_ids = np.arange(lon_total, dtype=np.int64)[:, None]
    order_ids = np.arange(orders, dtype=np.int64)[None, :]
    angles = (lon_ids * order_ids % lon_total).astype(np.float64) * (2.0 * math.pi / lon_total)
    amplitude = math.sqrt(2.0 / lon_total)
    table = np.concatenate([amplitude * np.cos(angles), -amplitude * np.sin(angles)], axis=1)
    return table.astype(ml_dtypes.bfloat16)


def colatitudes(lat_total):
    row_ids = np.arange(lat_total)
    mirror = np.minimum(row_ids, lat_total - 1 - row_ids)
    colatitude = (mirror.astype(np.float64) + 0.5) * (math.pi / lat_total)
    cosines = np.where(row_ids < lat_total // 2, np.cos(colatitude), -np.cos(colatitude))
    return cosines, np.sin(colatitude)


def legendre_table(cosines, sines, degrees, orders):
    rows = cosines.shape[0]
    table = np.zeros((degrees, orders, rows), np.float64)
    factor = math.sqrt(0.5)
    for m in range(orders):
        if m > 0:
            factor *= math.sqrt((2.0 * m + 1.0) / (2.0 * m))
        diagonal = factor * sines**m
        if m < degrees:
            table[m, m] = diagonal
        if m + 1 < degrees:
            table[m + 1, m] = math.sqrt(2.0 * m + 3.0) * cosines * diagonal
        for l in range(m + 2, degrees):
            a = math.sqrt((4.0 * l * l - 1.0) / (l * l - m * m))
            b = math.sqrt(((l - 1.0) ** 2 - m * m) / (4.0 * (l - 1.0) ** 2 - 1.0))
            table[l, m] = a * (cosines * table[l - 1, m] - b * table[l - 2, m])
    return np.concatenate([table, table], axis=1)


def legendre_scan(cosines_np, sines_np, degrees, orders):
    cosines = jnp.asarray(cosines_np.astype(np.float32))
    sines = jnp.asarray(sines_np.astype(np.float32))
    order_col = jnp.arange(orders, dtype=jnp.float32)[:, None]
    factors = [math.sqrt(0.5)]
    for order_num in range(1, orders):
        factors.append(factors[-1] * math.sqrt((2.0 * order_num + 1.0) / (2.0 * order_num)))
    diagonal_start = jnp.array(factors, dtype=jnp.float32)[:, None] * jnp.power(sines[None, :], order_col)
    next_start = jnp.sqrt(2.0 * order_col + 3.0) * cosines[None, :] * diagonal_start

    def advance(state_pair, degree):
        previous, earlier = state_pair
        deg_value = degree.astype(jnp.float32)
        deg_below = deg_value - 1.0
        ratio_up = jnp.sqrt(
            jnp.maximum(4.0 * deg_value * deg_value - 1.0, 1.0)
            / jnp.maximum(deg_value * deg_value - order_col * order_col, 1.0)
        )
        ratio_down = jnp.sqrt(
            jnp.maximum(deg_below * deg_below - order_col * order_col, 0.0)
            / jnp.maximum(4.0 * deg_below * deg_below - 1.0, 1.0)
        )
        recurred = ratio_up * (cosines[None, :] * previous - ratio_down * earlier)
        current = jnp.where(
            deg_value == order_col,
            diagonal_start,
            jnp.where(
                deg_value == order_col + 1.0,
                next_start,
                jnp.where(deg_value > order_col + 1.0, recurred, 0.0),
            ),
        )
        return ((current, previous), current)

    zeroed = jnp.zeros((orders, cosines.shape[0]), jnp.float32)
    _, stacked = lax.scan(advance, (zeroed, zeroed), jnp.arange(degrees, dtype=jnp.int32))
    return jnp.concatenate([stacked, stacked], axis=1)


def gelu_tanh(values):
    return jax.nn.gelu(values, approximate=True)


def xor_gather(x, axis_name, groups):
    bits = groups.bit_length() - 1
    cur = x[None]
    low = 0
    while low < bits:
        width = min(2, bits - low)
        parts = [cur]
        for k in range(1, 1 << width):
            mask = k << low
            parts.append(lax.ppermute(cur, axis_name, [(i, i ^ mask) for i in range(groups)]))
        cur = jnp.concatenate(parts, axis=0)
        low += width
    return cur


def xor_reduce_scatter(part, axis_name, groups, me):
    bits = groups.bit_length() - 1
    cur = part
    low = 0
    while low < bits:
        width = min(2, bits - low)
        fan = 1 << width
        view = cur.reshape((cur.shape[0] // fan, fan) + cur.shape[1:])
        mine = (me >> low) & (fan - 1)
        total = lax.dynamic_index_in_dim(view, mine, axis=1, keepdims=False)
        for k in range(1, fan):
            mask = k << low
            sent = lax.dynamic_index_in_dim(view, jnp.bitwise_xor(mine, k), axis=1, keepdims=False)
            total = total + lax.ppermute(sent, axis_name, [(i, i ^ mask) for i in range(groups)])
        cur = total
        low += width
    return cur[0]


def complex_apply(coeffs, weights, orders):
    real_in, imag_in = (coeffs[:, :orders], coeffs[:, orders:])
    real_w, imag_w = (weights[:, 0], weights[:, 1])

    def complex_term(operand_a, operand_b):
        return jnp.einsum("smc,scd->smd", operand_a, operand_b, preferred_element_type=jnp.float32)

    real_out = complex_term(real_in, real_w) - complex_term(imag_in, imag_w)
    imag_out = complex_term(real_in, imag_w) + complex_term(imag_in, real_w)
    return jnp.concatenate([real_out, imag_out], axis=1)


def complex_adjoint(coeffs, cotangents, weights, orders):
    real_in, imag_in = (coeffs[:, :orders], coeffs[:, orders:])
    real_g, imag_g = (cotangents[:, :orders], cotangents[:, orders:])
    real_w, imag_w = (weights[:, 0], weights[:, 1])

    def outer_sum(operand_a, operand_b):
        return jnp.einsum("smc,smd->scd", operand_a, operand_b, preferred_element_type=jnp.float32)

    def back_term(operand_a, operand_b):
        return jnp.einsum("smd,scd->smc", operand_a, operand_b, preferred_element_type=jnp.float32)

    grad_real = outer_sum(real_in, real_g) + outer_sum(imag_in, imag_g)
    grad_imag = outer_sum(real_in, imag_g) - outer_sum(imag_in, real_g)
    back_real = back_term(real_g, real_w) + back_term(imag_g, imag_w)
    back_imag = back_term(imag_g, real_w) - back_term(real_g, imag_w)
    return (
        jnp.stack([grad_real, grad_imag], axis=1),
        jnp.concatenate([back_real, back_imag], axis=1),
    )


def local(activations, upstream, skip_weight, spectral_weight, slot_degree):
    groups = lax.axis_size("lat")
    me = lax.axis_index("lat")
    lat_rows = activations.shape[0]
    lon_total = activations.shape[1]
    lat_total = lat_rows * groups
    per_owner = spectral_weight.shape[0]
    degrees = per_owner * groups
    orders = ORDERS
    highest = lax.Precision.HIGHEST

    fourier = jnp.asarray(fourier_table(lon_total, orders))
    cosines, sines = colatitudes(lat_total)
    plm_np = legendre_table(cosines, sines, degrees, orders)
    quad_np = plm_np * (math.pi / lat_total * sines)[None, None, :]
    if degrees * lat_total <= 64 * 64:
        plm_all = jnp.asarray(plm_np.astype(np.float32))
        quad_all = jnp.asarray(quad_np.astype(np.float32))
    else:
        plm_all = legendre_scan(cosines, sines, degrees, orders)
        quad_all = plm_all * jnp.asarray((math.pi / lat_total * sines).astype(np.float32))[None, None, :]

    both = jnp.concatenate([quad_all, plm_all], axis=1).transpose(0, 2, 1)
    row_ids = jnp.arange(lat_total, dtype=jnp.int32)
    row_cols = jnp.bitwise_xor(me, row_ids // lat_rows) * lat_rows + row_ids % lat_rows
    slot_ids = jnp.arange(degrees, dtype=jnp.int32)
    slot_src = jnp.bitwise_xor(me, slot_ids // per_owner) * per_owner + slot_ids % per_owner
    own_deg = lax.dynamic_slice_in_dim(slot_degree, me * per_owner, per_owner)
    own_both = both[own_deg[:, None], row_cols[None, :]]
    my_rows = me * lat_rows + jnp.arange(lat_rows, dtype=jnp.int32)
    rows_both = both[jnp.take(slot_degree, slot_src)[:, None], my_rows[None, :]]
    nf = 2 * orders
    own_quad = own_both[:, :, :nf].transpose(0, 2, 1)
    own_plm = own_both[:, :, nf:].transpose(0, 2, 1)
    rows_quad = rows_both[:, :, :nf].transpose(0, 2, 1)
    rows_plm = rows_both[:, :, nf:].transpose(0, 2, 1)

    def gather(values):
        out = xor_gather(values, "lat", groups)
        return out.reshape((-1,) + out.shape[2:])

    spectrum = jnp.einsum("jkc,kf->jfc", activations, fourier, preferred_element_type=jnp.float32)
    all_spectrum = gather(spectrum)
    coeffs = jnp.einsum("sfj,jfc->sfc", own_quad, all_spectrum, precision=highest).astype(jnp.bfloat16)
    filtered = complex_apply(coeffs, spectral_weight, orders).astype(jnp.bfloat16)
    all_filtered = gather(filtered).astype(jnp.float32)
    grid_modes = jnp.einsum("sfj,sfc->jfc", rows_plm, all_filtered, precision=highest).astype(jnp.bfloat16)

    spatial = jnp.einsum("jfc,kf->jkc", grid_modes, fourier, preferred_element_type=jnp.float32)
    skip_out = jnp.einsum("jkc,cd->jkd", activations, skip_weight, preferred_element_type=jnp.float32)
    _, pullback = jax.vjp(gelu_tanh, spatial + skip_out)
    slope_b = pullback(upstream.astype(jnp.float32))[0].astype(jnp.bfloat16)

    skip_terms = jnp.einsum("jkc,jkd->cd", activations, slope_b, preferred_element_type=jnp.float32)
    skip_blocks = skip_terms.reshape((groups, -1) + skip_terms.shape[1:])
    grad_skip = xor_reduce_scatter(skip_blocks, "lat", groups, me) * (1.0 / math.sqrt(lat_total * lon_total))
    through_skip = jnp.einsum("jkd,cd->jkc", slope_b, skip_weight, preferred_element_type=jnp.float32)

    mode_grads = jnp.einsum("jkc,kf->jfc", slope_b, fourier, preferred_element_type=jnp.float32)
    all_mode_grads = gather(mode_grads)
    coeff_grads = jnp.einsum("sfj,jfc->sfc", own_plm, all_mode_grads, precision=highest).astype(jnp.bfloat16)
    weight_grads, back_coeffs = complex_adjoint(coeffs, coeff_grads, spectral_weight, orders)
    back_b = back_coeffs.astype(jnp.bfloat16)
    all_back = gather(back_b).astype(jnp.float32)
    row_grads = jnp.einsum("sfj,sfc->jfc", rows_quad, all_back, precision=highest).astype(jnp.bfloat16)
    through_modes = jnp.einsum("jfc,kf->jkc", row_grads, fourier, preferred_element_type=jnp.float32)
    grad_activations = (upstream.astype(jnp.float32) + through_skip + through_modes).astype(jnp.bfloat16)
    return (grad_activations, weight_grads.astype(jnp.bfloat16), grad_skip)


def solution(mesh):
    in_specs = (
        P(("grp", "lat"), None, None),
        P(("grp", "lat"), None, None),
        P(),
        P("lat", None, None, None),
        P(),
    )
    out_specs = (
        P(("grp", "lat"), None, None),
        P(("grp", "lat"), None, None, None),
        P(("grp", "lat"), None),
    )
    return jax.shard_map(local, mesh=mesh, in_specs=in_specs, out_specs=out_specs, check_vma=False)
```

```python
import math

import jax
import jax.numpy as jnp
import ml_dtypes
import numpy as np
from jax import lax
from jax.sharding import PartitionSpec as P

ORDERS = 4


def fourier_table(lon_total, orders):
    lon_ids = np.arange(lon_total, dtype=np.int64)[:, None]
    order_ids = np.arange(orders, dtype=np.int64)[None, :]
    angles = (lon_ids * order_ids % lon_total).astype(np.float64) * (2.0 * math.pi / lon_total)
    amplitude = math.sqrt(2.0 / lon_total)
    table = np.concatenate([amplitude * np.cos(angles), -amplitude * np.sin(angles)], axis=1)
    return table.astype(ml_dtypes.bfloat16)


def colatitudes(lat_total):
    row_ids = np.arange(lat_total)
    mirror = np.minimum(row_ids, lat_total - 1 - row_ids)
    colatitude = (mirror.astype(np.float64) + 0.5) * (math.pi / lat_total)
    cosines = np.where(row_ids < lat_total // 2, np.cos(colatitude), -np.cos(colatitude))
    return cosines, np.sin(colatitude)


def legendre_table(cosines, sines, degrees, orders):
    rows = cosines.shape[0]
    table = np.zeros((degrees, orders, rows), np.float64)
    factor = math.sqrt(0.5)
    for m in range(orders):
        if m > 0:
            factor *= math.sqrt((2.0 * m + 1.0) / (2.0 * m))
        diagonal = factor * sines**m
        if m < degrees:
            table[m, m] = diagonal
        if m + 1 < degrees:
            table[m + 1, m] = math.sqrt(2.0 * m + 3.0) * cosines * diagonal
        for l in range(m + 2, degrees):
            a = math.sqrt((4.0 * l * l - 1.0) / (l * l - m * m))
            b = math.sqrt(((l - 1.0) ** 2 - m * m) / (4.0 * (l - 1.0) ** 2 - 1.0))
            table[l, m] = a * (cosines * table[l - 1, m] - b * table[l - 2, m])
    return np.concatenate([table, table], axis=1)


def legendre_scan(cosines_np, sines_np, degrees, orders):
    cosines = jnp.asarray(cosines_np.astype(np.float32))
    sines = jnp.asarray(sines_np.astype(np.float32))
    order_col = jnp.arange(orders, dtype=jnp.float32)[:, None]
    factors = [math.sqrt(0.5)]
    for order_num in range(1, orders):
        factors.append(factors[-1] * math.sqrt((2.0 * order_num + 1.0) / (2.0 * order_num)))
    diagonal_start = jnp.array(factors, dtype=jnp.float32)[:, None] * jnp.power(sines[None, :], order_col)
    next_start = jnp.sqrt(2.0 * order_col + 3.0) * cosines[None, :] * diagonal_start

    def advance(state_pair, degree):
        previous, earlier = state_pair
        deg_value = degree.astype(jnp.float32)
        deg_below = deg_value - 1.0
        ratio_up = jnp.sqrt(
            jnp.maximum(4.0 * deg_value * deg_value - 1.0, 1.0)
            / jnp.maximum(deg_value * deg_value - order_col * order_col, 1.0)
        )
        ratio_down = jnp.sqrt(
            jnp.maximum(deg_below * deg_below - order_col * order_col, 0.0)
            / jnp.maximum(4.0 * deg_below * deg_below - 1.0, 1.0)
        )
        recurred = ratio_up * (cosines[None, :] * previous - ratio_down * earlier)
        current = jnp.where(
            deg_value == order_col,
            diagonal_start,
            jnp.where(
                deg_value == order_col + 1.0,
                next_start,
                jnp.where(deg_value > order_col + 1.0, recurred, 0.0),
            ),
        )
        return ((current, previous), current)

    zeroed = jnp.zeros((orders, cosines.shape[0]), jnp.float32)
    _, stacked = lax.scan(advance, (zeroed, zeroed), jnp.arange(degrees, dtype=jnp.int32))
    return jnp.concatenate([stacked, stacked], axis=1)


def gelu_tanh(values):
    return jax.nn.gelu(values, approximate=True)


def xor_gather(x, axis_name, groups):
    bits = groups.bit_length() - 1
    cur = x[None]
    low = 0
    while low < bits:
        width = min(2, bits - low)
        parts = [cur]
        for k in range(1, 1 << width):
            mask = k << low
            parts.append(lax.ppermute(cur, axis_name, [(i, i ^ mask) for i in range(groups)]))
        cur = jnp.concatenate(parts, axis=0)
        low += width
    return cur


def xor_reduce_scatter(part, axis_name, groups, me):
    bits = groups.bit_length() - 1
    cur = part
    low = 0
    while low < bits:
        width = min(2, bits - low)
        fan = 1 << width
        view = cur.reshape((cur.shape[0] // fan, fan) + cur.shape[1:])
        mine = (me >> low) & (fan - 1)
        total = lax.dynamic_index_in_dim(view, mine, axis=1, keepdims=False)
        for k in range(1, fan):
            mask = k << low
            sent = lax.dynamic_index_in_dim(view, jnp.bitwise_xor(mine, k), axis=1, keepdims=False)
            total = total + lax.ppermute(sent, axis_name, [(i, i ^ mask) for i in range(groups)])
        cur = total
        low += width
    return cur[0]


def xor_exchange(values, table, axis_name, groups, me, lo, spec):
    parts = [values]
    for k in range(1, 1 << lo):
        parts.append(lax.ppermute(values, axis_name, [(i, i ^ k) for i in range(groups)]))
    stacked = jnp.stack(parts).astype(jnp.float32)
    cur = jnp.einsum(spec, table, stacked, precision=lax.Precision.HIGHEST)
    hi = groups.bit_length() - 1 - lo
    b = 0
    while b < hi:
        width = min(2, hi - b)
        fan = 1 << width
        view = cur.reshape((cur.shape[0] // fan, fan) + cur.shape[1:])
        total = view[:, 0]
        for k in range(1, fan):
            mask = k << (lo + b)
            total = total + lax.ppermute(view[:, k], axis_name, [(i, i ^ mask) for i in range(groups)])
        cur = total
        b += width
    return cur[0]


def complex_apply(coeffs, weights, orders):
    real_in, imag_in = (coeffs[:, :orders], coeffs[:, orders:])
    real_w, imag_w = (weights[:, 0], weights[:, 1])

    def complex_term(operand_a, operand_b):
        return jnp.einsum("smc,scd->smd", operand_a, operand_b, preferred_element_type=jnp.float32)

    real_out = complex_term(real_in, real_w) - complex_term(imag_in, imag_w)
    imag_out = complex_term(real_in, imag_w) + complex_term(imag_in, real_w)
    return jnp.concatenate([real_out, imag_out], axis=1)


def complex_adjoint(coeffs, cotangents, weights, orders):
    real_in, imag_in = (coeffs[:, :orders], coeffs[:, orders:])
    real_g, imag_g = (cotangents[:, :orders], cotangents[:, orders:])
    real_w, imag_w = (weights[:, 0], weights[:, 1])

    def outer_sum(operand_a, operand_b):
        return jnp.einsum("smc,smd->scd", operand_a, operand_b, preferred_element_type=jnp.float32)

    def back_term(operand_a, operand_b):
        return jnp.einsum("smd,scd->smc", operand_a, operand_b, preferred_element_type=jnp.float32)

    grad_real = outer_sum(real_in, real_g) + outer_sum(imag_in, imag_g)
    grad_imag = outer_sum(real_in, imag_g) - outer_sum(imag_in, real_g)
    back_real = back_term(real_g, real_w) + back_term(imag_g, imag_w)
    back_imag = back_term(imag_g, real_w) - back_term(real_g, imag_w)
    return (
        jnp.stack([grad_real, grad_imag], axis=1),
        jnp.concatenate([back_real, back_imag], axis=1),
    )


def local(activations, upstream, skip_weight, spectral_weight, slot_degree):
    groups = lax.axis_size("lat")
    me = lax.axis_index("lat")
    lat_rows = activations.shape[0]
    lon_total = activations.shape[1]
    lat_total = lat_rows * groups
    per_owner = spectral_weight.shape[0]
    degrees = per_owner * groups
    orders = ORDERS
    highest = lax.Precision.HIGHEST

    fourier = jnp.asarray(fourier_table(lon_total, orders))
    cosines, sines = colatitudes(lat_total)
    plm_np = legendre_table(cosines, sines, degrees, orders)
    quad_np = plm_np * (math.pi / lat_total * sines)[None, None, :]
    if degrees * lat_total <= 64 * 64:
        plm_all = jnp.asarray(plm_np.astype(np.float32))
        quad_all = jnp.asarray(quad_np.astype(np.float32))
    else:
        plm_all = legendre_scan(cosines, sines, degrees, orders)
        quad_all = plm_all * jnp.asarray((math.pi / lat_total * sines).astype(np.float32))[None, None, :]

    bits = groups.bit_length() - 1
    lo = min(2, bits)
    both = jnp.concatenate([quad_all, plm_all], axis=1).transpose(0, 2, 1)
    near = jnp.bitwise_xor(me, jnp.arange(1 << lo, dtype=jnp.int32))
    far = jnp.bitwise_xor(me >> lo, jnp.arange(groups >> lo, dtype=jnp.int32)) * (1 << lo) + (me & ((1 << lo) - 1))
    slot_r = jnp.arange(per_owner, dtype=jnp.int32)
    row_r = jnp.arange(lat_rows, dtype=jnp.int32)
    far_deg = jnp.take(slot_degree, far[:, None] * per_owner + slot_r[None, :])
    near_rows = near[:, None] * lat_rows + row_r[None, :]
    own_both = both[far_deg[:, :, None, None], near_rows[None, None, :, :]]
    near_deg = jnp.take(slot_degree, near[:, None] * per_owner + slot_r[None, :])
    far_rows = far[:, None] * lat_rows + row_r[None, :]
    rows_both = both[near_deg[None, :, :, None], far_rows[:, None, None, :]]
    nf = 2 * orders
    own_quad, own_plm = own_both[..., :nf], own_both[..., nf:]
    rows_plm, rows_quad = rows_both[..., nf:], rows_both[..., :nf]
    to_owners = "xskrf,krfc->xsfc"
    to_rows = "xksrf,ksfc->xrfc"

    def exchange(values, table, spec):
        return xor_exchange(values, table, "lat", groups, me, lo, spec)

    spectrum = jnp.einsum("jkc,kf->jfc", activations, fourier, preferred_element_type=jnp.float32)
    coeffs = exchange(spectrum, own_quad, to_owners).astype(jnp.bfloat16)
    filtered = complex_apply(coeffs, spectral_weight, orders).astype(jnp.bfloat16)
    grid_modes = exchange(filtered, rows_plm, to_rows).astype(jnp.bfloat16)

    spatial = jnp.einsum("jfc,kf->jkc", grid_modes, fourier, preferred_element_type=jnp.float32)
    skip_out = jnp.einsum("jkc,cd->jkd", activations, skip_weight, preferred_element_type=jnp.float32)
    _, pullback = jax.vjp(gelu_tanh, spatial + skip_out)
    slope_b = pullback(upstream.astype(jnp.float32))[0].astype(jnp.bfloat16)

    skip_terms = jnp.einsum("jkc,jkd->cd", activations, slope_b, preferred_element_type=jnp.float32)
    skip_blocks = skip_terms.reshape((groups, -1) + skip_terms.shape[1:])
    grad_skip = xor_reduce_scatter(skip_blocks, "lat", groups, me) * (1.0 / math.sqrt(lat_total * lon_total))
    through_skip = jnp.einsum("jkd,cd->jkc", slope_b, skip_weight, preferred_element_type=jnp.float32)

    mode_grads = jnp.einsum("jkc,kf->jfc", slope_b, fourier, preferred_element_type=jnp.float32)
    coeff_grads = exchange(mode_grads, own_plm, to_owners).astype(jnp.bfloat16)
    weight_grads, back_coeffs = complex_adjoint(coeffs, coeff_grads, spectral_weight, orders)
    row_grads = exchange(back_coeffs.astype(jnp.bfloat16), rows_quad, to_rows).astype(jnp.bfloat16)
    through_modes = jnp.einsum("jfc,kf->jkc", row_grads, fourier, preferred_element_type=jnp.float32)
    grad_activations = (upstream.astype(jnp.float32) + through_skip + through_modes).astype(jnp.bfloat16)
    return (grad_activations, weight_grads.astype(jnp.bfloat16), grad_skip)


def solution(mesh):
    in_specs = (
        P(("grp", "lat"), None, None),
        P(("grp", "lat"), None, None),
        P(),
        P("lat", None, None, None),
        P(),
    )
    out_specs = (
        P(("grp", "lat"), None, None),
        P(("grp", "lat"), None, None, None),
        P(("grp", "lat"), None),
    )
    return jax.shard_map(local, mesh=mesh, in_specs=in_specs, out_specs=out_specs, check_vma=False)
```

```python
import math

import jax
import jax.numpy as jnp
import ml_dtypes
import numpy as np
from jax import lax
from jax.sharding import PartitionSpec as P

ORDERS = 4


def fourier_table(lon_total, orders):
    lon_ids = np.arange(lon_total, dtype=np.int64)[:, None]
    order_ids = np.arange(orders, dtype=np.int64)[None, :]
    angles = (lon_ids * order_ids % lon_total).astype(np.float64) * (2.0 * math.pi / lon_total)
    amplitude = math.sqrt(2.0 / lon_total)
    table = np.concatenate([amplitude * np.cos(angles), -amplitude * np.sin(angles)], axis=1)
    return table.astype(ml_dtypes.bfloat16)


def colatitudes(lat_total):
    row_ids = np.arange(lat_total)
    mirror = np.minimum(row_ids, lat_total - 1 - row_ids)
    colatitude = (mirror.astype(np.float64) + 0.5) * (math.pi / lat_total)
    cosines = np.where(row_ids < lat_total // 2, np.cos(colatitude), -np.cos(colatitude))
    return cosines, np.sin(colatitude)


def legendre_table(cosines, sines, degrees, orders):
    rows = cosines.shape[0]
    table = np.zeros((degrees, orders, rows), np.float64)
    factor = math.sqrt(0.5)
    for m in range(orders):
        if m > 0:
            factor *= math.sqrt((2.0 * m + 1.0) / (2.0 * m))
        diagonal = factor * sines**m
        if m < degrees:
            table[m, m] = diagonal
        if m + 1 < degrees:
            table[m + 1, m] = math.sqrt(2.0 * m + 3.0) * cosines * diagonal
        for l in range(m + 2, degrees):
            a = math.sqrt((4.0 * l * l - 1.0) / (l * l - m * m))
            b = math.sqrt(((l - 1.0) ** 2 - m * m) / (4.0 * (l - 1.0) ** 2 - 1.0))
            table[l, m] = a * (cosines * table[l - 1, m] - b * table[l - 2, m])
    return np.concatenate([table, table], axis=1)


def legendre_scan(cosines_np, sines_np, degrees, orders):
    cosines = jnp.asarray(cosines_np.astype(np.float32))
    sines = jnp.asarray(sines_np.astype(np.float32))
    order_col = jnp.arange(orders, dtype=jnp.float32)[:, None]
    factors = [math.sqrt(0.5)]
    for order_num in range(1, orders):
        factors.append(factors[-1] * math.sqrt((2.0 * order_num + 1.0) / (2.0 * order_num)))
    diagonal_start = jnp.array(factors, dtype=jnp.float32)[:, None] * jnp.power(sines[None, :], order_col)
    next_start = jnp.sqrt(2.0 * order_col + 3.0) * cosines[None, :] * diagonal_start

    def advance(state_pair, degree):
        previous, earlier = state_pair
        deg_value = degree.astype(jnp.float32)
        deg_below = deg_value - 1.0
        ratio_up = jnp.sqrt(
            jnp.maximum(4.0 * deg_value * deg_value - 1.0, 1.0)
            / jnp.maximum(deg_value * deg_value - order_col * order_col, 1.0)
        )
        ratio_down = jnp.sqrt(
            jnp.maximum(deg_below * deg_below - order_col * order_col, 0.0)
            / jnp.maximum(4.0 * deg_below * deg_below - 1.0, 1.0)
        )
        recurred = ratio_up * (cosines[None, :] * previous - ratio_down * earlier)
        current = jnp.where(
            deg_value == order_col,
            diagonal_start,
            jnp.where(
                deg_value == order_col + 1.0,
                next_start,
                jnp.where(deg_value > order_col + 1.0, recurred, 0.0),
            ),
        )
        return ((current, previous), current)

    zeroed = jnp.zeros((orders, cosines.shape[0]), jnp.float32)
    _, stacked = lax.scan(advance, (zeroed, zeroed), jnp.arange(degrees, dtype=jnp.int32))
    return jnp.concatenate([stacked, stacked], axis=1)


def gelu_tanh(values):
    return jax.nn.gelu(values, approximate=True)


def xor_gather(x, axis_name, groups):
    bits = groups.bit_length() - 1
    cur = x[None]
    low = 0
    while low < bits:
        width = min(2, bits - low)
        parts = [cur]
        for k in range(1, 1 << width):
            mask = k << low
            parts.append(lax.ppermute(cur, axis_name, [(i, i ^ mask) for i in range(groups)]))
        cur = jnp.concatenate(parts, axis=0)
        low += width
    return cur


def xor_reduce_scatter(part, axis_name, groups, me):
    bits = groups.bit_length() - 1
    cur = part
    low = 0
    while low < bits:
        width = min(2, bits - low)
        fan = 1 << width
        view = cur.reshape((cur.shape[0] // fan, fan) + cur.shape[1:])
        mine = (me >> low) & (fan - 1)
        total = lax.dynamic_index_in_dim(view, mine, axis=1, keepdims=False)
        for k in range(1, fan):
            mask = k << low
            sent = lax.dynamic_index_in_dim(view, jnp.bitwise_xor(mine, k), axis=1, keepdims=False)
            total = total + lax.ppermute(sent, axis_name, [(i, i ^ mask) for i in range(groups)])
        cur = total
        low += width
    return cur[0]


def xor_exchange(values, table, axis_name, groups, me, lo, spec, extra=None):
    fan_lo = 1 << lo
    size = values.size
    if extra is not None:
        extra_view = extra.reshape((extra.shape[0] // fan_lo, fan_lo, -1))
        extra_sum = extra_view[:, 0]
    parts = [values.astype(jnp.float32) if extra is not None else values]
    for k in range(1, fan_lo):
        pairs = [(i, i ^ k) for i in range(groups)]
        if extra is None:
            parts.append(lax.ppermute(values, axis_name, pairs))
        else:
            message = jnp.concatenate([values.astype(jnp.float32).reshape(-1), extra_view[:, k].reshape(-1)])
            moved = lax.ppermute(message, axis_name, pairs)
            parts.append(moved[:size].reshape(values.shape))
            extra_sum = extra_sum + moved[size:].reshape(extra_sum.shape)
    stacked = jnp.stack(parts).astype(jnp.float32)
    cur = jnp.einsum(spec, table, stacked, precision=lax.Precision.HIGHEST)
    out_shape = cur.shape[1:]
    cur = cur.reshape((cur.shape[0], -1))
    if extra is not None:
        cur = jnp.concatenate([cur, extra_sum], axis=1)
    hi = groups.bit_length() - 1 - lo
    b = 0
    while b < hi:
        width = min(2, hi - b)
        fan = 1 << width
        view = cur.reshape((cur.shape[0] // fan, fan) + cur.shape[1:])
        total = view[:, 0]
        for k in range(1, fan):
            mask = k << (lo + b)
            total = total + lax.ppermute(view[:, k], axis_name, [(i, i ^ mask) for i in range(groups)])
        cur = total
        b += width
    n = math.prod(out_shape)
    return cur[0, :n].reshape(out_shape), cur[0, n:]


def complex_apply(coeffs, weights, orders):
    real_in, imag_in = (coeffs[:, :orders], coeffs[:, orders:])
    real_w, imag_w = (weights[:, 0], weights[:, 1])

    def complex_term(operand_a, operand_b):
        return jnp.einsum("smc,scd->smd", operand_a, operand_b, preferred_element_type=jnp.float32)

    real_out = complex_term(real_in, real_w) - complex_term(imag_in, imag_w)
    imag_out = complex_term(real_in, imag_w) + complex_term(imag_in, real_w)
    return jnp.concatenate([real_out, imag_out], axis=1)


def complex_adjoint(coeffs, cotangents, weights, orders):
    real_in, imag_in = (coeffs[:, :orders], coeffs[:, orders:])
    real_g, imag_g = (cotangents[:, :orders], cotangents[:, orders:])
    real_w, imag_w = (weights[:, 0], weights[:, 1])

    def outer_sum(operand_a, operand_b):
        return jnp.einsum("smc,smd->scd", operand_a, operand_b, preferred_element_type=jnp.float32)

    def back_term(operand_a, operand_b):
        return jnp.einsum("smd,scd->smc", operand_a, operand_b, preferred_element_type=jnp.float32)

    grad_real = outer_sum(real_in, real_g) + outer_sum(imag_in, imag_g)
    grad_imag = outer_sum(real_in, imag_g) - outer_sum(imag_in, real_g)
    back_real = back_term(real_g, real_w) + back_term(imag_g, imag_w)
    back_imag = back_term(imag_g, real_w) - back_term(real_g, imag_w)
    return (
        jnp.stack([grad_real, grad_imag], axis=1),
        jnp.concatenate([back_real, back_imag], axis=1),
    )


def local(activations, upstream, skip_weight, spectral_weight, slot_degree):
    groups = lax.axis_size("lat")
    me = lax.axis_index("lat")
    lat_rows = activations.shape[0]
    lon_total = activations.shape[1]
    lat_total = lat_rows * groups
    per_owner = spectral_weight.shape[0]
    degrees = per_owner * groups
    orders = ORDERS
    highest = lax.Precision.HIGHEST

    fourier = jnp.asarray(fourier_table(lon_total, orders))
    cosines, sines = colatitudes(lat_total)
    plm_np = legendre_table(cosines, sines, degrees, orders)
    quad_np = plm_np * (math.pi / lat_total * sines)[None, None, :]
    if degrees * lat_total <= 64 * 64:
        plm_all = jnp.asarray(plm_np.astype(np.float32))
        quad_all = jnp.asarray(quad_np.astype(np.float32))
    else:
        plm_all = legendre_scan(cosines, sines, degrees, orders)
        quad_all = plm_all * jnp.asarray((math.pi / lat_total * sines).astype(np.float32))[None, None, :]

    bits = groups.bit_length() - 1
    lo = min(2, bits)
    both = jnp.concatenate([quad_all, plm_all], axis=1).transpose(0, 2, 1)
    near = jnp.bitwise_xor(me, jnp.arange(1 << lo, dtype=jnp.int32))
    far = jnp.bitwise_xor(me >> lo, jnp.arange(groups >> lo, dtype=jnp.int32)) * (1 << lo) + (me & ((1 << lo) - 1))
    slot_r = jnp.arange(per_owner, dtype=jnp.int32)
    row_r = jnp.arange(lat_rows, dtype=jnp.int32)
    far_deg = jnp.take(slot_degree, far[:, None] * per_owner + slot_r[None, :])
    near_rows = near[:, None] * lat_rows + row_r[None, :]
    own_both = both[far_deg[:, :, None, None], near_rows[None, None, :, :]]
    near_deg = jnp.take(slot_degree, near[:, None] * per_owner + slot_r[None, :])
    far_rows = far[:, None] * lat_rows + row_r[None, :]
    rows_both = both[near_deg[None, :, :, None], far_rows[:, None, None, :]]
    nf = 2 * orders
    own_quad, own_plm = own_both[..., :nf], own_both[..., nf:]
    rows_plm, rows_quad = rows_both[..., nf:], rows_both[..., :nf]
    to_owners = "xskrf,krfc->xsfc"
    to_rows = "xksrf,ksfc->xrfc"

    def exchange(values, table, spec, extra=None):
        return xor_exchange(values, table, "lat", groups, me, lo, spec, extra)

    spectrum = jnp.einsum("jkc,kf->jfc", activations, fourier, preferred_element_type=jnp.float32)
    coeffs = exchange(spectrum, own_quad, to_owners)[0].astype(jnp.bfloat16)
    filtered = complex_apply(coeffs, spectral_weight, orders).astype(jnp.bfloat16)
    grid_modes = exchange(filtered, rows_plm, to_rows)[0].astype(jnp.bfloat16)

    spatial = jnp.einsum("jfc,kf->jkc", grid_modes, fourier, preferred_element_type=jnp.float32)
    skip_out = jnp.einsum("jkc,cd->jkd", activations, skip_weight, preferred_element_type=jnp.float32)
    _, pullback = jax.vjp(gelu_tanh, spatial + skip_out)
    slope_b = pullback(upstream.astype(jnp.float32))[0].astype(jnp.bfloat16)

    skip_terms = jnp.einsum("jkc,jkd->cd", activations, slope_b, preferred_element_type=jnp.float32)
    skip_blocks = skip_terms.reshape((groups, -1) + skip_terms.shape[1:])
    skip_rel = jnp.take(skip_blocks, jnp.bitwise_xor(me, jnp.arange(groups, dtype=jnp.int32)), axis=0)
    through_skip = jnp.einsum("jkd,cd->jkc", slope_b, skip_weight, preferred_element_type=jnp.float32)

    mode_grads = jnp.einsum("jkc,kf->jfc", slope_b, fourier, preferred_element_type=jnp.float32)
    coeff_grads = exchange(mode_grads, own_plm, to_owners)[0].astype(jnp.bfloat16)
    weight_grads, back_coeffs = complex_adjoint(coeffs, coeff_grads, spectral_weight, orders)
    row_sums, skip_sums = exchange(back_coeffs.astype(jnp.bfloat16), rows_quad, to_rows, skip_rel)
    row_grads = row_sums.astype(jnp.bfloat16)
    grad_skip = skip_sums.reshape(skip_blocks.shape[1:]) * (1.0 / math.sqrt(lat_total * lon_total))
    through_modes = jnp.einsum("jfc,kf->jkc", row_grads, fourier, preferred_element_type=jnp.float32)
    grad_activations = (upstream.astype(jnp.float32) + through_skip + through_modes).astype(jnp.bfloat16)
    return (grad_activations, weight_grads.astype(jnp.bfloat16), grad_skip)


def solution(mesh):
    in_specs = (
        P(("grp", "lat"), None, None),
        P(("grp", "lat"), None, None),
        P(),
        P("lat", None, None, None),
        P(),
    )
    out_specs = (
        P(("grp", "lat"), None, None),
        P(("grp", "lat"), None, None, None),
        P(("grp", "lat"), None),
    )
    return jax.shard_map(local, mesh=mesh, in_specs=in_specs, out_specs=out_specs, check_vma=False)
```

```python
import math

import jax
import jax.numpy as jnp
import ml_dtypes
import numpy as np
from jax import lax
from jax.sharding import PartitionSpec as P

ORDERS = 4


def fourier_table(lon_total, orders):
    lon_ids = np.arange(lon_total, dtype=np.int64)[:, None]
    order_ids = np.arange(orders, dtype=np.int64)[None, :]
    angles = (lon_ids * order_ids % lon_total).astype(np.float64) * (2.0 * math.pi / lon_total)
    amplitude = math.sqrt(2.0 / lon_total)
    table = np.concatenate([amplitude * np.cos(angles), -amplitude * np.sin(angles)], axis=1)
    return table.astype(ml_dtypes.bfloat16)


def colatitudes(lat_total):
    row_ids = np.arange(lat_total)
    mirror = np.minimum(row_ids, lat_total - 1 - row_ids)
    colatitude = (mirror.astype(np.float64) + 0.5) * (math.pi / lat_total)
    cosines = np.where(row_ids < lat_total // 2, np.cos(colatitude), -np.cos(colatitude))
    return cosines, np.sin(colatitude)


def legendre_table(cosines, sines, degrees, orders):
    rows = cosines.shape[0]
    table = np.zeros((degrees, orders, rows), np.float64)
    factor = math.sqrt(0.5)
    for m in range(orders):
        if m > 0:
            factor *= math.sqrt((2.0 * m + 1.0) / (2.0 * m))
        diagonal = factor * sines**m
        if m < degrees:
            table[m, m] = diagonal
        if m + 1 < degrees:
            table[m + 1, m] = math.sqrt(2.0 * m + 3.0) * cosines * diagonal
        for l in range(m + 2, degrees):
            a = math.sqrt((4.0 * l * l - 1.0) / (l * l - m * m))
            b = math.sqrt(((l - 1.0) ** 2 - m * m) / (4.0 * (l - 1.0) ** 2 - 1.0))
            table[l, m] = a * (cosines * table[l - 1, m] - b * table[l - 2, m])
    return np.concatenate([table, table], axis=1)


def legendre_scan(cosines_np, sines_np, degrees, orders):
    cosines = jnp.asarray(cosines_np.astype(np.float32))
    sines = jnp.asarray(sines_np.astype(np.float32))
    order_col = jnp.arange(orders, dtype=jnp.float32)[:, None]
    factors = [math.sqrt(0.5)]
    for order_num in range(1, orders):
        factors.append(factors[-1] * math.sqrt((2.0 * order_num + 1.0) / (2.0 * order_num)))
    diagonal_start = jnp.array(factors, dtype=jnp.float32)[:, None] * jnp.power(sines[None, :], order_col)
    next_start = jnp.sqrt(2.0 * order_col + 3.0) * cosines[None, :] * diagonal_start

    def advance(state_pair, degree):
        previous, earlier = state_pair
        deg_value = degree.astype(jnp.float32)
        deg_below = deg_value - 1.0
        ratio_up = jnp.sqrt(
            jnp.maximum(4.0 * deg_value * deg_value - 1.0, 1.0)
            / jnp.maximum(deg_value * deg_value - order_col * order_col, 1.0)
        )
        ratio_down = jnp.sqrt(
            jnp.maximum(deg_below * deg_below - order_col * order_col, 0.0)
            / jnp.maximum(4.0 * deg_below * deg_below - 1.0, 1.0)
        )
        recurred = ratio_up * (cosines[None, :] * previous - ratio_down * earlier)
        current = jnp.where(
            deg_value == order_col,
            diagonal_start,
            jnp.where(
                deg_value == order_col + 1.0,
                next_start,
                jnp.where(deg_value > order_col + 1.0, recurred, 0.0),
            ),
        )
        return ((current, previous), current)

    zeroed = jnp.zeros((orders, cosines.shape[0]), jnp.float32)
    _, stacked = lax.scan(advance, (zeroed, zeroed), jnp.arange(degrees, dtype=jnp.int32))
    return jnp.concatenate([stacked, stacked], axis=1)


def gelu_tanh(values):
    return jax.nn.gelu(values, approximate=True)


def xor_gather(x, axis_name, groups):
    bits = groups.bit_length() - 1
    cur = x[None]
    low = 0
    while low < bits:
        width = min(2, bits - low)
        parts = [cur]
        for k in range(1, 1 << width):
            mask = k << low
            parts.append(lax.ppermute(cur, axis_name, [(i, i ^ mask) for i in range(groups)]))
        cur = jnp.concatenate(parts, axis=0)
        low += width
    return cur


def xor_reduce_scatter(part, axis_name, groups, me):
    bits = groups.bit_length() - 1
    cur = part
    low = 0
    while low < bits:
        width = min(2, bits - low)
        fan = 1 << width
        view = cur.reshape((cur.shape[0] // fan, fan) + cur.shape[1:])
        mine = (me >> low) & (fan - 1)
        total = lax.dynamic_index_in_dim(view, mine, axis=1, keepdims=False)
        for k in range(1, fan):
            mask = k << low
            sent = lax.dynamic_index_in_dim(view, jnp.bitwise_xor(mine, k), axis=1, keepdims=False)
            total = total + lax.ppermute(sent, axis_name, [(i, i ^ mask) for i in range(groups)])
        cur = total
        low += width
    return cur[0]


def xor_exchange(values, table, axis_name, groups, me, lo, spec):
    parts = [values]
    for k in range(1, 1 << lo):
        parts.append(lax.ppermute(values, axis_name, [(i, i ^ k) for i in range(groups)]))
    stacked = jnp.stack(parts).astype(jnp.float32)
    hi = groups.bit_length() - 1 - lo
    if hi == 0:
        return jnp.einsum(spec, table, stacked, precision=lax.Precision.HIGHEST)[0]
    width = min(2, hi)
    fan = 1 << width
    tables = table.reshape((table.shape[0] // fan, fan) + table.shape[1:])
    cur = None
    for k in range(fan):
        piece = jnp.einsum(spec, tables[:, k], stacked, precision=lax.Precision.HIGHEST)
        if k > 0:
            mask = k << lo
            piece = lax.ppermute(piece, axis_name, [(i, i ^ mask) for i in range(groups)])
        cur = piece if cur is None else cur + piece
    b = width
    while b < hi:
        width = min(2, hi - b)
        fan = 1 << width
        view = cur.reshape((cur.shape[0] // fan, fan) + cur.shape[1:])
        total = view[:, 0]
        for k in range(1, fan):
            mask = k << (lo + b)
            total = total + lax.ppermute(view[:, k], axis_name, [(i, i ^ mask) for i in range(groups)])
        cur = total
        b += width
    return cur[0]


def complex_apply(coeffs, weights, orders):
    real_in, imag_in = (coeffs[:, :orders], coeffs[:, orders:])
    real_w, imag_w = (weights[:, 0], weights[:, 1])

    def complex_term(operand_a, operand_b):
        return jnp.einsum("smc,scd->smd", operand_a, operand_b, preferred_element_type=jnp.float32)

    real_out = complex_term(real_in, real_w) - complex_term(imag_in, imag_w)
    imag_out = complex_term(real_in, imag_w) + complex_term(imag_in, real_w)
    return jnp.concatenate([real_out, imag_out], axis=1)


def complex_adjoint(coeffs, cotangents, weights, orders):
    real_in, imag_in = (coeffs[:, :orders], coeffs[:, orders:])
    real_g, imag_g = (cotangents[:, :orders], cotangents[:, orders:])
    real_w, imag_w = (weights[:, 0], weights[:, 1])

    def outer_sum(operand_a, operand_b):
        return jnp.einsum("smc,smd->scd", operand_a, operand_b, preferred_element_type=jnp.float32)

    def back_term(operand_a, operand_b):
        return jnp.einsum("smd,scd->smc", operand_a, operand_b, preferred_element_type=jnp.float32)

    grad_real = outer_sum(real_in, real_g) + outer_sum(imag_in, imag_g)
    grad_imag = outer_sum(real_in, imag_g) - outer_sum(imag_in, real_g)
    back_real = back_term(real_g, real_w) + back_term(imag_g, imag_w)
    back_imag = back_term(imag_g, real_w) - back_term(real_g, imag_w)
    return (
        jnp.stack([grad_real, grad_imag], axis=1),
        jnp.concatenate([back_real, back_imag], axis=1),
    )


def local(activations, upstream, skip_weight, spectral_weight, slot_degree):
    groups = lax.axis_size("lat")
    me = lax.axis_index("lat")
    lat_rows = activations.shape[0]
    lon_total = activations.shape[1]
    lat_total = lat_rows * groups
    per_owner = spectral_weight.shape[0]
    degrees = per_owner * groups
    orders = ORDERS
    highest = lax.Precision.HIGHEST

    fourier = jnp.asarray(fourier_table(lon_total, orders))
    cosines, sines = colatitudes(lat_total)
    plm_np = legendre_table(cosines, sines, degrees, orders)
    quad_np = plm_np * (math.pi / lat_total * sines)[None, None, :]
    if degrees * lat_total <= 64 * 64:
        plm_all = jnp.asarray(plm_np.astype(np.float32))
        quad_all = jnp.asarray(quad_np.astype(np.float32))
    else:
        plm_all = legendre_scan(cosines, sines, degrees, orders)
        quad_all = plm_all * jnp.asarray((math.pi / lat_total * sines).astype(np.float32))[None, None, :]

    bits = groups.bit_length() - 1
    lo = min(2, bits)
    both = jnp.concatenate([quad_all, plm_all], axis=1).transpose(0, 2, 1)
    near = jnp.bitwise_xor(me, jnp.arange(1 << lo, dtype=jnp.int32))
    far = jnp.bitwise_xor(me >> lo, jnp.arange(groups >> lo, dtype=jnp.int32)) * (1 << lo) + (me & ((1 << lo) - 1))
    slot_r = jnp.arange(per_owner, dtype=jnp.int32)
    row_r = jnp.arange(lat_rows, dtype=jnp.int32)
    far_deg = jnp.take(slot_degree, far[:, None] * per_owner + slot_r[None, :])
    near_rows = near[:, None] * lat_rows + row_r[None, :]
    own_both = both[far_deg[:, :, None, None], near_rows[None, None, :, :]]
    near_deg = jnp.take(slot_degree, near[:, None] * per_owner + slot_r[None, :])
    far_rows = far[:, None] * lat_rows + row_r[None, :]
    rows_both = both[near_deg[None, :, :, None], far_rows[:, None, None, :]]
    nf = 2 * orders
    own_quad, own_plm = own_both[..., :nf], own_both[..., nf:]
    rows_plm, rows_quad = rows_both[..., nf:], rows_both[..., :nf]
    to_owners = "xskrf,krfc->xsfc"
    to_rows = "xksrf,ksfc->xrfc"

    def exchange(values, table, spec):
        return xor_exchange(values, table, "lat", groups, me, lo, spec)

    spectrum = jnp.einsum("jkc,kf->jfc", activations, fourier, preferred_element_type=jnp.float32)
    coeffs = exchange(spectrum, own_quad, to_owners).astype(jnp.bfloat16)
    filtered = complex_apply(coeffs, spectral_weight, orders).astype(jnp.bfloat16)
    grid_modes = exchange(filtered, rows_plm, to_rows).astype(jnp.bfloat16)

    spatial = jnp.einsum("jfc,kf->jkc", grid_modes, fourier, preferred_element_type=jnp.float32)
    skip_out = jnp.einsum("jkc,cd->jkd", activations, skip_weight, preferred_element_type=jnp.float32)
    _, pullback = jax.vjp(gelu_tanh, spatial + skip_out)
    slope_b = pullback(upstream.astype(jnp.float32))[0].astype(jnp.bfloat16)

    skip_terms = jnp.einsum("jkc,jkd->cd", activations, slope_b, preferred_element_type=jnp.float32)
    skip_blocks = skip_terms.reshape((groups, -1) + skip_terms.shape[1:])
    grad_skip = xor_reduce_scatter(skip_blocks, "lat", groups, me) * (1.0 / math.sqrt(lat_total * lon_total))
    through_skip = jnp.einsum("jkd,cd->jkc", slope_b, skip_weight, preferred_element_type=jnp.float32)

    mode_grads = jnp.einsum("jkc,kf->jfc", slope_b, fourier, preferred_element_type=jnp.float32)
    coeff_grads = exchange(mode_grads, own_plm, to_owners).astype(jnp.bfloat16)
    weight_grads, back_coeffs = complex_adjoint(coeffs, coeff_grads, spectral_weight, orders)
    row_grads = exchange(back_coeffs.astype(jnp.bfloat16), rows_quad, to_rows).astype(jnp.bfloat16)
    through_modes = jnp.einsum("jfc,kf->jkc", row_grads, fourier, preferred_element_type=jnp.float32)
    grad_activations = (upstream.astype(jnp.float32) + through_skip + through_modes).astype(jnp.bfloat16)
    return (grad_activations, weight_grads.astype(jnp.bfloat16), grad_skip)


def solution(mesh):
    in_specs = (
        P(("grp", "lat"), None, None),
        P(("grp", "lat"), None, None),
        P(),
        P("lat", None, None, None),
        P(),
    )
    out_specs = (
        P(("grp", "lat"), None, None),
        P(("grp", "lat"), None, None, None),
        P(("grp", "lat"), None),
    )
    return jax.shard_map(local, mesh=mesh, in_specs=in_specs, out_specs=out_specs, check_vma=False)
```

```python
import math

import jax
import jax.numpy as jnp
import ml_dtypes
import numpy as np
from jax import lax
from jax.sharding import PartitionSpec as P

ORDERS = 4


def fourier_table(lon_total, orders):
    lon_ids = np.arange(lon_total, dtype=np.int64)[:, None]
    order_ids = np.arange(orders, dtype=np.int64)[None, :]
    angles = (lon_ids * order_ids % lon_total).astype(np.float64) * (2.0 * math.pi / lon_total)
    amplitude = math.sqrt(2.0 / lon_total)
    table = np.concatenate([amplitude * np.cos(angles), -amplitude * np.sin(angles)], axis=1)
    return table.astype(ml_dtypes.bfloat16)


def colatitudes(lat_total):
    row_ids = np.arange(lat_total)
    mirror = np.minimum(row_ids, lat_total - 1 - row_ids)
    colatitude = (mirror.astype(np.float64) + 0.5) * (math.pi / lat_total)
    cosines = np.where(row_ids < lat_total // 2, np.cos(colatitude), -np.cos(colatitude))
    return cosines, np.sin(colatitude)


def legendre_table(cosines, sines, degrees, orders):
    rows = cosines.shape[0]
    table = np.zeros((degrees, orders, rows), np.float64)
    factor = math.sqrt(0.5)
    for m in range(orders):
        if m > 0:
            factor *= math.sqrt((2.0 * m + 1.0) / (2.0 * m))
        diagonal = factor * sines**m
        if m < degrees:
            table[m, m] = diagonal
        if m + 1 < degrees:
            table[m + 1, m] = math.sqrt(2.0 * m + 3.0) * cosines * diagonal
        for l in range(m + 2, degrees):
            a = math.sqrt((4.0 * l * l - 1.0) / (l * l - m * m))
            b = math.sqrt(((l - 1.0) ** 2 - m * m) / (4.0 * (l - 1.0) ** 2 - 1.0))
            table[l, m] = a * (cosines * table[l - 1, m] - b * table[l - 2, m])
    return np.concatenate([table, table], axis=1)


def legendre_scan(cosines_np, sines_np, degrees, orders):
    cosines = jnp.asarray(cosines_np.astype(np.float32))
    sines = jnp.asarray(sines_np.astype(np.float32))
    order_col = jnp.arange(orders, dtype=jnp.float32)[:, None]
    factors = [math.sqrt(0.5)]
    for order_num in range(1, orders):
        factors.append(factors[-1] * math.sqrt((2.0 * order_num + 1.0) / (2.0 * order_num)))
    diagonal_start = jnp.array(factors, dtype=jnp.float32)[:, None] * jnp.power(sines[None, :], order_col)
    next_start = jnp.sqrt(2.0 * order_col + 3.0) * cosines[None, :] * diagonal_start

    def advance(state_pair, degree):
        previous, earlier = state_pair
        deg_value = degree.astype(jnp.float32)
        deg_below = deg_value - 1.0
        ratio_up = jnp.sqrt(
            jnp.maximum(4.0 * deg_value * deg_value - 1.0, 1.0)
            / jnp.maximum(deg_value * deg_value - order_col * order_col, 1.0)
        )
        ratio_down = jnp.sqrt(
            jnp.maximum(deg_below * deg_below - order_col * order_col, 0.0)
            / jnp.maximum(4.0 * deg_below * deg_below - 1.0, 1.0)
        )
        recurred = ratio_up * (cosines[None, :] * previous - ratio_down * earlier)
        current = jnp.where(
            deg_value == order_col,
            diagonal_start,
            jnp.where(
                deg_value == order_col + 1.0,
                next_start,
                jnp.where(deg_value > order_col + 1.0, recurred, 0.0),
            ),
        )
        return ((current, previous), current)

    zeroed = jnp.zeros((orders, cosines.shape[0]), jnp.float32)
    _, stacked = lax.scan(advance, (zeroed, zeroed), jnp.arange(degrees, dtype=jnp.int32))
    return jnp.concatenate([stacked, stacked], axis=1)


def gelu_tanh(values):
    return jax.nn.gelu(values, approximate=True)


def xor_gather(x, axis_name, groups):
    bits = groups.bit_length() - 1
    cur = x[None]
    low = 0
    while low < bits:
        width = min(2, bits - low)
        parts = [cur]
        for k in range(1, 1 << width):
            mask = k << low
            parts.append(lax.ppermute(cur, axis_name, [(i, i ^ mask) for i in range(groups)]))
        cur = jnp.concatenate(parts, axis=0)
        low += width
    return cur


def xor_reduce_scatter(part, axis_name, groups, me, step=2):
    bits = groups.bit_length() - 1
    cur = part
    low = 0
    while low < bits:
        width = min(step, bits - low)
        fan = 1 << width
        view = cur.reshape((cur.shape[0] // fan, fan) + cur.shape[1:])
        mine = (me >> low) & (fan - 1)
        total = lax.dynamic_index_in_dim(view, mine, axis=1, keepdims=False)
        for k in range(1, fan):
            mask = k << low
            sent = lax.dynamic_index_in_dim(view, jnp.bitwise_xor(mine, k), axis=1, keepdims=False)
            total = total + lax.ppermute(sent, axis_name, [(i, i ^ mask) for i in range(groups)])
        cur = total
        low += width
    return cur[0]


def xor_exchange(values, table, axis_name, groups, me, lo, spec):
    parts = [values]
    for k in range(1, 1 << lo):
        parts.append(lax.ppermute(values, axis_name, [(i, i ^ k) for i in range(groups)]))
    stacked = jnp.stack(parts).astype(jnp.float32)
    cur = jnp.einsum(spec, table, stacked, precision=lax.Precision.HIGHEST)
    hi = groups.bit_length() - 1 - lo
    b = 0
    while b < hi:
        width = min(2, hi - b)
        fan = 1 << width
        view = cur.reshape((cur.shape[0] // fan, fan) + cur.shape[1:])
        total = view[:, 0]
        for k in range(1, fan):
            mask = k << (lo + b)
            total = total + lax.ppermute(view[:, k], axis_name, [(i, i ^ mask) for i in range(groups)])
        cur = total
        b += width
    return cur[0]


def complex_apply(coeffs, weights, orders):
    real_in, imag_in = (coeffs[:, :orders], coeffs[:, orders:])
    real_w, imag_w = (weights[:, 0], weights[:, 1])

    def complex_term(operand_a, operand_b):
        return jnp.einsum("smc,scd->smd", operand_a, operand_b, preferred_element_type=jnp.float32)

    real_out = complex_term(real_in, real_w) - complex_term(imag_in, imag_w)
    imag_out = complex_term(real_in, imag_w) + complex_term(imag_in, real_w)
    return jnp.concatenate([real_out, imag_out], axis=1)


def complex_adjoint(coeffs, cotangents, weights, orders):
    real_in, imag_in = (coeffs[:, :orders], coeffs[:, orders:])
    real_g, imag_g = (cotangents[:, :orders], cotangents[:, orders:])
    real_w, imag_w = (weights[:, 0], weights[:, 1])

    def outer_sum(operand_a, operand_b):
        return jnp.einsum("smc,smd->scd", operand_a, operand_b, preferred_element_type=jnp.float32)

    def back_term(operand_a, operand_b):
        return jnp.einsum("smd,scd->smc", operand_a, operand_b, preferred_element_type=jnp.float32)

    grad_real = outer_sum(real_in, real_g) + outer_sum(imag_in, imag_g)
    grad_imag = outer_sum(real_in, imag_g) - outer_sum(imag_in, real_g)
    back_real = back_term(real_g, real_w) + back_term(imag_g, imag_w)
    back_imag = back_term(imag_g, real_w) - back_term(real_g, imag_w)
    return (
        jnp.stack([grad_real, grad_imag], axis=1),
        jnp.concatenate([back_real, back_imag], axis=1),
    )


def local(activations, upstream, skip_weight, spectral_weight, slot_degree):
    groups = lax.axis_size("lat")
    me = lax.axis_index("lat")
    lat_rows = activations.shape[0]
    lon_total = activations.shape[1]
    lat_total = lat_rows * groups
    per_owner = spectral_weight.shape[0]
    degrees = per_owner * groups
    orders = ORDERS
    highest = lax.Precision.HIGHEST

    fourier = jnp.asarray(fourier_table(lon_total, orders))
    cosines, sines = colatitudes(lat_total)
    plm_np = legendre_table(cosines, sines, degrees, orders)
    quad_np = plm_np * (math.pi / lat_total * sines)[None, None, :]
    if degrees * lat_total <= 64 * 64:
        plm_all = jnp.asarray(plm_np.astype(np.float32))
        quad_all = jnp.asarray(quad_np.astype(np.float32))
    else:
        plm_all = legendre_scan(cosines, sines, degrees, orders)
        quad_all = plm_all * jnp.asarray((math.pi / lat_total * sines).astype(np.float32))[None, None, :]

    bits = groups.bit_length() - 1
    lo = min(2, bits)
    both = jnp.concatenate([quad_all, plm_all], axis=1).transpose(0, 2, 1)
    near = jnp.bitwise_xor(me, jnp.arange(1 << lo, dtype=jnp.int32))
    far = jnp.bitwise_xor(me >> lo, jnp.arange(groups >> lo, dtype=jnp.int32)) * (1 << lo) + (me & ((1 << lo) - 1))
    slot_r = jnp.arange(per_owner, dtype=jnp.int32)
    row_r = jnp.arange(lat_rows, dtype=jnp.int32)
    far_deg = jnp.take(slot_degree, far[:, None] * per_owner + slot_r[None, :])
    near_rows = near[:, None] * lat_rows + row_r[None, :]
    own_both = both[far_deg[:, :, None, None], near_rows[None, None, :, :]]
    near_deg = jnp.take(slot_degree, near[:, None] * per_owner + slot_r[None, :])
    far_rows = far[:, None] * lat_rows + row_r[None, :]
    rows_both = both[near_deg[None, :, :, None], far_rows[:, None, None, :]]
    nf = 2 * orders
    own_quad, own_plm = own_both[..., :nf], own_both[..., nf:]
    rows_plm, rows_quad = rows_both[..., nf:], rows_both[..., :nf]
    to_owners = "xskrf,krfc->xsfc"
    to_rows = "xksrf,ksfc->xrfc"

    def exchange(values, table, spec):
        return xor_exchange(values, table, "lat", groups, me, lo, spec)

    spectrum = jnp.einsum("jkc,kf->jfc", activations, fourier, preferred_element_type=jnp.float32)
    coeffs = exchange(spectrum, own_quad, to_owners).astype(jnp.bfloat16)
    filtered = complex_apply(coeffs, spectral_weight, orders).astype(jnp.bfloat16)
    grid_modes = exchange(filtered, rows_plm, to_rows).astype(jnp.bfloat16)

    spatial = jnp.einsum("jfc,kf->jkc", grid_modes, fourier, preferred_element_type=jnp.float32)
    skip_out = jnp.einsum("jkc,cd->jkd", activations, skip_weight, preferred_element_type=jnp.float32)
    _, pullback = jax.vjp(gelu_tanh, spatial + skip_out)
    slope_b = pullback(upstream.astype(jnp.float32))[0].astype(jnp.bfloat16)

    skip_terms = jnp.einsum("jkc,jkd->cd", activations, slope_b, preferred_element_type=jnp.float32)
    skip_blocks = skip_terms.reshape((groups, -1) + skip_terms.shape[1:])
    grad_skip = xor_reduce_scatter(skip_blocks, "lat", groups, me, 1) * (1.0 / math.sqrt(lat_total * lon_total))
    through_skip = jnp.einsum("jkd,cd->jkc", slope_b, skip_weight, preferred_element_type=jnp.float32)

    mode_grads = jnp.einsum("jkc,kf->jfc", slope_b, fourier, preferred_element_type=jnp.float32)
    coeff_grads = exchange(mode_grads, own_plm, to_owners).astype(jnp.bfloat16)
    weight_grads, back_coeffs = complex_adjoint(coeffs, coeff_grads, spectral_weight, orders)
    row_grads = exchange(back_coeffs.astype(jnp.bfloat16), rows_quad, to_rows).astype(jnp.bfloat16)
    through_modes = jnp.einsum("jfc,kf->jkc", row_grads, fourier, preferred_element_type=jnp.float32)
    grad_activations = (upstream.astype(jnp.float32) + through_skip + through_modes).astype(jnp.bfloat16)
    return (grad_activations, weight_grads.astype(jnp.bfloat16), grad_skip)


def solution(mesh):
    in_specs = (
        P(("grp", "lat"), None, None),
        P(("grp", "lat"), None, None),
        P(),
        P("lat", None, None, None),
        P(),
    )
    out_specs = (
        P(("grp", "lat"), None, None),
        P(("grp", "lat"), None, None, None),
        P(("grp", "lat"), None),
    )
    return jax.shard_map(local, mesh=mesh, in_specs=in_specs, out_specs=out_specs, check_vma=False)
```

```python
import math

import jax
import jax.numpy as jnp
import ml_dtypes
import numpy as np
from jax import lax
from jax.sharding import PartitionSpec as P

ORDERS = 4


def fourier_table(lon_total, orders):
    lon_ids = np.arange(lon_total, dtype=np.int64)[:, None]
    order_ids = np.arange(orders, dtype=np.int64)[None, :]
    angles = (lon_ids * order_ids % lon_total).astype(np.float64) * (2.0 * math.pi / lon_total)
    amplitude = math.sqrt(2.0 / lon_total)
    table = np.concatenate([amplitude * np.cos(angles), -amplitude * np.sin(angles)], axis=1)
    return table.astype(ml_dtypes.bfloat16)


def colatitudes(lat_total):
    row_ids = np.arange(lat_total)
    mirror = np.minimum(row_ids, lat_total - 1 - row_ids)
    colatitude = (mirror.astype(np.float64) + 0.5) * (math.pi / lat_total)
    cosines = np.where(row_ids < lat_total // 2, np.cos(colatitude), -np.cos(colatitude))
    return cosines, np.sin(colatitude)


def legendre_table(cosines, sines, degrees, orders):
    rows = cosines.shape[0]
    table = np.zeros((degrees, orders, rows), np.float64)
    factor = math.sqrt(0.5)
    for m in range(orders):
        if m > 0:
            factor *= math.sqrt((2.0 * m + 1.0) / (2.0 * m))
        diagonal = factor * sines**m
        if m < degrees:
            table[m, m] = diagonal
        if m + 1 < degrees:
            table[m + 1, m] = math.sqrt(2.0 * m + 3.0) * cosines * diagonal
        for l in range(m + 2, degrees):
            a = math.sqrt((4.0 * l * l - 1.0) / (l * l - m * m))
            b = math.sqrt(((l - 1.0) ** 2 - m * m) / (4.0 * (l - 1.0) ** 2 - 1.0))
            table[l, m] = a * (cosines * table[l - 1, m] - b * table[l - 2, m])
    return np.concatenate([table, table], axis=1)


def legendre_scan(cosines_np, sines_np, degrees, orders):
    cosines = jnp.asarray(cosines_np.astype(np.float32))
    sines = jnp.asarray(sines_np.astype(np.float32))
    order_col = jnp.arange(orders, dtype=jnp.float32)[:, None]
    factors = [math.sqrt(0.5)]
    for order_num in range(1, orders):
        factors.append(factors[-1] * math.sqrt((2.0 * order_num + 1.0) / (2.0 * order_num)))
    diagonal_start = jnp.array(factors, dtype=jnp.float32)[:, None] * jnp.power(sines[None, :], order_col)
    next_start = jnp.sqrt(2.0 * order_col + 3.0) * cosines[None, :] * diagonal_start

    def advance(state_pair, degree):
        previous, earlier = state_pair
        deg_value = degree.astype(jnp.float32)
        deg_below = deg_value - 1.0
        ratio_up = jnp.sqrt(
            jnp.maximum(4.0 * deg_value * deg_value - 1.0, 1.0)
            / jnp.maximum(deg_value * deg_value - order_col * order_col, 1.0)
        )
        ratio_down = jnp.sqrt(
            jnp.maximum(deg_below * deg_below - order_col * order_col, 0.0)
            / jnp.maximum(4.0 * deg_below * deg_below - 1.0, 1.0)
        )
        recurred = ratio_up * (cosines[None, :] * previous - ratio_down * earlier)
        current = jnp.where(
            deg_value == order_col,
            diagonal_start,
            jnp.where(
                deg_value == order_col + 1.0,
                next_start,
                jnp.where(deg_value > order_col + 1.0, recurred, 0.0),
            ),
        )
        return ((current, previous), current)

    zeroed = jnp.zeros((orders, cosines.shape[0]), jnp.float32)
    _, stacked = lax.scan(advance, (zeroed, zeroed), jnp.arange(degrees, dtype=jnp.int32))
    return jnp.concatenate([stacked, stacked], axis=1)


def gelu_tanh(values):
    return jax.nn.gelu(values, approximate=True)


def xor_gather(x, axis_name, groups):
    bits = groups.bit_length() - 1
    cur = x[None]
    low = 0
    while low < bits:
        width = min(2, bits - low)
        parts = [cur]
        for k in range(1, 1 << width):
            mask = k << low
            parts.append(lax.ppermute(cur, axis_name, [(i, i ^ mask) for i in range(groups)]))
        cur = jnp.concatenate(parts, axis=0)
        low += width
    return cur


def xor_reduce_scatter(part, axis_name, groups, me, step=2, narrow=0):
    bits = groups.bit_length() - 1
    cur = part
    low = 0
    while low < bits:
        width = min(step, bits - low)
        fan = 1 << width
        view = cur.reshape((cur.shape[0] // fan, fan) + cur.shape[1:])
        mine = (me >> low) & (fan - 1)
        total = lax.dynamic_index_in_dim(view, mine, axis=1, keepdims=False)
        for k in range(1, fan):
            mask = k << low
            sent = lax.dynamic_index_in_dim(view, jnp.bitwise_xor(mine, k), axis=1, keepdims=False)
            if low < narrow:
                sent = sent.astype(jnp.bfloat16)
            moved = lax.ppermute(sent, axis_name, [(i, i ^ mask) for i in range(groups)])
            total = total + moved.astype(jnp.float32)
        cur = total
        low += width
    return cur[0]


def xor_exchange(values, table, axis_name, groups, me, lo, spec):
    parts = [values]
    for k in range(1, 1 << lo):
        parts.append(lax.ppermute(values, axis_name, [(i, i ^ k) for i in range(groups)]))
    stacked = jnp.stack(parts).astype(jnp.float32)
    cur = jnp.einsum(spec, table, stacked, precision=lax.Precision.HIGHEST)
    hi = groups.bit_length() - 1 - lo
    b = 0
    while b < hi:
        width = min(2, hi - b)
        fan = 1 << width
        view = cur.reshape((cur.shape[0] // fan, fan) + cur.shape[1:])
        total = view[:, 0]
        for k in range(1, fan):
            mask = k << (lo + b)
            total = total + lax.ppermute(view[:, k], axis_name, [(i, i ^ mask) for i in range(groups)])
        cur = total
        b += width
    return cur[0]


def complex_apply(coeffs, weights, orders):
    real_in, imag_in = (coeffs[:, :orders], coeffs[:, orders:])
    real_w, imag_w = (weights[:, 0], weights[:, 1])

    def complex_term(operand_a, operand_b):
        return jnp.einsum("smc,scd->smd", operand_a, operand_b, preferred_element_type=jnp.float32)

    real_out = complex_term(real_in, real_w) - complex_term(imag_in, imag_w)
    imag_out = complex_term(real_in, imag_w) + complex_term(imag_in, real_w)
    return jnp.concatenate([real_out, imag_out], axis=1)


def complex_adjoint(coeffs, cotangents, weights, orders):
    real_in, imag_in = (coeffs[:, :orders], coeffs[:, orders:])
    real_g, imag_g = (cotangents[:, :orders], cotangents[:, orders:])
    real_w, imag_w = (weights[:, 0], weights[:, 1])

    def outer_sum(operand_a, operand_b):
        return jnp.einsum("smc,smd->scd", operand_a, operand_b, preferred_element_type=jnp.float32)

    def back_term(operand_a, operand_b):
        return jnp.einsum("smd,scd->smc", operand_a, operand_b, preferred_element_type=jnp.float32)

    grad_real = outer_sum(real_in, real_g) + outer_sum(imag_in, imag_g)
    grad_imag = outer_sum(real_in, imag_g) - outer_sum(imag_in, real_g)
    back_real = back_term(real_g, real_w) + back_term(imag_g, imag_w)
    back_imag = back_term(imag_g, real_w) - back_term(real_g, imag_w)
    return (
        jnp.stack([grad_real, grad_imag], axis=1),
        jnp.concatenate([back_real, back_imag], axis=1),
    )


def local(activations, upstream, skip_weight, spectral_weight, slot_degree):
    groups = lax.axis_size("lat")
    me = lax.axis_index("lat")
    lat_rows = activations.shape[0]
    lon_total = activations.shape[1]
    lat_total = lat_rows * groups
    per_owner = spectral_weight.shape[0]
    degrees = per_owner * groups
    orders = ORDERS
    highest = lax.Precision.HIGHEST

    fourier = jnp.asarray(fourier_table(lon_total, orders))
    cosines, sines = colatitudes(lat_total)
    plm_np = legendre_table(cosines, sines, degrees, orders)
    quad_np = plm_np * (math.pi / lat_total * sines)[None, None, :]
    if degrees * lat_total <= 64 * 64:
        plm_all = jnp.asarray(plm_np.astype(np.float32))
        quad_all = jnp.asarray(quad_np.astype(np.float32))
    else:
        plm_all = legendre_scan(cosines, sines, degrees, orders)
        quad_all = plm_all * jnp.asarray((math.pi / lat_total * sines).astype(np.float32))[None, None, :]

    bits = groups.bit_length() - 1
    lo = min(2, bits)
    both = jnp.concatenate([quad_all, plm_all], axis=1).transpose(0, 2, 1)
    near = jnp.bitwise_xor(me, jnp.arange(1 << lo, dtype=jnp.int32))
    far = jnp.bitwise_xor(me >> lo, jnp.arange(groups >> lo, dtype=jnp.int32)) * (1 << lo) + (me & ((1 << lo) - 1))
    slot_r = jnp.arange(per_owner, dtype=jnp.int32)
    row_r = jnp.arange(lat_rows, dtype=jnp.int32)
    far_deg = jnp.take(slot_degree, far[:, None] * per_owner + slot_r[None, :])
    near_rows = near[:, None] * lat_rows + row_r[None, :]
    own_both = both[far_deg[:, :, None, None], near_rows[None, None, :, :]]
    near_deg = jnp.take(slot_degree, near[:, None] * per_owner + slot_r[None, :])
    far_rows = far[:, None] * lat_rows + row_r[None, :]
    rows_both = both[near_deg[None, :, :, None], far_rows[:, None, None, :]]
    nf = 2 * orders
    own_quad, own_plm = own_both[..., :nf], own_both[..., nf:]
    rows_plm, rows_quad = rows_both[..., nf:], rows_both[..., :nf]
    to_owners = "xskrf,krfc->xsfc"
    to_rows = "xksrf,ksfc->xrfc"

    def exchange(values, table, spec):
        return xor_exchange(values, table, "lat", groups, me, lo, spec)

    spectrum = jnp.einsum("jkc,kf->jfc", activations, fourier, preferred_element_type=jnp.float32)
    coeffs = exchange(spectrum, own_quad, to_owners).astype(jnp.bfloat16)
    filtered = complex_apply(coeffs, spectral_weight, orders).astype(jnp.bfloat16)
    grid_modes = exchange(filtered, rows_plm, to_rows).astype(jnp.bfloat16)

    spatial = jnp.einsum("jfc,kf->jkc", grid_modes, fourier, preferred_element_type=jnp.float32)
    skip_out = jnp.einsum("jkc,cd->jkd", activations, skip_weight, preferred_element_type=jnp.float32)
    _, pullback = jax.vjp(gelu_tanh, spatial + skip_out)
    slope_b = pullback(upstream.astype(jnp.float32))[0].astype(jnp.bfloat16)

    skip_terms = jnp.einsum("jkc,jkd->cd", activations, slope_b, preferred_element_type=jnp.float32)
    skip_blocks = skip_terms.reshape((groups, -1) + skip_terms.shape[1:])
    grad_skip = xor_reduce_scatter(skip_blocks, "lat", groups, me, 1, 2) * (1.0 / math.sqrt(lat_total * lon_total))
    through_skip = jnp.einsum("jkd,cd->jkc", slope_b, skip_weight, preferred_element_type=jnp.float32)

    mode_grads = jnp.einsum("jkc,kf->jfc", slope_b, fourier, preferred_element_type=jnp.float32)
    coeff_grads = exchange(mode_grads, own_plm, to_owners).astype(jnp.bfloat16)
    weight_grads, back_coeffs = complex_adjoint(coeffs, coeff_grads, spectral_weight, orders)
    row_grads = exchange(back_coeffs.astype(jnp.bfloat16), rows_quad, to_rows).astype(jnp.bfloat16)
    through_modes = jnp.einsum("jfc,kf->jkc", row_grads, fourier, preferred_element_type=jnp.float32)
    grad_activations = (upstream.astype(jnp.float32) + through_skip + through_modes).astype(jnp.bfloat16)
    return (grad_activations, weight_grads.astype(jnp.bfloat16), grad_skip)


def solution(mesh):
    in_specs = (
        P(("grp", "lat"), None, None),
        P(("grp", "lat"), None, None),
        P(),
        P("lat", None, None, None),
        P(),
    )
    out_specs = (
        P(("grp", "lat"), None, None),
        P(("grp", "lat"), None, None, None),
        P(("grp", "lat"), None),
    )
    return jax.shard_map(local, mesh=mesh, in_specs=in_specs, out_specs=out_specs, check_vma=False)
```

```python
import math

import jax
import jax.numpy as jnp
import ml_dtypes
import numpy as np
from jax import lax
from jax.sharding import PartitionSpec as P

ORDERS = 4


def fourier_table(lon_total, orders):
    lon_ids = np.arange(lon_total, dtype=np.int64)[:, None]
    order_ids = np.arange(orders, dtype=np.int64)[None, :]
    angles = (lon_ids * order_ids % lon_total).astype(np.float64) * (2.0 * math.pi / lon_total)
    amplitude = math.sqrt(2.0 / lon_total)
    table = np.concatenate([amplitude * np.cos(angles), -amplitude * np.sin(angles)], axis=1)
    return table.astype(ml_dtypes.bfloat16)


def colatitudes(lat_total):
    row_ids = np.arange(lat_total)
    mirror = np.minimum(row_ids, lat_total - 1 - row_ids)
    colatitude = (mirror.astype(np.float64) + 0.5) * (math.pi / lat_total)
    cosines = np.where(row_ids < lat_total // 2, np.cos(colatitude), -np.cos(colatitude))
    return cosines, np.sin(colatitude)


def legendre_table(cosines, sines, degrees, orders):
    rows = cosines.shape[0]
    table = np.zeros((degrees, orders, rows), np.float64)
    factor = math.sqrt(0.5)
    for m in range(orders):
        if m > 0:
            factor *= math.sqrt((2.0 * m + 1.0) / (2.0 * m))
        diagonal = factor * sines**m
        if m < degrees:
            table[m, m] = diagonal
        if m + 1 < degrees:
            table[m + 1, m] = math.sqrt(2.0 * m + 3.0) * cosines * diagonal
        for l in range(m + 2, degrees):
            a = math.sqrt((4.0 * l * l - 1.0) / (l * l - m * m))
            b = math.sqrt(((l - 1.0) ** 2 - m * m) / (4.0 * (l - 1.0) ** 2 - 1.0))
            table[l, m] = a * (cosines * table[l - 1, m] - b * table[l - 2, m])
    return np.concatenate([table, table], axis=1)


def legendre_scan(cosines_np, sines_np, degrees, orders):
    cosines = jnp.asarray(cosines_np.astype(np.float32))
    sines = jnp.asarray(sines_np.astype(np.float32))
    order_col = jnp.arange(orders, dtype=jnp.float32)[:, None]
    factors = [math.sqrt(0.5)]
    for order_num in range(1, orders):
        factors.append(factors[-1] * math.sqrt((2.0 * order_num + 1.0) / (2.0 * order_num)))
    diagonal_start = jnp.array(factors, dtype=jnp.float32)[:, None] * jnp.power(sines[None, :], order_col)
    next_start = jnp.sqrt(2.0 * order_col + 3.0) * cosines[None, :] * diagonal_start

    def advance(state_pair, degree):
        previous, earlier = state_pair
        deg_value = degree.astype(jnp.float32)
        deg_below = deg_value - 1.0
        ratio_up = jnp.sqrt(
            jnp.maximum(4.0 * deg_value * deg_value - 1.0, 1.0)
            / jnp.maximum(deg_value * deg_value - order_col * order_col, 1.0)
        )
        ratio_down = jnp.sqrt(
            jnp.maximum(deg_below * deg_below - order_col * order_col, 0.0)
            / jnp.maximum(4.0 * deg_below * deg_below - 1.0, 1.0)
        )
        recurred = ratio_up * (cosines[None, :] * previous - ratio_down * earlier)
        current = jnp.where(
            deg_value == order_col,
            diagonal_start,
            jnp.where(
                deg_value == order_col + 1.0,
                next_start,
                jnp.where(deg_value > order_col + 1.0, recurred, 0.0),
            ),
        )
        return ((current, previous), current)

    zeroed = jnp.zeros((orders, cosines.shape[0]), jnp.float32)
    _, stacked = lax.scan(advance, (zeroed, zeroed), jnp.arange(degrees, dtype=jnp.int32))
    return jnp.concatenate([stacked, stacked], axis=1)


def gelu_tanh(values):
    return jax.nn.gelu(values, approximate=True)


def xor_gather(x, axis_name, groups):
    bits = groups.bit_length() - 1
    cur = x[None]
    low = 0
    while low < bits:
        width = min(2, bits - low)
        parts = [cur]
        for k in range(1, 1 << width):
            mask = k << low
            parts.append(lax.ppermute(cur, axis_name, [(i, i ^ mask) for i in range(groups)]))
        cur = jnp.concatenate(parts, axis=0)
        low += width
    return cur


def xor_reduce_scatter(part, axis_name, groups, me, step=2):
    bits = groups.bit_length() - 1
    cur = part
    low = 0
    while low < bits:
        width = min(step, bits - low)
        fan = 1 << width
        view = cur.reshape((cur.shape[0] // fan, fan) + cur.shape[1:])
        mine = (me >> low) & (fan - 1)
        total = lax.dynamic_index_in_dim(view, mine, axis=1, keepdims=False)
        for k in range(1, fan):
            mask = k << low
            sent = lax.dynamic_index_in_dim(view, jnp.bitwise_xor(mine, k), axis=1, keepdims=False)
            total = total + lax.ppermute(sent, axis_name, [(i, i ^ mask) for i in range(groups)])
        cur = total
        low += width
    return cur[0]


def halve_round(cur, axis_name, groups, me, low):
    view = cur.reshape((cur.shape[0] // 2, 2) + cur.shape[1:])
    bit = (me >> low) & 1
    total = lax.dynamic_index_in_dim(view, bit, axis=1, keepdims=False)
    sent = lax.dynamic_index_in_dim(view, 1 - bit, axis=1, keepdims=False)
    mask = 1 << low
    return total + lax.ppermute(sent, axis_name, [(i, i ^ mask) for i in range(groups)])


def xor_exchange(values, table, axis_name, groups, me, lo, spec, side=None):
    parts = [values]
    for k in range(1, 1 << lo):
        parts.append(lax.ppermute(values, axis_name, [(i, i ^ k) for i in range(groups)]))
    stacked = jnp.stack(parts).astype(jnp.float32)
    cur = jnp.einsum(spec, table, stacked, precision=lax.Precision.HIGHEST)
    hi = groups.bit_length() - 1 - lo
    b = 0
    while b < hi:
        if side is not None and side[1] < side[2]:
            blocks, low, bits = side
            cur, blocks = lax.optimization_barrier((cur, blocks))
            side = (halve_round(blocks, axis_name, groups, me, low), low + 1, bits)
        width = min(2, hi - b)
        fan = 1 << width
        view = cur.reshape((cur.shape[0] // fan, fan) + cur.shape[1:])
        total = view[:, 0]
        for k in range(1, fan):
            mask = k << (lo + b)
            total = total + lax.ppermute(view[:, k], axis_name, [(i, i ^ mask) for i in range(groups)])
        cur = total
        b += width
    return cur[0], side


def complex_apply(coeffs, weights, orders):
    real_in, imag_in = (coeffs[:, :orders], coeffs[:, orders:])
    real_w, imag_w = (weights[:, 0], weights[:, 1])

    def complex_term(operand_a, operand_b):
        return jnp.einsum("smc,scd->smd", operand_a, operand_b, preferred_element_type=jnp.float32)

    real_out = complex_term(real_in, real_w) - complex_term(imag_in, imag_w)
    imag_out = complex_term(real_in, imag_w) + complex_term(imag_in, real_w)
    return jnp.concatenate([real_out, imag_out], axis=1)


def complex_adjoint(coeffs, cotangents, weights, orders):
    real_in, imag_in = (coeffs[:, :orders], coeffs[:, orders:])
    real_g, imag_g = (cotangents[:, :orders], cotangents[:, orders:])
    real_w, imag_w = (weights[:, 0], weights[:, 1])

    def outer_sum(operand_a, operand_b):
        return jnp.einsum("smc,smd->scd", operand_a, operand_b, preferred_element_type=jnp.float32)

    def back_term(operand_a, operand_b):
        return jnp.einsum("smd,scd->smc", operand_a, operand_b, preferred_element_type=jnp.float32)

    grad_real = outer_sum(real_in, real_g) + outer_sum(imag_in, imag_g)
    grad_imag = outer_sum(real_in, imag_g) - outer_sum(imag_in, real_g)
    back_real = back_term(real_g, real_w) + back_term(imag_g, imag_w)
    back_imag = back_term(imag_g, real_w) - back_term(real_g, imag_w)
    return (
        jnp.stack([grad_real, grad_imag], axis=1),
        jnp.concatenate([back_real, back_imag], axis=1),
    )


def local(activations, upstream, skip_weight, spectral_weight, slot_degree):
    groups = lax.axis_size("lat")
    me = lax.axis_index("lat")
    lat_rows = activations.shape[0]
    lon_total = activations.shape[1]
    lat_total = lat_rows * groups
    per_owner = spectral_weight.shape[0]
    degrees = per_owner * groups
    orders = ORDERS
    highest = lax.Precision.HIGHEST

    fourier = jnp.asarray(fourier_table(lon_total, orders))
    cosines, sines = colatitudes(lat_total)
    plm_np = legendre_table(cosines, sines, degrees, orders)
    quad_np = plm_np * (math.pi / lat_total * sines)[None, None, :]
    if degrees * lat_total <= 64 * 64:
        plm_all = jnp.asarray(plm_np.astype(np.float32))
        quad_all = jnp.asarray(quad_np.astype(np.float32))
    else:
        plm_all = legendre_scan(cosines, sines, degrees, orders)
        quad_all = plm_all * jnp.asarray((math.pi / lat_total * sines).astype(np.float32))[None, None, :]

    bits = groups.bit_length() - 1
    lo = min(2, bits)
    both = jnp.concatenate([quad_all, plm_all], axis=1).transpose(0, 2, 1)
    near = jnp.bitwise_xor(me, jnp.arange(1 << lo, dtype=jnp.int32))
    far = jnp.bitwise_xor(me >> lo, jnp.arange(groups >> lo, dtype=jnp.int32)) * (1 << lo) + (me & ((1 << lo) - 1))
    slot_r = jnp.arange(per_owner, dtype=jnp.int32)
    row_r = jnp.arange(lat_rows, dtype=jnp.int32)
    far_deg = jnp.take(slot_degree, far[:, None] * per_owner + slot_r[None, :])
    near_rows = near[:, None] * lat_rows + row_r[None, :]
    own_both = both[far_deg[:, :, None, None], near_rows[None, None, :, :]]
    near_deg = jnp.take(slot_degree, near[:, None] * per_owner + slot_r[None, :])
    far_rows = far[:, None] * lat_rows + row_r[None, :]
    rows_both = both[near_deg[None, :, :, None], far_rows[:, None, None, :]]
    nf = 2 * orders
    own_quad, own_plm = own_both[..., :nf], own_both[..., nf:]
    rows_plm, rows_quad = rows_both[..., nf:], rows_both[..., :nf]
    to_owners = "xskrf,krfc->xsfc"
    to_rows = "xksrf,ksfc->xrfc"

    def exchange(values, table, spec):
        return xor_exchange(values, table, "lat", groups, me, lo, spec)[0]

    spectrum = jnp.einsum("jkc,kf->jfc", activations, fourier, preferred_element_type=jnp.float32)
    coeffs = exchange(spectrum, own_quad, to_owners).astype(jnp.bfloat16)
    filtered = complex_apply(coeffs, spectral_weight, orders).astype(jnp.bfloat16)
    grid_modes = exchange(filtered, rows_plm, to_rows).astype(jnp.bfloat16)

    spatial = jnp.einsum("jfc,kf->jkc", grid_modes, fourier, preferred_element_type=jnp.float32)
    skip_out = jnp.einsum("jkc,cd->jkd", activations, skip_weight, preferred_element_type=jnp.float32)
    _, pullback = jax.vjp(gelu_tanh, spatial + skip_out)
    slope_b = pullback(upstream.astype(jnp.float32))[0].astype(jnp.bfloat16)

    skip_terms = jnp.einsum("jkc,jkd->cd", activations, slope_b, preferred_element_type=jnp.float32)
    skip_blocks = skip_terms.reshape((groups, -1) + skip_terms.shape[1:])
    skip_side = (halve_round(skip_blocks, "lat", groups, me, 0), 1, bits) if bits > 0 else (skip_blocks, 0, 0)
    through_skip = jnp.einsum("jkd,cd->jkc", slope_b, skip_weight, preferred_element_type=jnp.float32)

    mode_grads = jnp.einsum("jkc,kf->jfc", slope_b, fourier, preferred_element_type=jnp.float32)
    coeff_grads = exchange(mode_grads, own_plm, to_owners).astype(jnp.bfloat16)
    weight_grads, back_coeffs = complex_adjoint(coeffs, coeff_grads, spectral_weight, orders)
    back_b = back_coeffs.astype(jnp.bfloat16)
    if skip_side[1] < skip_side[2]:
        back_b, held = lax.optimization_barrier((back_b, skip_side[0]))
        skip_side = (halve_round(held, "lat", groups, me, skip_side[1]), skip_side[1] + 1, bits)
    row_sums, skip_side = xor_exchange(back_b, rows_quad, "lat", groups, me, lo, to_rows, skip_side)
    row_grads = row_sums.astype(jnp.bfloat16)
    skip_sum, low = skip_side[0], skip_side[1]
    while low < bits:
        skip_sum = halve_round(skip_sum, "lat", groups, me, low)
        low += 1
    grad_skip = skip_sum[0] * (1.0 / math.sqrt(lat_total * lon_total))
    through_modes = jnp.einsum("jfc,kf->jkc", row_grads, fourier, preferred_element_type=jnp.float32)
    grad_activations = (upstream.astype(jnp.float32) + through_skip + through_modes).astype(jnp.bfloat16)
    return (grad_activations, weight_grads.astype(jnp.bfloat16), grad_skip)


def solution(mesh):
    in_specs = (
        P(("grp", "lat"), None, None),
        P(("grp", "lat"), None, None),
        P(),
        P("lat", None, None, None),
        P(),
    )
    out_specs = (
        P(("grp", "lat"), None, None),
        P(("grp", "lat"), None, None, None),
        P(("grp", "lat"), None),
    )
    return jax.shard_map(local, mesh=mesh, in_specs=in_specs, out_specs=out_specs, check_vma=False)
```

```python
import math

import jax
import jax.numpy as jnp
import ml_dtypes
import numpy as np
from jax import lax
from jax.sharding import PartitionSpec as P

ORDERS = 4


def fourier_table(lon_total, orders):
    lon_ids = np.arange(lon_total, dtype=np.int64)[:, None]
    order_ids = np.arange(orders, dtype=np.int64)[None, :]
    angles = (lon_ids * order_ids % lon_total).astype(np.float64) * (2.0 * math.pi / lon_total)
    amplitude = math.sqrt(2.0 / lon_total)
    table = np.concatenate([amplitude * np.cos(angles), -amplitude * np.sin(angles)], axis=1)
    return table.astype(ml_dtypes.bfloat16)


def colatitudes(lat_total):
    row_ids = np.arange(lat_total)
    mirror = np.minimum(row_ids, lat_total - 1 - row_ids)
    colatitude = (mirror.astype(np.float64) + 0.5) * (math.pi / lat_total)
    cosines = np.where(row_ids < lat_total // 2, np.cos(colatitude), -np.cos(colatitude))
    return cosines, np.sin(colatitude)


def legendre_table(cosines, sines, degrees, orders):
    rows = cosines.shape[0]
    table = np.zeros((degrees, orders, rows), np.float64)
    factor = math.sqrt(0.5)
    for m in range(orders):
        if m > 0:
            factor *= math.sqrt((2.0 * m + 1.0) / (2.0 * m))
        diagonal = factor * sines**m
        if m < degrees:
            table[m, m] = diagonal
        if m + 1 < degrees:
            table[m + 1, m] = math.sqrt(2.0 * m + 3.0) * cosines * diagonal
        for l in range(m + 2, degrees):
            a = math.sqrt((4.0 * l * l - 1.0) / (l * l - m * m))
            b = math.sqrt(((l - 1.0) ** 2 - m * m) / (4.0 * (l - 1.0) ** 2 - 1.0))
            table[l, m] = a * (cosines * table[l - 1, m] - b * table[l - 2, m])
    return np.concatenate([table, table], axis=1)


def legendre_scan(cosines_np, sines_np, degrees, orders):
    cosines = jnp.asarray(cosines_np.astype(np.float32))
    sines = jnp.asarray(sines_np.astype(np.float32))
    order_col = jnp.arange(orders, dtype=jnp.float32)[:, None]
    factors = [math.sqrt(0.5)]
    for order_num in range(1, orders):
        factors.append(factors[-1] * math.sqrt((2.0 * order_num + 1.0) / (2.0 * order_num)))
    diagonal_start = jnp.array(factors, dtype=jnp.float32)[:, None] * jnp.power(sines[None, :], order_col)
    next_start = jnp.sqrt(2.0 * order_col + 3.0) * cosines[None, :] * diagonal_start

    def advance(state_pair, degree):
        previous, earlier = state_pair
        deg_value = degree.astype(jnp.float32)
        deg_below = deg_value - 1.0
        ratio_up = jnp.sqrt(
            jnp.maximum(4.0 * deg_value * deg_value - 1.0, 1.0)
            / jnp.maximum(deg_value * deg_value - order_col * order_col, 1.0)
        )
        ratio_down = jnp.sqrt(
            jnp.maximum(deg_below * deg_below - order_col * order_col, 0.0)
            / jnp.maximum(4.0 * deg_below * deg_below - 1.0, 1.0)
        )
        recurred = ratio_up * (cosines[None, :] * previous - ratio_down * earlier)
        current = jnp.where(
            deg_value == order_col,
            diagonal_start,
            jnp.where(
                deg_value == order_col + 1.0,
                next_start,
                jnp.where(deg_value > order_col + 1.0, recurred, 0.0),
            ),
        )
        return ((current, previous), current)

    zeroed = jnp.zeros((orders, cosines.shape[0]), jnp.float32)
    _, stacked = lax.scan(advance, (zeroed, zeroed), jnp.arange(degrees, dtype=jnp.int32))
    return jnp.concatenate([stacked, stacked], axis=1)


def gelu_tanh(values):
    return jax.nn.gelu(values, approximate=True)


def xor_gather(x, axis_name, groups):
    bits = groups.bit_length() - 1
    cur = x[None]
    low = 0
    while low < bits:
        width = min(2, bits - low)
        parts = [cur]
        for k in range(1, 1 << width):
            mask = k << low
            parts.append(lax.ppermute(cur, axis_name, [(i, i ^ mask) for i in range(groups)]))
        cur = jnp.concatenate(parts, axis=0)
        low += width
    return cur


def xor_reduce_scatter(part, axis_name, groups, me, step=2):
    bits = groups.bit_length() - 1
    cur = part
    low = 0
    while low < bits:
        width = min(step if low < 2 else 2, bits - low)
        fan = 1 << width
        view = cur.reshape((cur.shape[0] // fan, fan) + cur.shape[1:])
        mine = (me >> low) & (fan - 1)
        total = lax.dynamic_index_in_dim(view, mine, axis=1, keepdims=False)
        for k in range(1, fan):
            mask = k << low
            sent = lax.dynamic_index_in_dim(view, jnp.bitwise_xor(mine, k), axis=1, keepdims=False)
            total = total + lax.ppermute(sent, axis_name, [(i, i ^ mask) for i in range(groups)])
        cur = total
        low += width
    return cur[0]


def xor_exchange(values, table, axis_name, groups, me, lo, spec):
    parts = [values]
    for k in range(1, 1 << lo):
        parts.append(lax.ppermute(values, axis_name, [(i, i ^ k) for i in range(groups)]))
    stacked = jnp.stack(parts).astype(jnp.float32)
    cur = jnp.einsum(spec, table, stacked, precision=lax.Precision.HIGHEST)
    hi = groups.bit_length() - 1 - lo
    b = 0
    while b < hi:
        width = min(2, hi - b)
        fan = 1 << width
        view = cur.reshape((cur.shape[0] // fan, fan) + cur.shape[1:])
        total = view[:, 0]
        for k in range(1, fan):
            mask = k << (lo + b)
            total = total + lax.ppermute(view[:, k], axis_name, [(i, i ^ mask) for i in range(groups)])
        cur = total
        b += width
    return cur[0]


def complex_apply(coeffs, weights, orders):
    real_in, imag_in = (coeffs[:, :orders], coeffs[:, orders:])
    real_w, imag_w = (weights[:, 0], weights[:, 1])

    def complex_term(operand_a, operand_b):
        return jnp.einsum("smc,scd->smd", operand_a, operand_b, preferred_element_type=jnp.float32)

    real_out = complex_term(real_in, real_w) - complex_term(imag_in, imag_w)
    imag_out = complex_term(real_in, imag_w) + complex_term(imag_in, real_w)
    return jnp.concatenate([real_out, imag_out], axis=1)


def complex_adjoint(coeffs, cotangents, weights, orders):
    real_in, imag_in = (coeffs[:, :orders], coeffs[:, orders:])
    real_g, imag_g = (cotangents[:, :orders], cotangents[:, orders:])
    real_w, imag_w = (weights[:, 0], weights[:, 1])

    def outer_sum(operand_a, operand_b):
        return jnp.einsum("smc,smd->scd", operand_a, operand_b, preferred_element_type=jnp.float32)

    def back_term(operand_a, operand_b):
        return jnp.einsum("smd,scd->smc", operand_a, operand_b, preferred_element_type=jnp.float32)

    grad_real = outer_sum(real_in, real_g) + outer_sum(imag_in, imag_g)
    grad_imag = outer_sum(real_in, imag_g) - outer_sum(imag_in, real_g)
    back_real = back_term(real_g, real_w) + back_term(imag_g, imag_w)
    back_imag = back_term(imag_g, real_w) - back_term(real_g, imag_w)
    return (
        jnp.stack([grad_real, grad_imag], axis=1),
        jnp.concatenate([back_real, back_imag], axis=1),
    )


def local(activations, upstream, skip_weight, spectral_weight, slot_degree):
    groups = lax.axis_size("lat")
    me = lax.axis_index("lat")
    lat_rows = activations.shape[0]
    lon_total = activations.shape[1]
    lat_total = lat_rows * groups
    per_owner = spectral_weight.shape[0]
    degrees = per_owner * groups
    orders = ORDERS
    highest = lax.Precision.HIGHEST

    fourier = jnp.asarray(fourier_table(lon_total, orders))
    cosines, sines = colatitudes(lat_total)
    plm_np = legendre_table(cosines, sines, degrees, orders)
    quad_np = plm_np * (math.pi / lat_total * sines)[None, None, :]
    if degrees * lat_total <= 64 * 64:
        plm_all = jnp.asarray(plm_np.astype(np.float32))
        quad_all = jnp.asarray(quad_np.astype(np.float32))
    else:
        plm_all = legendre_scan(cosines, sines, degrees, orders)
        quad_all = plm_all * jnp.asarray((math.pi / lat_total * sines).astype(np.float32))[None, None, :]

    bits = groups.bit_length() - 1
    lo = min(2, bits)
    both = jnp.concatenate([quad_all, plm_all], axis=1).transpose(0, 2, 1)
    near = jnp.bitwise_xor(me, jnp.arange(1 << lo, dtype=jnp.int32))
    far = jnp.bitwise_xor(me >> lo, jnp.arange(groups >> lo, dtype=jnp.int32)) * (1 << lo) + (me & ((1 << lo) - 1))
    slot_r = jnp.arange(per_owner, dtype=jnp.int32)
    row_r = jnp.arange(lat_rows, dtype=jnp.int32)
    far_deg = jnp.take(slot_degree, far[:, None] * per_owner + slot_r[None, :])
    near_rows = near[:, None] * lat_rows + row_r[None, :]
    own_both = both[far_deg[:, :, None, None], near_rows[None, None, :, :]]
    near_deg = jnp.take(slot_degree, near[:, None] * per_owner + slot_r[None, :])
    far_rows = far[:, None] * lat_rows + row_r[None, :]
    rows_both = both[near_deg[None, :, :, None], far_rows[:, None, None, :]]
    nf = 2 * orders
    own_quad, own_plm = own_both[..., :nf], own_both[..., nf:]
    rows_plm, rows_quad = rows_both[..., nf:], rows_both[..., :nf]
    to_owners = "xskrf,krfc->xsfc"
    to_rows = "xksrf,ksfc->xrfc"

    def exchange(values, table, spec):
        return xor_exchange(values, table, "lat", groups, me, lo, spec)

    spectrum = jnp.einsum("jkc,kf->jfc", activations, fourier, preferred_element_type=jnp.float32)
    coeffs = exchange(spectrum, own_quad, to_owners).astype(jnp.bfloat16)
    filtered = complex_apply(coeffs, spectral_weight, orders).astype(jnp.bfloat16)
    grid_modes = exchange(filtered, rows_plm, to_rows).astype(jnp.bfloat16)

    spatial = jnp.einsum("jfc,kf->jkc", grid_modes, fourier, preferred_element_type=jnp.float32)
    skip_out = jnp.einsum("jkc,cd->jkd", activations, skip_weight, preferred_element_type=jnp.float32)
    _, pullback = jax.vjp(gelu_tanh, spatial + skip_out)
    slope_b = pullback(upstream.astype(jnp.float32))[0].astype(jnp.bfloat16)

    skip_terms = jnp.einsum("jkc,jkd->cd", activations, slope_b, preferred_element_type=jnp.float32)
    skip_blocks = skip_terms.reshape((groups, -1) + skip_terms.shape[1:])
    grad_skip = xor_reduce_scatter(skip_blocks, "lat", groups, me, 1) * (1.0 / math.sqrt(lat_total * lon_total))
    through_skip = jnp.einsum("jkd,cd->jkc", slope_b, skip_weight, preferred_element_type=jnp.float32)

    mode_grads = jnp.einsum("jkc,kf->jfc", slope_b, fourier, preferred_element_type=jnp.float32)
    coeff_grads = exchange(mode_grads, own_plm, to_owners).astype(jnp.bfloat16)
    weight_grads, back_coeffs = complex_adjoint(coeffs, coeff_grads, spectral_weight, orders)
    row_grads = exchange(back_coeffs.astype(jnp.bfloat16), rows_quad, to_rows).astype(jnp.bfloat16)
    through_modes = jnp.einsum("jfc,kf->jkc", row_grads, fourier, preferred_element_type=jnp.float32)
    grad_activations = (upstream.astype(jnp.float32) + through_skip + through_modes).astype(jnp.bfloat16)
    return (grad_activations, weight_grads.astype(jnp.bfloat16), grad_skip)


def solution(mesh):
    in_specs = (
        P(("grp", "lat"), None, None),
        P(("grp", "lat"), None, None),
        P(),
        P("lat", None, None, None),
        P(),
    )
    out_specs = (
        P(("grp", "lat"), None, None),
        P(("grp", "lat"), None, None, None),
        P(("grp", "lat"), None),
    )
    return jax.shard_map(local, mesh=mesh, in_specs=in_specs, out_specs=out_specs, check_vma=False)
```

```python
import math

import jax
import jax.numpy as jnp
import ml_dtypes
import numpy as np
from jax import lax
from jax.sharding import PartitionSpec as P

ORDERS = 4


def fourier_table(lon_total, orders):
    lon_ids = np.arange(lon_total, dtype=np.int64)[:, None]
    order_ids = np.arange(orders, dtype=np.int64)[None, :]
    angles = (lon_ids * order_ids % lon_total).astype(np.float64) * (2.0 * math.pi / lon_total)
    amplitude = math.sqrt(2.0 / lon_total)
    table = np.concatenate([amplitude * np.cos(angles), -amplitude * np.sin(angles)], axis=1)
    return table.astype(ml_dtypes.bfloat16)


def colatitudes(lat_total):
    row_ids = np.arange(lat_total)
    mirror = np.minimum(row_ids, lat_total - 1 - row_ids)
    colatitude = (mirror.astype(np.float64) + 0.5) * (math.pi / lat_total)
    cosines = np.where(row_ids < lat_total // 2, np.cos(colatitude), -np.cos(colatitude))
    return cosines, np.sin(colatitude)


def legendre_table(cosines, sines, degrees, orders):
    rows = cosines.shape[0]
    table = np.zeros((degrees, orders, rows), np.float64)
    factor = math.sqrt(0.5)
    for m in range(orders):
        if m > 0:
            factor *= math.sqrt((2.0 * m + 1.0) / (2.0 * m))
        diagonal = factor * sines**m
        if m < degrees:
            table[m, m] = diagonal
        if m + 1 < degrees:
            table[m + 1, m] = math.sqrt(2.0 * m + 3.0) * cosines * diagonal
        for l in range(m + 2, degrees):
            a = math.sqrt((4.0 * l * l - 1.0) / (l * l - m * m))
            b = math.sqrt(((l - 1.0) ** 2 - m * m) / (4.0 * (l - 1.0) ** 2 - 1.0))
            table[l, m] = a * (cosines * table[l - 1, m] - b * table[l - 2, m])
    return np.concatenate([table, table], axis=1)


def legendre_scan(cosines_np, sines_np, degrees, orders):
    cosines = jnp.asarray(cosines_np.astype(np.float32))
    sines = jnp.asarray(sines_np.astype(np.float32))
    order_col = jnp.arange(orders, dtype=jnp.float32)[:, None]
    factors = [math.sqrt(0.5)]
    for order_num in range(1, orders):
        factors.append(factors[-1] * math.sqrt((2.0 * order_num + 1.0) / (2.0 * order_num)))
    diagonal_start = jnp.array(factors, dtype=jnp.float32)[:, None] * jnp.power(sines[None, :], order_col)
    next_start = jnp.sqrt(2.0 * order_col + 3.0) * cosines[None, :] * diagonal_start

    def advance(state_pair, degree):
        previous, earlier = state_pair
        deg_value = degree.astype(jnp.float32)
        deg_below = deg_value - 1.0
        ratio_up = jnp.sqrt(
            jnp.maximum(4.0 * deg_value * deg_value - 1.0, 1.0)
            / jnp.maximum(deg_value * deg_value - order_col * order_col, 1.0)
        )
        ratio_down = jnp.sqrt(
            jnp.maximum(deg_below * deg_below - order_col * order_col, 0.0)
            / jnp.maximum(4.0 * deg_below * deg_below - 1.0, 1.0)
        )
        recurred = ratio_up * (cosines[None, :] * previous - ratio_down * earlier)
        current = jnp.where(
            deg_value == order_col,
            diagonal_start,
            jnp.where(
                deg_value == order_col + 1.0,
                next_start,
                jnp.where(deg_value > order_col + 1.0, recurred, 0.0),
            ),
        )
        return ((current, previous), current)

    zeroed = jnp.zeros((orders, cosines.shape[0]), jnp.float32)
    _, stacked = lax.scan(advance, (zeroed, zeroed), jnp.arange(degrees, dtype=jnp.int32))
    return jnp.concatenate([stacked, stacked], axis=1)


def gelu_tanh(values):
    return jax.nn.gelu(values, approximate=True)


def xor_gather(x, axis_name, groups):
    bits = groups.bit_length() - 1
    cur = x[None]
    low = 0
    while low < bits:
        width = min(2, bits - low)
        parts = [cur]
        for k in range(1, 1 << width):
            mask = k << low
            parts.append(lax.ppermute(cur, axis_name, [(i, i ^ mask) for i in range(groups)]))
        cur = jnp.concatenate(parts, axis=0)
        low += width
    return cur


def xor_reduce_scatter(part, axis_name, groups, me, step=2):
    bits = groups.bit_length() - 1
    cur = part
    low = 0
    while low < bits:
        width = min(step if low < 2 else 2, bits - low)
        fan = 1 << width
        view = cur.reshape((cur.shape[0] // fan, fan) + cur.shape[1:])
        mine = (me >> low) & (fan - 1)
        total = lax.dynamic_index_in_dim(view, mine, axis=1, keepdims=False)
        for k in range(1, fan):
            mask = k << low
            sent = lax.dynamic_index_in_dim(view, jnp.bitwise_xor(mine, k), axis=1, keepdims=False)
            total = total + lax.ppermute(sent, axis_name, [(i, i ^ mask) for i in range(groups)])
        cur = total
        low += width
    return cur[0]


def xor_exchange(values, table, axis_name, groups, me, lo, spec):
    parts = [values]
    for k in range(1, 1 << lo):
        parts.append(lax.ppermute(values, axis_name, [(i, i ^ k) for i in range(groups)]))
    stacked = jnp.stack(parts).astype(jnp.float32)
    cur = jnp.einsum(spec, table, stacked, precision=lax.Precision.HIGHEST)
    hi = groups.bit_length() - 1 - lo
    b = 0
    while b < hi:
        width = min(2, hi - b)
        fan = 1 << width
        view = cur.reshape((cur.shape[0] // fan, fan) + cur.shape[1:])
        total = view[:, 0]
        for k in range(1, fan):
            mask = k << (lo + b)
            total = total + lax.ppermute(view[:, k], axis_name, [(i, i ^ mask) for i in range(groups)])
        cur = total
        b += width
    return cur[0]


def complex_apply(coeffs, weights, orders):
    real_in, imag_in = (coeffs[:, :orders], coeffs[:, orders:])
    real_w, imag_w = (weights[:, 0], weights[:, 1])

    def complex_term(operand_a, operand_b):
        return jnp.einsum("smc,scd->smd", operand_a, operand_b, preferred_element_type=jnp.float32)

    real_out = complex_term(real_in, real_w) - complex_term(imag_in, imag_w)
    imag_out = complex_term(real_in, imag_w) + complex_term(imag_in, real_w)
    return jnp.concatenate([real_out, imag_out], axis=1)


def complex_adjoint(coeffs, cotangents, weights, orders):
    real_in, imag_in = (coeffs[:, :orders], coeffs[:, orders:])
    real_g, imag_g = (cotangents[:, :orders], cotangents[:, orders:])
    real_w, imag_w = (weights[:, 0], weights[:, 1])

    def outer_sum(operand_a, operand_b):
        return jnp.einsum("smc,smd->scd", operand_a, operand_b, preferred_element_type=jnp.float32)

    def back_term(operand_a, operand_b):
        return jnp.einsum("smd,scd->smc", operand_a, operand_b, preferred_element_type=jnp.float32)

    grad_real = outer_sum(real_in, real_g) + outer_sum(imag_in, imag_g)
    grad_imag = outer_sum(real_in, imag_g) - outer_sum(imag_in, real_g)
    back_real = back_term(real_g, real_w) + back_term(imag_g, imag_w)
    back_imag = back_term(imag_g, real_w) - back_term(real_g, imag_w)
    return (
        jnp.stack([grad_real, grad_imag], axis=1),
        jnp.concatenate([back_real, back_imag], axis=1),
    )


def local(activations, upstream, skip_weight, spectral_weight, slot_degree):
    groups = lax.axis_size("lat")
    me = lax.axis_index("lat")
    lat_rows = activations.shape[0]
    lon_total = activations.shape[1]
    lat_total = lat_rows * groups
    per_owner = spectral_weight.shape[0]
    degrees = per_owner * groups
    orders = ORDERS
    highest = lax.Precision.HIGHEST

    fourier = jnp.asarray(fourier_table(lon_total, orders))
    cosines, sines = colatitudes(lat_total)
    plm_np = legendre_table(cosines, sines, degrees, orders)
    quad_np = plm_np * (math.pi / lat_total * sines)[None, None, :]
    if degrees * lat_total <= 64 * 64:
        plm_all = jnp.asarray(plm_np.astype(np.float32))
        quad_all = jnp.asarray(quad_np.astype(np.float32))
    else:
        plm_all = legendre_scan(cosines, sines, degrees, orders)
        quad_all = plm_all * jnp.asarray((math.pi / lat_total * sines).astype(np.float32))[None, None, :]

    bits = groups.bit_length() - 1
    lo = min(2, bits)
    both = jnp.concatenate([quad_all, plm_all], axis=1).transpose(0, 2, 1)
    near = jnp.bitwise_xor(me, jnp.arange(1 << lo, dtype=jnp.int32))
    far = jnp.bitwise_xor(me >> lo, jnp.arange(groups >> lo, dtype=jnp.int32)) * (1 << lo) + (me & ((1 << lo) - 1))
    slot_r = jnp.arange(per_owner, dtype=jnp.int32)
    row_r = jnp.arange(lat_rows, dtype=jnp.int32)
    far_deg = jnp.take(slot_degree, far[:, None] * per_owner + slot_r[None, :])
    near_rows = near[:, None] * lat_rows + row_r[None, :]
    own_both = both[far_deg[:, :, None, None], near_rows[None, None, :, :]]
    near_deg = jnp.take(slot_degree, near[:, None] * per_owner + slot_r[None, :])
    far_rows = far[:, None] * lat_rows + row_r[None, :]
    rows_both = both[near_deg[None, :, :, None], far_rows[:, None, None, :]]
    nf = 2 * orders
    own_quad, own_plm = own_both[..., :nf], own_both[..., nf:]
    rows_plm, rows_quad = rows_both[..., nf:], rows_both[..., :nf]
    to_owners = "xskrf,krfc->xsfc"
    to_rows = "xksrf,ksfc->xrfc"

    def exchange(values, table, spec):
        return xor_exchange(values, table, "lat", groups, me, lo, spec)

    spectrum = jnp.einsum("jkc,kf->jfc", activations, fourier, preferred_element_type=jnp.float32)
    coeffs = exchange(spectrum, own_quad, to_owners).astype(jnp.bfloat16)
    filtered = complex_apply(coeffs, spectral_weight, orders).astype(jnp.bfloat16)
    grid_modes = exchange(filtered, rows_plm, to_rows).astype(jnp.bfloat16)

    widened = jnp.concatenate(
        [activations, jnp.broadcast_to(fourier[None], (lat_rows,) + fourier.shape)], axis=2
    )
    stacked_w = jnp.concatenate(
        [jnp.broadcast_to(skip_weight[None], (lat_rows,) + skip_weight.shape), grid_modes], axis=1
    )
    preact = jnp.einsum("jkc,jcd->jkd", widened, stacked_w, preferred_element_type=jnp.float32)
    _, pullback = jax.vjp(gelu_tanh, preact)
    slope_b = pullback(upstream.astype(jnp.float32))[0].astype(jnp.bfloat16)

    skip_terms = jnp.einsum("jkc,jkd->cd", activations, slope_b, preferred_element_type=jnp.float32)
    skip_blocks = skip_terms.reshape((groups, -1) + skip_terms.shape[1:])
    grad_skip = xor_reduce_scatter(skip_blocks, "lat", groups, me, 1) * (1.0 / math.sqrt(lat_total * lon_total))
    through_skip = jnp.einsum("jkd,cd->jkc", slope_b, skip_weight, preferred_element_type=jnp.float32)

    mode_grads = jnp.einsum("jkc,kf->jfc", slope_b, fourier, preferred_element_type=jnp.float32)
    coeff_grads = exchange(mode_grads, own_plm, to_owners).astype(jnp.bfloat16)
    weight_grads, back_coeffs = complex_adjoint(coeffs, coeff_grads, spectral_weight, orders)
    row_grads = exchange(back_coeffs.astype(jnp.bfloat16), rows_quad, to_rows).astype(jnp.bfloat16)
    through_modes = jnp.einsum("jfc,kf->jkc", row_grads, fourier, preferred_element_type=jnp.float32)
    grad_activations = (upstream.astype(jnp.float32) + through_skip + through_modes).astype(jnp.bfloat16)
    return (grad_activations, weight_grads.astype(jnp.bfloat16), grad_skip)


def solution(mesh):
    in_specs = (
        P(("grp", "lat"), None, None),
        P(("grp", "lat"), None, None),
        P(),
        P("lat", None, None, None),
        P(),
    )
    out_specs = (
        P(("grp", "lat"), None, None),
        P(("grp", "lat"), None, None, None),
        P(("grp", "lat"), None),
    )
    return jax.shard_map(local, mesh=mesh, in_specs=in_specs, out_specs=out_specs, check_vma=False)
```

```python
import math

import jax
import jax.numpy as jnp
import ml_dtypes
import numpy as np
from jax import lax
from jax.sharding import PartitionSpec as P

ORDERS = 4


def fourier_table(lon_total, orders):
    lon_ids = np.arange(lon_total, dtype=np.int64)[:, None]
    order_ids = np.arange(orders, dtype=np.int64)[None, :]
    angles = (lon_ids * order_ids % lon_total).astype(np.float64) * (2.0 * math.pi / lon_total)
    amplitude = math.sqrt(2.0 / lon_total)
    table = np.concatenate([amplitude * np.cos(angles), -amplitude * np.sin(angles)], axis=1)
    return table.astype(ml_dtypes.bfloat16)


def colatitudes(lat_total):
    row_ids = np.arange(lat_total)
    mirror = np.minimum(row_ids, lat_total - 1 - row_ids)
    colatitude = (mirror.astype(np.float64) + 0.5) * (math.pi / lat_total)
    cosines = np.where(row_ids < lat_total // 2, np.cos(colatitude), -np.cos(colatitude))
    return cosines, np.sin(colatitude)


def legendre_table(cosines, sines, degrees, orders):
    rows = cosines.shape[0]
    table = np.zeros((degrees, orders, rows), np.float64)
    factor = math.sqrt(0.5)
    for m in range(orders):
        if m > 0:
            factor *= math.sqrt((2.0 * m + 1.0) / (2.0 * m))
        diagonal = factor * sines**m
        if m < degrees:
            table[m, m] = diagonal
        if m + 1 < degrees:
            table[m + 1, m] = math.sqrt(2.0 * m + 3.0) * cosines * diagonal
        for l in range(m + 2, degrees):
            a = math.sqrt((4.0 * l * l - 1.0) / (l * l - m * m))
            b = math.sqrt(((l - 1.0) ** 2 - m * m) / (4.0 * (l - 1.0) ** 2 - 1.0))
            table[l, m] = a * (cosines * table[l - 1, m] - b * table[l - 2, m])
    return np.concatenate([table, table], axis=1)


def legendre_scan(cosines_np, sines_np, degrees, orders):
    cosines = jnp.asarray(cosines_np.astype(np.float32))
    sines = jnp.asarray(sines_np.astype(np.float32))
    order_col = jnp.arange(orders, dtype=jnp.float32)[:, None]
    factors = [math.sqrt(0.5)]
    for order_num in range(1, orders):
        factors.append(factors[-1] * math.sqrt((2.0 * order_num + 1.0) / (2.0 * order_num)))
    diagonal_start = jnp.array(factors, dtype=jnp.float32)[:, None] * jnp.power(sines[None, :], order_col)
    next_start = jnp.sqrt(2.0 * order_col + 3.0) * cosines[None, :] * diagonal_start

    def advance(state_pair, degree):
        previous, earlier = state_pair
        deg_value = degree.astype(jnp.float32)
        deg_below = deg_value - 1.0
        ratio_up = jnp.sqrt(
            jnp.maximum(4.0 * deg_value * deg_value - 1.0, 1.0)
            / jnp.maximum(deg_value * deg_value - order_col * order_col, 1.0)
        )
        ratio_down = jnp.sqrt(
            jnp.maximum(deg_below * deg_below - order_col * order_col, 0.0)
            / jnp.maximum(4.0 * deg_below * deg_below - 1.0, 1.0)
        )
        recurred = ratio_up * (cosines[None, :] * previous - ratio_down * earlier)
        current = jnp.where(
            deg_value == order_col,
            diagonal_start,
            jnp.where(
                deg_value == order_col + 1.0,
                next_start,
                jnp.where(deg_value > order_col + 1.0, recurred, 0.0),
            ),
        )
        return ((current, previous), current)

    zeroed = jnp.zeros((orders, cosines.shape[0]), jnp.float32)
    _, stacked = lax.scan(advance, (zeroed, zeroed), jnp.arange(degrees, dtype=jnp.int32))
    return jnp.concatenate([stacked, stacked], axis=1)


def gelu_tanh(values):
    return jax.nn.gelu(values, approximate=True)


def xor_gather(x, axis_name, groups):
    bits = groups.bit_length() - 1
    cur = x[None]
    low = 0
    while low < bits:
        width = min(2, bits - low)
        parts = [cur]
        for k in range(1, 1 << width):
            mask = k << low
            parts.append(lax.ppermute(cur, axis_name, [(i, i ^ mask) for i in range(groups)]))
        cur = jnp.concatenate(parts, axis=0)
        low += width
    return cur


def xor_reduce_scatter(part, axis_name, groups, me, step=2, narrow=0):
    bits = groups.bit_length() - 1
    cur = part
    low = 0
    while low < bits:
        width = min(step, bits - low)
        fan = 1 << width
        view = cur.reshape((cur.shape[0] // fan, fan) + cur.shape[1:])
        mine = (me >> low) & (fan - 1)
        total = lax.dynamic_index_in_dim(view, mine, axis=1, keepdims=False)
        for k in range(1, fan):
            mask = k << low
            sent = lax.dynamic_index_in_dim(view, jnp.bitwise_xor(mine, k), axis=1, keepdims=False)
            if low < narrow:
                sent = sent.astype(jnp.bfloat16)
            moved = lax.ppermute(sent, axis_name, [(i, i ^ mask) for i in range(groups)])
            total = total + moved.astype(jnp.float32)
        cur = total
        low += width
    return cur[0]


def xor_exchange(values, table, axis_name, groups, me, lo, spec):
    parts = [values]
    for k in range(1, 1 << lo):
        parts.append(lax.ppermute(values, axis_name, [(i, i ^ k) for i in range(groups)]))
    stacked = jnp.stack(parts).astype(jnp.float32)
    cur = jnp.einsum(spec, table, stacked, precision=lax.Precision.HIGHEST)
    hi = groups.bit_length() - 1 - lo
    b = 0
    while b < hi:
        width = min(2, hi - b)
        fan = 1 << width
        view = cur.reshape((cur.shape[0] // fan, fan) + cur.shape[1:])
        total = view[:, 0]
        for k in range(1, fan):
            mask = k << (lo + b)
            total = total + lax.ppermute(view[:, k], axis_name, [(i, i ^ mask) for i in range(groups)])
        cur = total
        b += width
    return cur[0]


def complex_apply(coeffs, weights, orders):
    real_in, imag_in = (coeffs[:, :orders], coeffs[:, orders:])
    real_w, imag_w = (weights[:, 0], weights[:, 1])

    def complex_term(operand_a, operand_b):
        return jnp.einsum("smc,scd->smd", operand_a, operand_b, preferred_element_type=jnp.float32)

    real_out = complex_term(real_in, real_w) - complex_term(imag_in, imag_w)
    imag_out = complex_term(real_in, imag_w) + complex_term(imag_in, real_w)
    return jnp.concatenate([real_out, imag_out], axis=1)


def complex_adjoint(coeffs, cotangents, weights, orders):
    real_in, imag_in = (coeffs[:, :orders], coeffs[:, orders:])
    real_g, imag_g = (cotangents[:, :orders], cotangents[:, orders:])
    real_w, imag_w = (weights[:, 0], weights[:, 1])

    def outer_sum(operand_a, operand_b):
        return jnp.einsum("smc,smd->scd", operand_a, operand_b, preferred_element_type=jnp.float32)

    def back_term(operand_a, operand_b):
        return jnp.einsum("smd,scd->smc", operand_a, operand_b, preferred_element_type=jnp.float32)

    grad_real = outer_sum(real_in, real_g) + outer_sum(imag_in, imag_g)
    grad_imag = outer_sum(real_in, imag_g) - outer_sum(imag_in, real_g)
    back_real = back_term(real_g, real_w) + back_term(imag_g, imag_w)
    back_imag = back_term(imag_g, real_w) - back_term(real_g, imag_w)
    return (
        jnp.stack([grad_real, grad_imag], axis=1),
        jnp.concatenate([back_real, back_imag], axis=1),
    )


def local(activations, upstream, skip_weight, spectral_weight, slot_degree):
    groups = lax.axis_size("lat")
    me = lax.axis_index("lat")
    lat_rows = activations.shape[0]
    lon_total = activations.shape[1]
    lat_total = lat_rows * groups
    per_owner = spectral_weight.shape[0]
    degrees = per_owner * groups
    orders = ORDERS
    highest = lax.Precision.HIGHEST

    fourier = jnp.asarray(fourier_table(lon_total, orders))
    cosines, sines = colatitudes(lat_total)
    plm_np = legendre_table(cosines, sines, degrees, orders)
    quad_np = plm_np * (math.pi / lat_total * sines)[None, None, :]
    if degrees * lat_total <= 64 * 64:
        plm_all = jnp.asarray(plm_np.astype(np.float32))
        quad_all = jnp.asarray(quad_np.astype(np.float32))
    else:
        plm_all = legendre_scan(cosines, sines, degrees, orders)
        quad_all = plm_all * jnp.asarray((math.pi / lat_total * sines).astype(np.float32))[None, None, :]

    bits = groups.bit_length() - 1
    lo = min(2, bits)
    both = jnp.concatenate([quad_all, plm_all], axis=1).transpose(0, 2, 1)
    near = jnp.bitwise_xor(me, jnp.arange(1 << lo, dtype=jnp.int32))
    far = jnp.bitwise_xor(me >> lo, jnp.arange(groups >> lo, dtype=jnp.int32)) * (1 << lo) + (me & ((1 << lo) - 1))
    slot_r = jnp.arange(per_owner, dtype=jnp.int32)
    row_r = jnp.arange(lat_rows, dtype=jnp.int32)
    far_deg = jnp.take(slot_degree, far[:, None] * per_owner + slot_r[None, :])
    near_rows = near[:, None] * lat_rows + row_r[None, :]
    own_both = both[far_deg[:, :, None, None], near_rows[None, None, :, :]]
    near_deg = jnp.take(slot_degree, near[:, None] * per_owner + slot_r[None, :])
    far_rows = far[:, None] * lat_rows + row_r[None, :]
    rows_both = both[near_deg[None, :, :, None], far_rows[:, None, None, :]]
    nf = 2 * orders
    own_quad, own_plm = own_both[..., :nf], own_both[..., nf:]
    rows_plm, rows_quad = rows_both[..., nf:], rows_both[..., :nf]
    to_owners = "xskrf,krfc->xsfc"
    to_rows = "xksrf,ksfc->xrfc"

    def exchange(values, table, spec):
        return xor_exchange(values, table, "lat", groups, me, lo, spec)

    spectrum = jnp.einsum("jkc,kf->jfc", activations, fourier, preferred_element_type=jnp.float32)
    coeffs = exchange(spectrum, own_quad, to_owners).astype(jnp.bfloat16)
    filtered = complex_apply(coeffs, spectral_weight, orders).astype(jnp.bfloat16)
    grid_modes = exchange(filtered, rows_plm, to_rows).astype(jnp.bfloat16)

    spatial = jnp.einsum("jfc,kf->jkc", grid_modes, fourier, preferred_element_type=jnp.float32)
    skip_out = jnp.einsum("jkc,cd->jkd", activations, skip_weight, preferred_element_type=jnp.float32)
    x = spatial + skip_out
    k_gelu = math.sqrt(2.0 / math.pi)
    x2 = x * x
    t = jnp.tanh(k_gelu * (x + 0.044715 * x * x2))
    half = 0.5 * x * (1.0 - t * t) * (k_gelu * (1.0 + 3.0 * 0.044715 * x2))
    slope_b = (upstream.astype(jnp.float32) * (0.5 * (1.0 + t) + half)).astype(jnp.bfloat16)

    skip_terms = jnp.einsum("jkc,jkd->cd", activations, slope_b, preferred_element_type=jnp.float32)
    skip_blocks = skip_terms.reshape((groups, -1) + skip_terms.shape[1:])
    grad_skip = xor_reduce_scatter(skip_blocks, "lat", groups, me, 1, 2) * (1.0 / math.sqrt(lat_total * lon_total))
    through_skip = jnp.einsum("jkd,cd->jkc", slope_b, skip_weight, preferred_element_type=jnp.float32)

    mode_grads = jnp.einsum("jkc,kf->jfc", slope_b, fourier, preferred_element_type=jnp.float32)
    coeff_grads = exchange(mode_grads, own_plm, to_owners).astype(jnp.bfloat16)
    weight_grads, back_coeffs = complex_adjoint(coeffs, coeff_grads, spectral_weight, orders)
    row_grads = exchange(back_coeffs.astype(jnp.bfloat16), rows_quad, to_rows).astype(jnp.bfloat16)
    through_modes = jnp.einsum("jfc,kf->jkc", row_grads, fourier, preferred_element_type=jnp.float32)
    grad_activations = (upstream.astype(jnp.float32) + through_skip + through_modes).astype(jnp.bfloat16)
    return (grad_activations, weight_grads.astype(jnp.bfloat16), grad_skip)


def solution(mesh):
    in_specs = (
        P(("grp", "lat"), None, None),
        P(("grp", "lat"), None, None),
        P(),
        P("lat", None, None, None),
        P(),
    )
    out_specs = (
        P(("grp", "lat"), None, None),
        P(("grp", "lat"), None, None, None),
        P(("grp", "lat"), None),
    )
    return jax.shard_map(local, mesh=mesh, in_specs=in_specs, out_specs=out_specs, check_vma=False)
```

```python
import math

import jax
import jax.numpy as jnp
import ml_dtypes
import numpy as np
from jax import lax
from jax.sharding import PartitionSpec as P

ORDERS = 4


def fourier_table(lon_total, orders):
    lon_ids = np.arange(lon_total, dtype=np.int64)[:, None]
    order_ids = np.arange(orders, dtype=np.int64)[None, :]
    angles = (lon_ids * order_ids % lon_total).astype(np.float64) * (2.0 * math.pi / lon_total)
    amplitude = math.sqrt(2.0 / lon_total)
    table = np.concatenate([amplitude * np.cos(angles), -amplitude * np.sin(angles)], axis=1)
    return table.astype(ml_dtypes.bfloat16)


def colatitudes(lat_total):
    row_ids = np.arange(lat_total)
    mirror = np.minimum(row_ids, lat_total - 1 - row_ids)
    colatitude = (mirror.astype(np.float64) + 0.5) * (math.pi / lat_total)
    cosines = np.where(row_ids < lat_total // 2, np.cos(colatitude), -np.cos(colatitude))
    return cosines, np.sin(colatitude)


def legendre_table(cosines, sines, degrees, orders):
    rows = cosines.shape[0]
    table = np.zeros((degrees, orders, rows), np.float64)
    factor = math.sqrt(0.5)
    for m in range(orders):
        if m > 0:
            factor *= math.sqrt((2.0 * m + 1.0) / (2.0 * m))
        diagonal = factor * sines**m
        if m < degrees:
            table[m, m] = diagonal
        if m + 1 < degrees:
            table[m + 1, m] = math.sqrt(2.0 * m + 3.0) * cosines * diagonal
        for l in range(m + 2, degrees):
            a = math.sqrt((4.0 * l * l - 1.0) / (l * l - m * m))
            b = math.sqrt(((l - 1.0) ** 2 - m * m) / (4.0 * (l - 1.0) ** 2 - 1.0))
            table[l, m] = a * (cosines * table[l - 1, m] - b * table[l - 2, m])
    return np.concatenate([table, table], axis=1)


def legendre_scan(cosines_np, sines_np, degrees, orders):
    cosines = jnp.asarray(cosines_np.astype(np.float32))
    sines = jnp.asarray(sines_np.astype(np.float32))
    order_col = jnp.arange(orders, dtype=jnp.float32)[:, None]
    factors = [math.sqrt(0.5)]
    for order_num in range(1, orders):
        factors.append(factors[-1] * math.sqrt((2.0 * order_num + 1.0) / (2.0 * order_num)))
    diagonal_start = jnp.array(factors, dtype=jnp.float32)[:, None] * jnp.power(sines[None, :], order_col)
    next_start = jnp.sqrt(2.0 * order_col + 3.0) * cosines[None, :] * diagonal_start

    def advance(state_pair, degree):
        previous, earlier = state_pair
        deg_value = degree.astype(jnp.float32)
        deg_below = deg_value - 1.0
        ratio_up = jnp.sqrt(
            jnp.maximum(4.0 * deg_value * deg_value - 1.0, 1.0)
            / jnp.maximum(deg_value * deg_value - order_col * order_col, 1.0)
        )
        ratio_down = jnp.sqrt(
            jnp.maximum(deg_below * deg_below - order_col * order_col, 0.0)
            / jnp.maximum(4.0 * deg_below * deg_below - 1.0, 1.0)
        )
        recurred = ratio_up * (cosines[None, :] * previous - ratio_down * earlier)
        current = jnp.where(
            deg_value == order_col,
            diagonal_start,
            jnp.where(
                deg_value == order_col + 1.0,
                next_start,
                jnp.where(deg_value > order_col + 1.0, recurred, 0.0),
            ),
        )
        return ((current, previous), current)

    zeroed = jnp.zeros((orders, cosines.shape[0]), jnp.float32)
    _, stacked = lax.scan(advance, (zeroed, zeroed), jnp.arange(degrees, dtype=jnp.int32))
    return jnp.concatenate([stacked, stacked], axis=1)


def gelu_tanh(values):
    return jax.nn.gelu(values, approximate=True)


def xor_gather(x, axis_name, groups):
    bits = groups.bit_length() - 1
    cur = x[None]
    low = 0
    while low < bits:
        width = min(2, bits - low)
        parts = [cur]
        for k in range(1, 1 << width):
            mask = k << low
            parts.append(lax.ppermute(cur, axis_name, [(i, i ^ mask) for i in range(groups)]))
        cur = jnp.concatenate(parts, axis=0)
        low += width
    return cur


def xor_reduce_scatter(part, axis_name, groups, me, step=2, narrow=0):
    bits = groups.bit_length() - 1
    cur = part
    low = 0
    while low < bits:
        width = min(step, bits - low)
        fan = 1 << width
        view = cur.reshape((cur.shape[0] // fan, fan) + cur.shape[1:])
        mine = (me >> low) & (fan - 1)
        total = lax.dynamic_index_in_dim(view, mine, axis=1, keepdims=False)
        for k in range(1, fan):
            mask = k << low
            sent = lax.dynamic_index_in_dim(view, jnp.bitwise_xor(mine, k), axis=1, keepdims=False)
            if low < narrow:
                sent = sent.astype(jnp.bfloat16)
            moved = lax.ppermute(sent, axis_name, [(i, i ^ mask) for i in range(groups)])
            total = total + moved.astype(jnp.float32)
        cur = total
        low += width
    return cur[0]


def xor_exchange(values, table, axis_name, groups, me, lo, spec):
    parts = [values]
    for k in range(1, 1 << lo):
        parts.append(lax.ppermute(values, axis_name, [(i, i ^ k) for i in range(groups)]))
    stacked = jnp.stack(parts).astype(jnp.float32)
    cur = jnp.einsum(spec, table, stacked, precision=lax.Precision.HIGHEST)
    hi = groups.bit_length() - 1 - lo
    b = 0
    while b < hi:
        width = min(2, hi - b)
        fan = 1 << width
        view = cur.reshape((cur.shape[0] // fan, fan) + cur.shape[1:])
        total = view[:, 0]
        for k in range(1, fan):
            mask = k << (lo + b)
            total = total + lax.ppermute(view[:, k], axis_name, [(i, i ^ mask) for i in range(groups)])
        cur = total
        b += width
    return cur[0]


def complex_apply(coeffs, weights, orders):
    real_in, imag_in = (coeffs[:, :orders], coeffs[:, orders:])
    real_w, imag_w = (weights[:, 0], weights[:, 1])

    def complex_term(operand_a, operand_b):
        return jnp.einsum("smc,scd->smd", operand_a, operand_b, preferred_element_type=jnp.float32)

    real_out = complex_term(real_in, real_w) - complex_term(imag_in, imag_w)
    imag_out = complex_term(real_in, imag_w) + complex_term(imag_in, real_w)
    return jnp.concatenate([real_out, imag_out], axis=1)


def complex_adjoint(coeffs, cotangents, weights, orders):
    real_in, imag_in = (coeffs[:, :orders], coeffs[:, orders:])
    real_g, imag_g = (cotangents[:, :orders], cotangents[:, orders:])
    real_w, imag_w = (weights[:, 0], weights[:, 1])

    def outer_sum(operand_a, operand_b):
        return jnp.einsum("smc,smd->scd", operand_a, operand_b, preferred_element_type=jnp.float32)

    def back_term(operand_a, operand_b):
        return jnp.einsum("smd,scd->smc", operand_a, operand_b, preferred_element_type=jnp.float32)

    grad_real = outer_sum(real_in, real_g) + outer_sum(imag_in, imag_g)
    grad_imag = outer_sum(real_in, imag_g) - outer_sum(imag_in, real_g)
    back_real = back_term(real_g, real_w) + back_term(imag_g, imag_w)
    back_imag = back_term(imag_g, real_w) - back_term(real_g, imag_w)
    return (
        jnp.stack([grad_real, grad_imag], axis=1),
        jnp.concatenate([back_real, back_imag], axis=1),
    )


def local(activations, upstream, skip_weight, spectral_weight, slot_degree):
    groups = lax.axis_size("lat")
    me = lax.axis_index("lat")
    lat_rows = activations.shape[0]
    lon_total = activations.shape[1]
    lat_total = lat_rows * groups
    per_owner = spectral_weight.shape[0]
    degrees = per_owner * groups
    orders = ORDERS
    highest = lax.Precision.HIGHEST

    fourier = jnp.asarray(fourier_table(lon_total, orders))
    cosines, sines = colatitudes(lat_total)
    plm_np = legendre_table(cosines, sines, degrees, orders)
    quad_np = plm_np * (math.pi / lat_total * sines)[None, None, :]
    if degrees * lat_total <= 64 * 64:
        plm_all = jnp.asarray(plm_np.astype(np.float32))
        quad_all = jnp.asarray(quad_np.astype(np.float32))
    else:
        plm_all = legendre_scan(cosines, sines, degrees, orders)
        quad_all = plm_all * jnp.asarray((math.pi / lat_total * sines).astype(np.float32))[None, None, :]

    bits = groups.bit_length() - 1
    lo = min(2, bits)
    both = jnp.concatenate([quad_all, plm_all], axis=1).transpose(0, 2, 1)
    near = jnp.bitwise_xor(me, jnp.arange(1 << lo, dtype=jnp.int32))
    far = jnp.bitwise_xor(me >> lo, jnp.arange(groups >> lo, dtype=jnp.int32)) * (1 << lo) + (me & ((1 << lo) - 1))
    slot_r = jnp.arange(per_owner, dtype=jnp.int32)
    row_r = jnp.arange(lat_rows, dtype=jnp.int32)
    far_deg = jnp.take(slot_degree, far[:, None] * per_owner + slot_r[None, :])
    near_rows = near[:, None] * lat_rows + row_r[None, :]
    own_both = both[far_deg[:, :, None, None], near_rows[None, None, :, :]]
    near_deg = jnp.take(slot_degree, near[:, None] * per_owner + slot_r[None, :])
    far_rows = far[:, None] * lat_rows + row_r[None, :]
    rows_both = both[near_deg[None, :, :, None], far_rows[:, None, None, :]]
    nf = 2 * orders
    own_quad, own_plm = own_both[..., :nf], own_both[..., nf:]
    rows_plm, rows_quad = rows_both[..., nf:], rows_both[..., :nf]
    to_owners = "xskrf,krfc->xsfc"
    to_rows = "xksrf,ksfc->xrfc"

    def exchange(values, table, spec):
        return xor_exchange(values, table, "lat", groups, me, lo, spec)

    spectrum = jnp.einsum("jkc,kf->jfc", activations, fourier, preferred_element_type=jnp.float32)
    coeffs = exchange(spectrum, own_quad, to_owners).astype(jnp.bfloat16)
    filtered = complex_apply(coeffs, spectral_weight, orders).astype(jnp.bfloat16)
    grid_modes = exchange(filtered, rows_plm, to_rows).astype(jnp.bfloat16)

    spatial = jnp.einsum("jfc,kf->jkc", grid_modes, fourier, preferred_element_type=jnp.float32)
    skip_out = jnp.einsum("jkc,cd->jkd", activations, skip_weight, preferred_element_type=jnp.float32)
    x = spatial + skip_out
    k_gelu = math.sqrt(2.0 / math.pi)
    x2 = x * x
    t = jnp.tanh(k_gelu * (x + 0.044715 * x * x2))
    half = 0.5 * x * (1.0 - t * t) * (k_gelu * (1.0 + 3.0 * 0.044715 * x2))
    slope_b = (upstream.astype(jnp.float32) * (0.5 * (1.0 + t) + half)).astype(jnp.bfloat16)

    skip_terms = jnp.einsum("jkc,jkd->cd", activations, slope_b, preferred_element_type=jnp.float32) * (
        1.0 / math.sqrt(lat_total * lon_total)
    )
    skip_blocks = skip_terms.reshape((groups, -1) + skip_terms.shape[1:])
    grad_skip = xor_reduce_scatter(skip_blocks, "lat", groups, me, 1, 2)
    through_skip = jnp.einsum("jkd,cd->jkc", slope_b, skip_weight, preferred_element_type=jnp.float32)

    mode_grads = jnp.einsum("jkc,kf->jfc", slope_b, fourier, preferred_element_type=jnp.float32)
    coeff_grads = exchange(mode_grads, own_plm, to_owners).astype(jnp.bfloat16)
    weight_grads, back_coeffs = complex_adjoint(coeffs, coeff_grads, spectral_weight, orders)
    row_grads = exchange(back_coeffs.astype(jnp.bfloat16), rows_quad, to_rows).astype(jnp.bfloat16)
    through_modes = jnp.einsum("jfc,kf->jkc", row_grads, fourier, preferred_element_type=jnp.float32)
    grad_activations = (upstream.astype(jnp.float32) + through_skip + through_modes).astype(jnp.bfloat16)
    return (grad_activations, weight_grads.astype(jnp.bfloat16), grad_skip)


def solution(mesh):
    in_specs = (
        P(("grp", "lat"), None, None),
        P(("grp", "lat"), None, None),
        P(),
        P("lat", None, None, None),
        P(),
    )
    out_specs = (
        P(("grp", "lat"), None, None),
        P(("grp", "lat"), None, None, None),
        P(("grp", "lat"), None),
    )
    return jax.shard_map(local, mesh=mesh, in_specs=in_specs, out_specs=out_specs, check_vma=False)
```

```python
import math

import jax
import jax.numpy as jnp
import ml_dtypes
import numpy as np
from jax import lax
from jax.sharding import PartitionSpec as P

ORDERS = 4


def fourier_table(lon_total, orders):
    lon_ids = np.arange(lon_total, dtype=np.int64)[:, None]
    order_ids = np.arange(orders, dtype=np.int64)[None, :]
    angles = (lon_ids * order_ids % lon_total).astype(np.float64) * (2.0 * math.pi / lon_total)
    amplitude = math.sqrt(2.0 / lon_total)
    table = np.concatenate([amplitude * np.cos(angles), -amplitude * np.sin(angles)], axis=1)
    return table.astype(ml_dtypes.bfloat16)


def colatitudes(lat_total):
    row_ids = np.arange(lat_total)
    mirror = np.minimum(row_ids, lat_total - 1 - row_ids)
    colatitude = (mirror.astype(np.float64) + 0.5) * (math.pi / lat_total)
    cosines = np.where(row_ids < lat_total // 2, np.cos(colatitude), -np.cos(colatitude))
    return cosines, np.sin(colatitude)


def legendre_table(cosines, sines, degrees, orders):
    rows = cosines.shape[0]
    table = np.zeros((degrees, orders, rows), np.float64)
    factor = math.sqrt(0.5)
    for m in range(orders):
        if m > 0:
            factor *= math.sqrt((2.0 * m + 1.0) / (2.0 * m))
        diagonal = factor * sines**m
        if m < degrees:
            table[m, m] = diagonal
        if m + 1 < degrees:
            table[m + 1, m] = math.sqrt(2.0 * m + 3.0) * cosines * diagonal
        for l in range(m + 2, degrees):
            a = math.sqrt((4.0 * l * l - 1.0) / (l * l - m * m))
            b = math.sqrt(((l - 1.0) ** 2 - m * m) / (4.0 * (l - 1.0) ** 2 - 1.0))
            table[l, m] = a * (cosines * table[l - 1, m] - b * table[l - 2, m])
    return np.concatenate([table, table], axis=1)


def legendre_scan(cosines_np, sines_np, degrees, orders):
    cosines = jnp.asarray(cosines_np.astype(np.float32))
    sines = jnp.asarray(sines_np.astype(np.float32))
    order_col = jnp.arange(orders, dtype=jnp.float32)[:, None]
    factors = [math.sqrt(0.5)]
    for order_num in range(1, orders):
        factors.append(factors[-1] * math.sqrt((2.0 * order_num + 1.0) / (2.0 * order_num)))
    diagonal_start = jnp.array(factors, dtype=jnp.float32)[:, None] * jnp.power(sines[None, :], order_col)
    next_start = jnp.sqrt(2.0 * order_col + 3.0) * cosines[None, :] * diagonal_start

    def advance(state_pair, degree):
        previous, earlier = state_pair
        deg_value = degree.astype(jnp.float32)
        deg_below = deg_value - 1.0
        ratio_up = jnp.sqrt(
            jnp.maximum(4.0 * deg_value * deg_value - 1.0, 1.0)
            / jnp.maximum(deg_value * deg_value - order_col * order_col, 1.0)
        )
        ratio_down = jnp.sqrt(
            jnp.maximum(deg_below * deg_below - order_col * order_col, 0.0)
            / jnp.maximum(4.0 * deg_below * deg_below - 1.0, 1.0)
        )
        recurred = ratio_up * (cosines[None, :] * previous - ratio_down * earlier)
        current = jnp.where(
            deg_value == order_col,
            diagonal_start,
            jnp.where(
                deg_value == order_col + 1.0,
                next_start,
                jnp.where(deg_value > order_col + 1.0, recurred, 0.0),
            ),
        )
        return ((current, previous), current)

    zeroed = jnp.zeros((orders, cosines.shape[0]), jnp.float32)
    _, stacked = lax.scan(advance, (zeroed, zeroed), jnp.arange(degrees, dtype=jnp.int32))
    return jnp.concatenate([stacked, stacked], axis=1)


def gelu_tanh(values):
    return jax.nn.gelu(values, approximate=True)


def xor_gather(x, axis_name, groups):
    bits = groups.bit_length() - 1
    cur = x[None]
    low = 0
    while low < bits:
        width = min(2, bits - low)
        parts = [cur]
        for k in range(1, 1 << width):
            mask = k << low
            parts.append(lax.ppermute(cur, axis_name, [(i, i ^ mask) for i in range(groups)]))
        cur = jnp.concatenate(parts, axis=0)
        low += width
    return cur


def xor_reduce_scatter(part, axis_name, groups, me, step=2, narrow=0):
    bits = groups.bit_length() - 1
    cur = part
    low = 0
    while low < bits:
        width = min(step, bits - low)
        fan = 1 << width
        view = cur.reshape((cur.shape[0] // fan, fan) + cur.shape[1:])
        mine = (me >> low) & (fan - 1)
        total = lax.dynamic_index_in_dim(view, mine, axis=1, keepdims=False)
        for k in range(1, fan):
            mask = k << low
            sent = lax.dynamic_index_in_dim(view, jnp.bitwise_xor(mine, k), axis=1, keepdims=False)
            if low < narrow:
                sent = sent.astype(jnp.bfloat16)
            moved = lax.ppermute(sent, axis_name, [(i, i ^ mask) for i in range(groups)])
            total = total + moved.astype(jnp.float32)
        cur = total
        low += width
    return cur[0]


def xor_exchange(values, table, axis_name, groups, me, lo, spec):
    parts = [values]
    for k in range(1, 1 << lo):
        parts.append(lax.ppermute(values, axis_name, [(i, i ^ k) for i in range(groups)]))
    stacked = jnp.stack(parts).astype(jnp.float32)
    cur = jnp.einsum(spec, table, stacked, precision=lax.Precision.HIGHEST)
    hi = groups.bit_length() - 1 - lo
    b = 0
    while b < hi:
        width = min(2, hi - b)
        fan = 1 << width
        view = cur.reshape((cur.shape[0] // fan, fan) + cur.shape[1:])
        total = view[:, 0]
        for k in range(1, fan):
            mask = k << (lo + b)
            total = total + lax.ppermute(view[:, k], axis_name, [(i, i ^ mask) for i in range(groups)])
        cur = total
        b += width
    return cur[0]


def complex_apply(coeffs, weights, orders):
    real_in, imag_in = (coeffs[:, :orders], coeffs[:, orders:])
    real_w, imag_w = (weights[:, 0], weights[:, 1])

    def complex_term(operand_a, operand_b):
        return jnp.einsum("smc,scd->smd", operand_a, operand_b, preferred_element_type=jnp.float32)

    real_out = complex_term(real_in, real_w) - complex_term(imag_in, imag_w)
    imag_out = complex_term(real_in, imag_w) + complex_term(imag_in, real_w)
    return jnp.concatenate([real_out, imag_out], axis=1)


def complex_adjoint(coeffs, cotangents, weights, orders):
    real_in, imag_in = (coeffs[:, :orders], coeffs[:, orders:])
    real_g, imag_g = (cotangents[:, :orders], cotangents[:, orders:])
    real_w, imag_w = (weights[:, 0], weights[:, 1])

    def outer_sum(operand_a, operand_b):
        return jnp.einsum("smc,smd->scd", operand_a, operand_b, preferred_element_type=jnp.float32)

    def back_term(operand_a, operand_b):
        return jnp.einsum("smd,scd->smc", operand_a, operand_b, preferred_element_type=jnp.float32)

    grad_real = outer_sum(real_in, real_g) + outer_sum(imag_in, imag_g)
    grad_imag = outer_sum(real_in, imag_g) - outer_sum(imag_in, real_g)
    back_real = back_term(real_g, real_w) + back_term(imag_g, imag_w)
    back_imag = back_term(imag_g, real_w) - back_term(real_g, imag_w)
    return (
        jnp.stack([grad_real, grad_imag], axis=1),
        jnp.concatenate([back_real, back_imag], axis=1),
    )


def local(activations, upstream, skip_weight, spectral_weight, slot_degree):
    groups = lax.axis_size("lat")
    me = lax.axis_index("lat")
    lat_rows = activations.shape[0]
    lon_total = activations.shape[1]
    lat_total = lat_rows * groups
    per_owner = spectral_weight.shape[0]
    degrees = per_owner * groups
    orders = ORDERS
    highest = lax.Precision.HIGHEST

    fourier = jnp.asarray(fourier_table(lon_total, orders))
    cosines, sines = colatitudes(lat_total)
    plm_np = legendre_table(cosines, sines, degrees, orders)
    quad_np = plm_np * (math.pi / lat_total * sines)[None, None, :]
    if degrees * lat_total <= 64 * 64:
        plm_all = jnp.asarray(plm_np.astype(np.float32))
        quad_all = jnp.asarray(quad_np.astype(np.float32))
    else:
        plm_all = legendre_scan(cosines, sines, degrees, orders)
        quad_all = plm_all * jnp.asarray((math.pi / lat_total * sines).astype(np.float32))[None, None, :]

    bits = groups.bit_length() - 1
    lo = min(2, bits)
    both = jnp.concatenate([quad_all, plm_all], axis=1).transpose(0, 2, 1)
    near = jnp.bitwise_xor(me, jnp.arange(1 << lo, dtype=jnp.int32))
    far = jnp.bitwise_xor(me >> lo, jnp.arange(groups >> lo, dtype=jnp.int32)) * (1 << lo) + (me & ((1 << lo) - 1))
    slot_r = jnp.arange(per_owner, dtype=jnp.int32)
    row_r = jnp.arange(lat_rows, dtype=jnp.int32)
    far_deg = jnp.take(slot_degree, far[:, None] * per_owner + slot_r[None, :])
    near_rows = near[:, None] * lat_rows + row_r[None, :]
    own_both = both[far_deg[:, :, None, None], near_rows[None, None, :, :]]
    near_deg = jnp.take(slot_degree, near[:, None] * per_owner + slot_r[None, :])
    far_rows = far[:, None] * lat_rows + row_r[None, :]
    rows_both = both[near_deg[None, :, :, None], far_rows[:, None, None, :]]
    nf = 2 * orders
    own_quad, own_plm = own_both[..., :nf], own_both[..., nf:]
    rows_plm, rows_quad = rows_both[..., nf:], rows_both[..., :nf]
    to_owners = "xskrf,krfc->xsfc"
    to_rows = "xksrf,ksfc->xrfc"

    def exchange(values, table, spec):
        return xor_exchange(values, table, "lat", groups, me, lo, spec)

    spectrum = jnp.einsum("jkc,kf->jfc", activations, fourier, preferred_element_type=jnp.float32)
    coeffs = exchange(spectrum, own_quad, to_owners).astype(jnp.bfloat16)
    filtered = complex_apply(coeffs, spectral_weight, orders).astype(jnp.bfloat16)
    grid_modes = exchange(filtered, rows_plm, to_rows).astype(jnp.bfloat16)

    spatial = jnp.einsum("jfc,kf->jkc", grid_modes, fourier, preferred_element_type=jnp.float32)
    skip_out = jnp.einsum("jkc,cd->jkd", activations, skip_weight, preferred_element_type=jnp.float32)
    x = spatial + skip_out
    k_gelu = math.sqrt(2.0 / math.pi)
    x2 = x * x
    t = jnp.tanh(k_gelu * (x + 0.044715 * x * x2))
    half = 0.5 * x * (1.0 - t * t) * (k_gelu * (1.0 + 3.0 * 0.044715 * x2))
    slope_b = (upstream.astype(jnp.float32) * (0.5 * (1.0 + t) + half)).astype(jnp.bfloat16)

    skip_terms = jnp.einsum("jkc,jkd->cd", activations, slope_b, preferred_element_type=jnp.float32)
    skip_blocks = skip_terms.reshape((groups, -1) + skip_terms.shape[1:])
    grad_skip = xor_reduce_scatter(skip_blocks, "lat", groups, me, 1, bits) * (1.0 / math.sqrt(lat_total * lon_total))
    through_skip = jnp.einsum("jkd,cd->jkc", slope_b, skip_weight, preferred_element_type=jnp.float32)

    mode_grads = jnp.einsum("jkc,kf->jfc", slope_b, fourier, preferred_element_type=jnp.float32)
    coeff_grads = exchange(mode_grads, own_plm, to_owners).astype(jnp.bfloat16)
    weight_grads, back_coeffs = complex_adjoint(coeffs, coeff_grads, spectral_weight, orders)
    row_grads = exchange(back_coeffs.astype(jnp.bfloat16), rows_quad, to_rows).astype(jnp.bfloat16)
    through_modes = jnp.einsum("jfc,kf->jkc", row_grads, fourier, preferred_element_type=jnp.float32)
    grad_activations = (upstream.astype(jnp.float32) + through_skip + through_modes).astype(jnp.bfloat16)
    return (grad_activations, weight_grads.astype(jnp.bfloat16), grad_skip)


def solution(mesh):
    in_specs = (
        P(("grp", "lat"), None, None),
        P(("grp", "lat"), None, None),
        P(),
        P("lat", None, None, None),
        P(),
    )
    out_specs = (
        P(("grp", "lat"), None, None),
        P(("grp", "lat"), None, None, None),
        P(("grp", "lat"), None),
    )
    return jax.shard_map(local, mesh=mesh, in_specs=in_specs, out_specs=out_specs, check_vma=False)
```

```python
import math

import jax
import jax.numpy as jnp
import ml_dtypes
import numpy as np
from jax import lax
from jax.sharding import PartitionSpec as P

ORDERS = 4


def fourier_table(lon_total, orders):
    lon_ids = np.arange(lon_total, dtype=np.int64)[:, None]
    order_ids = np.arange(orders, dtype=np.int64)[None, :]
    angles = (lon_ids * order_ids % lon_total).astype(np.float64) * (2.0 * math.pi / lon_total)
    amplitude = math.sqrt(2.0 / lon_total)
    table = np.concatenate([amplitude * np.cos(angles), -amplitude * np.sin(angles)], axis=1)
    return table.astype(ml_dtypes.bfloat16)


def colatitudes(lat_total):
    row_ids = np.arange(lat_total)
    mirror = np.minimum(row_ids, lat_total - 1 - row_ids)
    colatitude = (mirror.astype(np.float64) + 0.5) * (math.pi / lat_total)
    cosines = np.where(row_ids < lat_total // 2, np.cos(colatitude), -np.cos(colatitude))
    return cosines, np.sin(colatitude)


def legendre_table(cosines, sines, degrees, orders):
    rows = cosines.shape[0]
    table = np.zeros((degrees, orders, rows), np.float64)
    factor = math.sqrt(0.5)
    for m in range(orders):
        if m > 0:
            factor *= math.sqrt((2.0 * m + 1.0) / (2.0 * m))
        diagonal = factor * sines**m
        if m < degrees:
            table[m, m] = diagonal
        if m + 1 < degrees:
            table[m + 1, m] = math.sqrt(2.0 * m + 3.0) * cosines * diagonal
        for l in range(m + 2, degrees):
            a = math.sqrt((4.0 * l * l - 1.0) / (l * l - m * m))
            b = math.sqrt(((l - 1.0) ** 2 - m * m) / (4.0 * (l - 1.0) ** 2 - 1.0))
            table[l, m] = a * (cosines * table[l - 1, m] - b * table[l - 2, m])
    return np.concatenate([table, table], axis=1)


def legendre_scan(cosines_np, sines_np, degrees, orders):
    cosines = jnp.asarray(cosines_np.astype(np.float32))
    sines = jnp.asarray(sines_np.astype(np.float32))
    order_col = jnp.arange(orders, dtype=jnp.float32)[:, None]
    factors = [math.sqrt(0.5)]
    for order_num in range(1, orders):
        factors.append(factors[-1] * math.sqrt((2.0 * order_num + 1.0) / (2.0 * order_num)))
    diagonal_start = jnp.array(factors, dtype=jnp.float32)[:, None] * jnp.power(sines[None, :], order_col)
    next_start = jnp.sqrt(2.0 * order_col + 3.0) * cosines[None, :] * diagonal_start

    def advance(state_pair, degree):
        previous, earlier = state_pair
        deg_value = degree.astype(jnp.float32)
        deg_below = deg_value - 1.0
        ratio_up = jnp.sqrt(
            jnp.maximum(4.0 * deg_value * deg_value - 1.0, 1.0)
            / jnp.maximum(deg_value * deg_value - order_col * order_col, 1.0)
        )
        ratio_down = jnp.sqrt(
            jnp.maximum(deg_below * deg_below - order_col * order_col, 0.0)
            / jnp.maximum(4.0 * deg_below * deg_below - 1.0, 1.0)
        )
        recurred = ratio_up * (cosines[None, :] * previous - ratio_down * earlier)
        current = jnp.where(
            deg_value == order_col,
            diagonal_start,
            jnp.where(
                deg_value == order_col + 1.0,
                next_start,
                jnp.where(deg_value > order_col + 1.0, recurred, 0.0),
            ),
        )
        return ((current, previous), current)

    zeroed = jnp.zeros((orders, cosines.shape[0]), jnp.float32)
    _, stacked = lax.scan(advance, (zeroed, zeroed), jnp.arange(degrees, dtype=jnp.int32))
    return jnp.concatenate([stacked, stacked], axis=1)


def gelu_tanh(values):
    return jax.nn.gelu(values, approximate=True)


def xor_gather(x, axis_name, groups):
    bits = groups.bit_length() - 1
    cur = x[None]
    low = 0
    while low < bits:
        width = min(2, bits - low)
        parts = [cur]
        for k in range(1, 1 << width):
            mask = k << low
            parts.append(lax.ppermute(cur, axis_name, [(i, i ^ mask) for i in range(groups)]))
        cur = jnp.concatenate(parts, axis=0)
        low += width
    return cur


def xor_reduce_scatter(part, axis_name, groups, me, step=2, narrow=0):
    bits = groups.bit_length() - 1
    cur = part
    low = 0
    while low < bits:
        width = min(step, bits - low)
        fan = 1 << width
        view = cur.reshape((cur.shape[0] // fan, fan) + cur.shape[1:])
        mine = (me >> low) & (fan - 1)
        total = lax.dynamic_index_in_dim(view, mine, axis=1, keepdims=False)
        for k in range(1, fan):
            mask = k << low
            sent = lax.dynamic_index_in_dim(view, jnp.bitwise_xor(mine, k), axis=1, keepdims=False)
            if low < narrow:
                sent = sent.astype(jnp.bfloat16)
            moved = lax.ppermute(sent, axis_name, [(i, i ^ mask) for i in range(groups)])
            total = total + moved.astype(jnp.float32)
        cur = total
        low += width
    return cur[0]


def reversed_halving(cur, axis_name, groups, me, bits):
    for r in range(bits):
        dev_bit = bits - 1 - r
        view = cur.reshape((cur.shape[0] // 2, 2) + cur.shape[1:])
        bit = (me >> dev_bit) & 1
        total = lax.dynamic_index_in_dim(view, bit, axis=1, keepdims=False)
        sent = lax.dynamic_index_in_dim(view, 1 - bit, axis=1, keepdims=False).astype(jnp.bfloat16)
        mask = 1 << dev_bit
        cur = total + lax.ppermute(sent, axis_name, [(i, i ^ mask) for i in range(groups)]).astype(jnp.float32)
    return cur[0]


def xor_exchange(values, table, axis_name, groups, me, lo, spec):
    parts = [values]
    for k in range(1, 1 << lo):
        parts.append(lax.ppermute(values, axis_name, [(i, i ^ k) for i in range(groups)]))
    stacked = jnp.stack(parts).astype(jnp.float32)
    cur = jnp.einsum(spec, table, stacked, precision=lax.Precision.HIGHEST)
    hi = groups.bit_length() - 1 - lo
    b = 0
    while b < hi:
        width = min(2, hi - b)
        fan = 1 << width
        view = cur.reshape((cur.shape[0] // fan, fan) + cur.shape[1:])
        total = view[:, 0]
        for k in range(1, fan):
            mask = k << (lo + b)
            total = total + lax.ppermute(view[:, k], axis_name, [(i, i ^ mask) for i in range(groups)])
        cur = total
        b += width
    return cur[0]


def complex_apply(coeffs, weights, orders):
    real_in, imag_in = (coeffs[:, :orders], coeffs[:, orders:])
    real_w, imag_w = (weights[:, 0], weights[:, 1])

    def complex_term(operand_a, operand_b):
        return jnp.einsum("smc,scd->smd", operand_a, operand_b, preferred_element_type=jnp.float32)

    real_out = complex_term(real_in, real_w) - complex_term(imag_in, imag_w)
    imag_out = complex_term(real_in, imag_w) + complex_term(imag_in, real_w)
    return jnp.concatenate([real_out, imag_out], axis=1)


def complex_adjoint(coeffs, cotangents, weights, orders):
    real_in, imag_in = (coeffs[:, :orders], coeffs[:, orders:])
    real_g, imag_g = (cotangents[:, :orders], cotangents[:, orders:])
    real_w, imag_w = (weights[:, 0], weights[:, 1])

    def outer_sum(operand_a, operand_b):
        return jnp.einsum("smc,smd->scd", operand_a, operand_b, preferred_element_type=jnp.float32)

    def back_term(operand_a, operand_b):
        return jnp.einsum("smd,scd->smc", operand_a, operand_b, preferred_element_type=jnp.float32)

    grad_real = outer_sum(real_in, real_g) + outer_sum(imag_in, imag_g)
    grad_imag = outer_sum(real_in, imag_g) - outer_sum(imag_in, real_g)
    back_real = back_term(real_g, real_w) + back_term(imag_g, imag_w)
    back_imag = back_term(imag_g, real_w) - back_term(real_g, imag_w)
    return (
        jnp.stack([grad_real, grad_imag], axis=1),
        jnp.concatenate([back_real, back_imag], axis=1),
    )


def local(activations, upstream, skip_weight, spectral_weight, slot_degree):
    groups = lax.axis_size("lat")
    me = lax.axis_index("lat")
    lat_rows = activations.shape[0]
    lon_total = activations.shape[1]
    lat_total = lat_rows * groups
    per_owner = spectral_weight.shape[0]
    degrees = per_owner * groups
    orders = ORDERS
    highest = lax.Precision.HIGHEST

    fourier = jnp.asarray(fourier_table(lon_total, orders))
    cosines, sines = colatitudes(lat_total)
    plm_np = legendre_table(cosines, sines, degrees, orders)
    quad_np = plm_np * (math.pi / lat_total * sines)[None, None, :]
    if degrees * lat_total <= 64 * 64:
        plm_all = jnp.asarray(plm_np.astype(np.float32))
        quad_all = jnp.asarray(quad_np.astype(np.float32))
    else:
        plm_all = legendre_scan(cosines, sines, degrees, orders)
        quad_all = plm_all * jnp.asarray((math.pi / lat_total * sines).astype(np.float32))[None, None, :]

    bits = groups.bit_length() - 1
    lo = min(2, bits)
    both = jnp.concatenate([quad_all, plm_all], axis=1).transpose(0, 2, 1)
    near = jnp.bitwise_xor(me, jnp.arange(1 << lo, dtype=jnp.int32))
    far = jnp.bitwise_xor(me >> lo, jnp.arange(groups >> lo, dtype=jnp.int32)) * (1 << lo) + (me & ((1 << lo) - 1))
    slot_r = jnp.arange(per_owner, dtype=jnp.int32)
    row_r = jnp.arange(lat_rows, dtype=jnp.int32)
    far_deg = jnp.take(slot_degree, far[:, None] * per_owner + slot_r[None, :])
    near_rows = near[:, None] * lat_rows + row_r[None, :]
    own_both = both[far_deg[:, :, None, None], near_rows[None, None, :, :]]
    near_deg = jnp.take(slot_degree, near[:, None] * per_owner + slot_r[None, :])
    far_rows = far[:, None] * lat_rows + row_r[None, :]
    rows_both = both[near_deg[None, :, :, None], far_rows[:, None, None, :]]
    nf = 2 * orders
    own_quad, own_plm = own_both[..., :nf], own_both[..., nf:]
    rows_plm, rows_quad = rows_both[..., nf:], rows_both[..., :nf]
    to_owners = "xskrf,krfc->xsfc"
    to_rows = "xksrf,ksfc->xrfc"

    def exchange(values, table, spec):
        return xor_exchange(values, table, "lat", groups, me, lo, spec)

    spectrum = jnp.einsum("jkc,kf->jfc", activations, fourier, preferred_element_type=jnp.float32)
    coeffs = exchange(spectrum, own_quad, to_owners).astype(jnp.bfloat16)
    filtered = complex_apply(coeffs, spectral_weight, orders).astype(jnp.bfloat16)
    grid_modes = exchange(filtered, rows_plm, to_rows).astype(jnp.bfloat16)

    spatial = jnp.einsum("jfc,kf->jkc", grid_modes, fourier, preferred_element_type=jnp.float32)
    skip_out = jnp.einsum("jkc,cd->jkd", activations, skip_weight, preferred_element_type=jnp.float32)
    x = spatial + skip_out
    k_gelu = math.sqrt(2.0 / math.pi)
    x2 = x * x
    t = jnp.tanh(k_gelu * (x + 0.044715 * x * x2))
    half = 0.5 * x * (1.0 - t * t) * (k_gelu * (1.0 + 3.0 * 0.044715 * x2))
    slope_b = (upstream.astype(jnp.float32) * (0.5 * (1.0 + t) + half)).astype(jnp.bfloat16)

    skip_terms = jnp.einsum("jkc,jkd->cd", activations, slope_b, preferred_element_type=jnp.float32)
    skip_blocks = skip_terms.reshape((groups, -1) + skip_terms.shape[1:])
    flips = skip_blocks.reshape((2,) * bits + skip_blocks.shape[1:])
    flips = flips.transpose(tuple(range(bits))[::-1] + (bits, bits + 1)).reshape(skip_blocks.shape)
    grad_skip = reversed_halving(flips, "lat", groups, me, bits) * (1.0 / math.sqrt(lat_total * lon_total))
    through_skip = jnp.einsum("jkd,cd->jkc", slope_b, skip_weight, preferred_element_type=jnp.float32)

    mode_grads = jnp.einsum("jkc,kf->jfc", slope_b, fourier, preferred_element_type=jnp.float32)
    coeff_grads = exchange(mode_grads, own_plm, to_owners).astype(jnp.bfloat16)
    weight_grads, back_coeffs = complex_adjoint(coeffs, coeff_grads, spectral_weight, orders)
    row_grads = exchange(back_coeffs.astype(jnp.bfloat16), rows_quad, to_rows).astype(jnp.bfloat16)
    through_modes = jnp.einsum("jfc,kf->jkc", row_grads, fourier, preferred_element_type=jnp.float32)
    grad_activations = (upstream.astype(jnp.float32) + through_skip + through_modes).astype(jnp.bfloat16)
    return (grad_activations, weight_grads.astype(jnp.bfloat16), grad_skip)


def solution(mesh):
    in_specs = (
        P(("grp", "lat"), None, None),
        P(("grp", "lat"), None, None),
        P(),
        P("lat", None, None, None),
        P(),
    )
    out_specs = (
        P(("grp", "lat"), None, None),
        P(("grp", "lat"), None, None, None),
        P(("grp", "lat"), None),
    )
    return jax.shard_map(local, mesh=mesh, in_specs=in_specs, out_specs=out_specs, check_vma=False)
```
